512 devices in a mesh: grp: 16 (over y, core), dev: 32 (over z, x).
Axes of the slice: x: 4, y: 8, z: 8, core: 2. Of those that a mesh axis runs over, the one named last changes fastest.
Arguments:
- panel_inverse: float32 [16, 32, 256, 256], P('grp', 'dev')
- coupling: float32 [16, 32, 256, 256], P('grp', 'dev'), may hold values from -0.875 to 0.875
- loads: float32 [16, 32, 16, 256], P('grp', 'dev'), may hold values from -6 to 6
- stiffness: float32 [24, 24], replicated
- element_substructure: int32 [16, 32, 1024], P('grp', 'dev'), may hold values from 0 to 31
- element_rows: int32 [16, 32, 24, 1024], P('grp', 'dev'), may hold values from 0 to 255
- element_density: float32 [16, 32, 1024], P('grp', 'dev'), may hold values from 0.2 to 1
- send_elements: int32 [16, 32, 32, 64], P('grp', 'dev'), may hold values from 0 to 1023
- receive_cells: int32 [16, 32, 32, 64], P('grp', 'dev'), may hold values from -1 to 16383, as said below
- design_density: float32 [16, 32, 128, 128], P('grp', 'dev'), may hold values from 0.3 to 1
- filter_offsets: int32 [8], replicated, may hold values from -3 to 3, as said below
- filter_weights: float32 [8], replicated, may hold values from 0.2 to 1
Outputs:
- interface: float32 [16, 32, 16, 256], P('grp', 'dev')
- filtered: float32 [16, 32, 128, 128], P('grp', 'dev')
The draws below stay inside these ranges and needn't reach their ends.
Inputs may be any that keep to these rules, and one draw needn't show every extreme that they name: `receive_cells`: each receiver's slots from one source are filled in order: the first 64, 32, 16 or 8 hold a cell, the rest -1; in every group one owner is full from every source. `filter_offsets`: the offsets -3 and 3 are always among them; offsets may repeat.
All inputs are finite; a program needn't handle non-finite values.
Results may differ from the reference program's by a relative error of at most 0.0003.
Values sent between devices are 32-bit elements; how exact they have to be, the bound alone decides.
No kernel may reach another device: no remote copies, remote signals or barrier semaphores. Data moves between devices by JAX's collectives and lax.ppermute only.
A program may use at most 64 MiB of HBM per device.

```python
import math
import jax
import jax.numpy as jnp
from jax import lax

P_SIZE = 256
L = 16
EDOF = 24
E_DEV = 1024
DR = 128
NK = 8
RADIUS = 3
GROUPS = 16
SLABS = 32
CAP = 64


def draw_panel_inverse(key, part):
    first_key, second_key = jax.random.split(key)
    diagonal = jax.random.uniform(first_key, (GROUPS, SLABS, P_SIZE), jnp.float32, 0.7, 1.3)
    spread = jax.random.normal(second_key, (GROUPS, SLABS, P_SIZE, P_SIZE), jnp.float32) * (0.3 / math.sqrt(P_SIZE))
    identity = jnp.eye(P_SIZE, dtype=jnp.float32)
    return spread * (1.0 - identity) + diagonal[..., :, None] * identity


def draw_stiffness(key, part):
    first_key, second_key = jax.random.split(key)
    raw_part = jax.random.normal(first_key, (EDOF, EDOF), jnp.float32) * 0.2
    diagonal = jax.random.uniform(second_key, (EDOF,), jnp.float32, 2.0, 4.0)
    identity = jnp.eye(EDOF, dtype=jnp.float32)
    return (raw_part + raw_part.T) * 0.5 * (1.0 - identity) + diagonal[:, None] * identity


def draw_receive_cells(key, part):
    first_key, second_key, third_key = jax.random.split(key, 3)
    halving = jax.random.randint(first_key, (GROUPS, SLABS, SLABS), 0, 4)
    full_owner = jax.random.randint(second_key, (GROUPS,), 0, SLABS)
    is_full = jnp.arange(SLABS, dtype=jnp.int32)[None, :, None] == full_owner[:, None, None]
    halving = jnp.where(is_full, 0, halving)
    live_count = CAP // jnp.left_shift(jnp.ones_like(halving), halving)
    cell_draw = jax.random.randint(third_key, (GROUPS, SLABS, SLABS, CAP), 0, DR * 128)
    slot_ids = jnp.arange(CAP, dtype=jnp.int32)
    return jnp.where(slot_ids < live_count[..., None], cell_draw, -1).astype(jnp.int32)


def draw_filter_offsets(key, part):
    others = jax.random.randint(key, (NK - 2,), -RADIUS, RADIUS + 1).astype(jnp.int32)
    ends = jnp.array([-RADIUS, RADIUS], dtype=jnp.int32)
    return jnp.concatenate([ends, others])


def set_ends(values, own_key, smallest, high):
    extent = values.shape
    spot = [jax.random.randint(jax.random.fold_in(own_key, axis), (), 0, extent[axis]) for axis in range(len(extent))]
    values = values.at[tuple(spot)].set(smallest)
    longest = extent.index(max(extent))
    spot[longest] = (spot[longest] + 1) % extent[longest]
    return values.at[tuple(spot)].set(high)


def block_scale(key, extent, shards, low, largest):
    def one(position, blocks):
        heights = jax.random.uniform(jax.random.fold_in(jax.random.fold_in(key, 6), position), (blocks,), jnp.float32, low / len(shards), largest / len(shards))
        return jnp.repeat(jnp.exp(heights), extent[position] // blocks).reshape((-1,) + (1,) * (len(extent) - position - 1))

    gain = one(*shards[0])
    for cut in shards[1:]:
        gain = gain * one(*cut)
    return gain


def bell_draw(own_key, dims, width, reach, cuts=(), kind=jnp.bfloat16):
    gain = block_scale(own_key, dims, cuts, -0.22, 0.18) if cuts else 1.0
    values = jax.random.normal(own_key, dims, jnp.float32) * width * gain
    return jnp.minimum(jnp.maximum(values, -reach), reach).astype(kind)


def setup_inputs(seed: int = 0) -> dict:
    arg_keys = jax.random.split(jax.random.key(seed), 13)
    panel_inverse = draw_panel_inverse(jax.random.fold_in(arg_keys[12], 71), 0)
    coupling = bell_draw(arg_keys[1], (GROUPS, SLABS, P_SIZE, P_SIZE), (0.9 * P_SIZE ** -0.5), 0.875, ((0, 16), (1, 32)), jnp.float32)
    loads = bell_draw(arg_keys[2], (GROUPS, SLABS, L, P_SIZE), 1.0, 6.0, ((0, 16), (1, 32)), jnp.float32)
    stiffness = draw_stiffness(jax.random.fold_in(arg_keys[12], 71), 0)
    element_substructure = set_ends(jax.random.randint(arg_keys[4], (GROUPS, SLABS, E_DEV), 0, SLABS), jax.random.fold_in(arg_keys[4], 1), 0, SLABS - 1).astype(jnp.int32)
    element_rows = set_ends(jax.random.randint(arg_keys[5], (GROUPS, SLABS, EDOF, E_DEV), 0, P_SIZE), jax.random.fold_in(arg_keys[5], 1), 0, P_SIZE - 1).astype(jnp.int32)
    element_density = jnp.clip(0.2 + 0.8 * jax.random.uniform(arg_keys[6], (GROUPS, SLABS, E_DEV), jnp.float32) ** block_scale(arg_keys[6], (GROUPS, SLABS, E_DEV), ((0, 16), (1, 32)), -0.2, 0.2), 0.2, 1.0)
    send_elements = set_ends(jax.random.randint(arg_keys[7], (GROUPS, SLABS, SLABS, CAP), 0, E_DEV), jax.random.fold_in(arg_keys[7], 1), 0, E_DEV - 1).astype(jnp.int32)
    receive_cells = draw_receive_cells(jax.random.fold_in(arg_keys[12], 71), 0)
    design_density = jnp.clip(0.3 + 0.7 * jax.random.uniform(arg_keys[9], (GROUPS, SLABS, DR, 128), jnp.float32) ** block_scale(arg_keys[9], (GROUPS, SLABS, DR, 128), ((0, 16), (1, 32)), -0.2, 0.2), 0.3, 1.0)
    filter_offsets = draw_filter_offsets(jax.random.fold_in(arg_keys[12], 71), 0)
    filter_weights = jnp.clip(jnp.exp(jax.random.uniform(arg_keys[11], (NK,), jnp.float32, math.log(0.2), math.log(1.0))), 0.2, 1.0)
    return dict(panel_inverse=panel_inverse, coupling=coupling, loads=loads, stiffness=stiffness, element_substructure=element_substructure, element_rows=element_rows, element_density=element_density, send_elements=send_elements, receive_cells=receive_cells, design_density=design_density, filter_offsets=filter_offsets, filter_weights=filter_weights)


exact_mode = lax.Precision.HIGHEST
penalty = 3.0
energy_scale = 1.0 / 4096.0


def reference(panel_inverse, coupling, loads, stiffness, element_substructure, element_rows, element_density, send_elements, receive_cells, design_density, filter_offsets, filter_weights):
    def level(previous, blocks):
        inverse, couple, rights = blocks
        pushed = jnp.einsum('sli,sij->slj', previous, couple, precision=exact_mode)
        current = jnp.einsum('sli,sij->slj', rights - pushed, inverse, precision=exact_mode)
        return current, current

    start = jnp.zeros((SLABS, L, P_SIZE), jnp.float32)
    _, interface = lax.scan(level, start, (panel_inverse, coupling, loads))

    def group_sens(blocks):
        panels, subs, rows, density = blocks
        columns = jnp.transpose(panels, (1, 0, 2)).reshape(L, SLABS * P_SIZE)
        lookup = (subs[:, None, :] * P_SIZE + rows).astype(jnp.int32)
        motion = jnp.take(columns, lookup, axis=1)
        forces = jnp.einsum('ij,lsje->lsie', stiffness, motion, precision=exact_mode)
        energy = jnp.sum(motion * forces, axis=(0, 2))
        return -penalty * density * density * energy * energy_scale

    sensitivity = lax.map(group_sens, (interface, element_substructure, element_rows, element_density))
    cells = DR * 128
    picked = jnp.take_along_axis(sensitivity, send_elements.reshape(GROUPS, SLABS, SLABS * CAP), axis=2)
    picked = jnp.transpose(picked.reshape(GROUPS, SLABS, SLABS, CAP), (0, 2, 1, 3))
    owner_ids = jnp.arange(GROUPS * SLABS, dtype=jnp.int32).reshape(GROUPS, SLABS, 1, 1)
    targets = jnp.where(receive_cells >= 0, receive_cells, cells).astype(jnp.int32)
    segment_ids = owner_ids * (cells + 1) + targets
    collected = jax.ops.segment_sum(picked.ravel(), segment_ids.ravel(), num_segments=GROUPS * SLABS * (cells + 1))
    collected = collected.reshape(GROUPS, SLABS, cells + 1)[:, :, :cells]
    weighted = design_density.reshape(GROUPS, SLABS * DR, 128) * collected.reshape(GROUPS, SLABS * DR, 128)
    padded = jnp.pad(weighted, ((0, 0), (RADIUS, RADIUS), (0, 0)))
    global_rows = jnp.arange(SLABS * DR, dtype=jnp.int32)
    accum = jnp.zeros((GROUPS, SLABS * DR, 128), jnp.float32)
    weight_sum = jnp.zeros((SLABS * DR,), jnp.float32)
    for which in range(NK):
        offset = filter_offsets[which].astype(jnp.int32)
        window_rows = lax.dynamic_slice_in_dim(padded, RADIUS + offset, SLABS * DR, 1)
        inside = ((global_rows + offset >= 0) & (global_rows + offset < SLABS * DR)).astype(jnp.float32)
        accum = accum + filter_weights[which] * window_rows
        weight_sum = weight_sum + filter_weights[which] * inside
    density_rows = design_density.reshape(GROUPS, SLABS * DR, 128)
    filtered = accum / (density_rows * weight_sum[None, :, None])
    return interface, filtered.reshape(GROUPS, SLABS, DR, 128)
```

```python
import jax
import jax.numpy as jnp
from jax import lax
from jax.sharding import PartitionSpec as P

NK = 8
RADIUS = 3


exact_mode = lax.Precision.HIGHEST
penalty = 3.0
energy_scale = 1.0 / 4096.0


def passed_along(value, axis, steps):
    count = lax.axis_size(axis)
    leading, last = (max(0, -steps), min(count, count - steps))
    return lax.ppermute(value, axis, [(source, source + steps) for source in range(leading, last)])


def padded_2(cells, sides, width):
    for axis, dim in sides:
        count = lax.axis_size(axis)
        ends = count - 1
        head = lax.slice_in_dim(cells, 0, width, axis=dim)
        tail = lax.slice_in_dim(cells, cells.shape[dim] - width, cells.shape[dim], axis=dim)
        cells = jnp.concatenate(
            [
                lax.ppermute(tail, axis, [(i, (i + 1) % count) for i in range(ends)]),
                cells,
                lax.ppermute(head, axis, [((i + 1) % count, i) for i in range(ends)]),
            ],
            axis=dim,
        )
    return cells


def product(left, right):
    return jnp.dot(left, right, precision=exact_mode, preferred_element_type=jnp.float32)


def interface_chain(inverse, couple, rights):
    offset = product(rights, inverse)
    step = -product(couple, inverse)
    order = rights.shape[0]
    levels = lax.axis_size("grp")
    shift = 1
    while shift < levels:
        if 2 * shift < levels:
            packed = passed_along(jnp.concatenate([offset, step], axis=0), "grp", shift)
            earlier_offset, earlier_step = packed[:order], packed[order:]
            offset = product(earlier_offset, step) + offset
            step = product(earlier_step, step)
        else:
            earlier_offset = passed_along(offset, "grp", shift)
            offset = product(earlier_offset, step) + offset
        shift *= 2
    return offset


def picked(values, index):
    lanes = 128
    table = values.reshape(-1, lanes)
    flat = index.reshape(-1)
    high = flat // lanes
    low = flat % lanes
    rows = jnp.zeros((flat.shape[0], lanes), values.dtype)
    for which in range(table.shape[0]):
        rows = rows + jnp.where((high == which)[:, None], table[which][None, :], 0.0)
    lane_ids = lax.broadcasted_iota(jnp.int32, (1, lanes), 1)
    chosen = jnp.sum(jnp.where(lane_ids == low[:, None], rows, 0.0), axis=1)
    return chosen.reshape(index.shape)


def scattered(values, targets, row_count):
    lanes = 128
    flat_values = values.reshape(-1)
    flat_targets = targets.reshape(-1)
    row = jnp.where(flat_targets >= 0, flat_targets // lanes, -1)
    col = flat_targets % lanes
    row_ids = lax.broadcasted_iota(jnp.int32, (1, row_count), 1)
    lane_ids = lax.broadcasted_iota(jnp.int32, (1, lanes), 1)
    rows_hot = (row[:, None] == row_ids).astype(jnp.float32)
    cols_hot = jnp.where(col[:, None] == lane_ids, flat_values[:, None], 0.0)
    return lax.dot_general(
        rows_hot,
        cols_hot,
        (((0,), (0,)), ((), ())),
        precision=exact_mode,
        preferred_element_type=jnp.float32,
    )


def on_device(
    panel_inverse,
    coupling,
    loads,
    stiffness,
    element_substructure,
    element_rows,
    element_density,
    send_elements,
    receive_cells,
    design_density,
    filter_offsets,
    filter_weights,
):
    inverse = panel_inverse[0, 0]
    couple = coupling[0, 0]
    rights = loads[0, 0]
    solved = interface_chain(inverse, couple, rights)

    panels = lax.all_gather(solved, "dev", axis=0, tiled=False)
    slabs, order, panel_order = panels.shape
    table = jnp.transpose(panels, (0, 2, 1)).reshape(slabs * panel_order, order)
    lookup = element_substructure[0, 0][None, :] * panel_order + element_rows[0, 0]
    dofs, elements = lookup.shape
    motion = jnp.take(table, lookup.reshape(-1), axis=0).reshape(dofs, elements, order)
    forces = jnp.einsum("ij,jel->iel", stiffness, motion, precision=exact_mode)
    energy = jnp.sum(motion * forces, axis=(0, 2))
    density = element_density[0, 0]
    sensitivity = -penalty * density * density * energy * energy_scale
    outgoing = picked(sensitivity, send_elements[0, 0])
    received = lax.all_to_all(outgoing, "dev", split_axis=0, concat_axis=0, tiled=True)
    owned = design_density[0, 0]
    row_count = owned.shape[0]
    collected = scattered(received, receive_cells[0, 0], row_count)
    weighted = owned * collected
    padded = padded_2(weighted, (("dev", 0),), RADIUS)
    total_rows = lax.axis_size("dev") * row_count
    global_rows = lax.axis_index("dev") * row_count + jnp.arange(row_count, dtype=jnp.int32)
    accum = jnp.zeros((row_count, 128), jnp.float32)
    weight_sum = jnp.zeros((row_count,), jnp.float32)
    for which in range(NK):
        offset = filter_offsets[which]
        window_rows = lax.dynamic_slice_in_dim(padded, RADIUS + offset, row_count, 0)
        inside = ((global_rows + offset >= 0) & (global_rows + offset < total_rows)).astype(
            jnp.float32
        )
        accum = accum + filter_weights[which] * window_rows
        weight_sum = weight_sum + filter_weights[which] * inside
    filtered = accum / (owned * weight_sum[:, None])
    return (solved[None, None], filtered[None, None])


def solution(mesh):
    placed = (
        P("grp", "dev", None, None),
        P("grp", "dev", None, None),
        P("grp", "dev", None, None),
        P(),
        P("grp", "dev", None),
        P("grp", "dev", None, None),
        P("grp", "dev", None),
        P("grp", "dev", None, None),
        P("grp", "dev", None, None),
        P("grp", "dev", None, None),
        P(),
        P(),
    )
    return jax.shard_map(
        on_device,
        mesh=mesh,
        in_specs=placed,
        out_specs=(P("grp", "dev", None, None), P("grp", "dev", None, None)),
        check_vma=False,
    )
```

```python
import jax
import jax.numpy as jnp
from jax import lax
from jax.sharding import PartitionSpec as P
from jax.experimental import pallas as pl
from jax.experimental.pallas import tpu as pltpu

NK = 8
RADIUS = 3


exact_mode = lax.Precision.HIGHEST
penalty = 3.0
energy_scale = 1.0 / 4096.0


def passed_along(value, axis, steps):
    count = lax.axis_size(axis)
    leading, last = (max(0, -steps), min(count, count - steps))
    return lax.ppermute(value, axis, [(source, source + steps) for source in range(leading, last)])


def padded_2(cells, sides, width):
    for axis, dim in sides:
        count = lax.axis_size(axis)
        ends = count - 1
        head = lax.slice_in_dim(cells, 0, width, axis=dim)
        tail = lax.slice_in_dim(cells, cells.shape[dim] - width, cells.shape[dim], axis=dim)
        cells = jnp.concatenate(
            [
                lax.ppermute(tail, axis, [(i, (i + 1) % count) for i in range(ends)]),
                cells,
                lax.ppermute(head, axis, [((i + 1) % count, i) for i in range(ends)]),
            ],
            axis=dim,
        )
    return cells


def product(left, right):
    return jnp.dot(left, right, precision=exact_mode, preferred_element_type=jnp.float32)


def interface_chain(inverse, couple, rights):
    offset = product(rights, inverse)
    step = -product(couple, inverse)
    order = rights.shape[0]
    levels = lax.axis_size("grp")
    shift = 1
    while shift < levels:
        if 2 * shift < levels:
            packed = passed_along(jnp.concatenate([offset, step], axis=0), "grp", shift)
            earlier_offset, earlier_step = packed[:order], packed[order:]
            offset = product(earlier_offset, step) + offset
            step = product(earlier_step, step)
        else:
            earlier_offset = passed_along(offset, "grp", shift)
            offset = product(earlier_offset, step) + offset
        shift *= 2
    return offset


def picked(values, index):
    lanes = 128
    table = values.reshape(-1, lanes)
    flat = index.reshape(-1)
    high = flat // lanes
    low = flat % lanes
    rows = jnp.zeros((flat.shape[0], lanes), values.dtype)
    for which in range(table.shape[0]):
        rows = rows + jnp.where((high == which)[:, None], table[which][None, :], 0.0)
    lane_ids = lax.broadcasted_iota(jnp.int32, (1, lanes), 1)
    chosen = jnp.sum(jnp.where(lane_ids == low[:, None], rows, 0.0), axis=1)
    return chosen.reshape(index.shape)


def scattered(values, targets, row_count):
    lanes = 128
    flat_values = values.reshape(-1)
    flat_targets = targets.reshape(-1)
    row = jnp.where(flat_targets >= 0, flat_targets // lanes, -1)
    col = flat_targets % lanes
    row_ids = lax.broadcasted_iota(jnp.int32, (1, row_count), 1)
    lane_ids = lax.broadcasted_iota(jnp.int32, (1, lanes), 1)
    rows_hot = (row[:, None] == row_ids).astype(jnp.float32)
    cols_hot = jnp.where(col[:, None] == lane_ids, flat_values[:, None], 0.0)
    return lax.dot_general(
        rows_hot,
        cols_hot,
        (((0,), (0,)), ((), ())),
        precision=exact_mode,
        preferred_element_type=jnp.float32,
    )


def gather_kernel(lookup_ref, table_ref, out_ref):
    chunk = pl.program_id(0)
    rows = out_ref.shape[0]
    pack = out_ref.shape[1] // 16
    group = lax.broadcasted_iota(jnp.int32, (1, out_ref.shape[1]), 1) // 16
    base = chunk * rows * pack

    def body(row, carry):
        packed_row = jnp.zeros((1, out_ref.shape[1]), jnp.float32)
        for part in range(pack):
            where = lookup_ref[base + row * pack + part]
            packed_row = jnp.where(group == part, table_ref[pl.ds(where, 1), :], packed_row)
        out_ref[pl.ds(row, 1), :] = packed_row
        return carry

    lax.fori_loop(0, rows, body, 0, unroll=8)


def gathered_rows(table, lookup):
    width = table.shape[1]
    pack = 128 // width
    wide = jnp.tile(table, (1, pack))
    total = lookup.shape[0]
    out_rows = total // pack
    chunks = 8
    rows = out_rows // chunks
    return pl.pallas_call(
        gather_kernel,
        out_shape=jax.ShapeDtypeStruct((out_rows, 128), jnp.float32),
        grid_spec=pltpu.PrefetchScalarGridSpec(
            num_scalar_prefetch=1,
            grid=(chunks,),
            in_specs=[pl.BlockSpec(wide.shape, lambda c, idx: (0, 0))],
            out_specs=pl.BlockSpec((rows, 128), lambda c, idx: (c, 0)),
        ),
        cost_estimate=pl.CostEstimate(flops=0, bytes_accessed=wide.size * 4 + out_rows * 512, transcendentals=0),
    )(lookup, wide)


def on_device(
    panel_inverse,
    coupling,
    loads,
    stiffness,
    element_substructure,
    element_rows,
    element_density,
    send_elements,
    receive_cells,
    design_density,
    filter_offsets,
    filter_weights,
):
    inverse = panel_inverse[0, 0]
    couple = coupling[0, 0]
    rights = loads[0, 0]
    solved = interface_chain(inverse, couple, rights)

    panels = lax.all_gather(solved, "dev", axis=0, tiled=False)
    slabs, order, panel_order = panels.shape
    table = jnp.transpose(panels, (0, 2, 1)).reshape(slabs * panel_order, order)
    lookup = element_substructure[0, 0][None, :] * panel_order + element_rows[0, 0]
    dofs, elements = lookup.shape
    pack = 128 // order
    motion = gathered_rows(table, lookup.reshape(-1)).reshape(dofs, elements // pack, 128)
    forces = jnp.einsum("ij,jab->iab", stiffness, motion, precision=exact_mode)
    energy = jnp.sum(jnp.sum(motion * forces, axis=0).reshape(elements // pack, pack, order), axis=2)
    energy = energy.reshape(elements)
    density = element_density[0, 0]
    sensitivity = -penalty * density * density * energy * energy_scale
    outgoing = picked(sensitivity, send_elements[0, 0])
    received = lax.all_to_all(outgoing, "dev", split_axis=0, concat_axis=0, tiled=True)
    owned = design_density[0, 0]
    row_count = owned.shape[0]
    collected = scattered(received, receive_cells[0, 0], row_count)
    weighted = owned * collected
    padded = padded_2(weighted, (("dev", 0),), RADIUS)
    total_rows = lax.axis_size("dev") * row_count
    global_rows = lax.axis_index("dev") * row_count + jnp.arange(row_count, dtype=jnp.int32)
    accum = jnp.zeros((row_count, 128), jnp.float32)
    weight_sum = jnp.zeros((row_count,), jnp.float32)
    for which in range(NK):
        offset = filter_offsets[which]
        window_rows = lax.dynamic_slice_in_dim(padded, RADIUS + offset, row_count, 0)
        inside = ((global_rows + offset >= 0) & (global_rows + offset < total_rows)).astype(
            jnp.float32
        )
        accum = accum + filter_weights[which] * window_rows
        weight_sum = weight_sum + filter_weights[which] * inside
    filtered = accum / (owned * weight_sum[:, None])
    return (solved[None, None], filtered[None, None])


def solution(mesh):
    placed = (
        P("grp", "dev", None, None),
        P("grp", "dev", None, None),
        P("grp", "dev", None, None),
        P(),
        P("grp", "dev", None),
        P("grp", "dev", None, None),
        P("grp", "dev", None),
        P("grp", "dev", None, None),
        P("grp", "dev", None, None),
        P("grp", "dev", None, None),
        P(),
        P(),
    )
    return jax.shard_map(
        on_device,
        mesh=mesh,
        in_specs=placed,
        out_specs=(P("grp", "dev", None, None), P("grp", "dev", None, None)),
        check_vma=False,
    )
```

```python
import jax
import jax.numpy as jnp
from jax import lax
from jax.sharding import PartitionSpec as P
from jax.experimental import pallas as pl
from jax.experimental.pallas import tpu as pltpu

NK = 8
RADIUS = 3


exact_mode = lax.Precision.HIGHEST
penalty = 3.0
energy_scale = 1.0 / 4096.0


def passed_along(value, axis, steps):
    count = lax.axis_size(axis)
    leading, last = (max(0, -steps), min(count, count - steps))
    return lax.ppermute(value, axis, [(source, source + steps) for source in range(leading, last)])


def padded_2(cells, sides, width):
    for axis, dim in sides:
        count = lax.axis_size(axis)
        ends = count - 1
        head = lax.slice_in_dim(cells, 0, width, axis=dim)
        tail = lax.slice_in_dim(cells, cells.shape[dim] - width, cells.shape[dim], axis=dim)
        cells = jnp.concatenate(
            [
                lax.ppermute(tail, axis, [(i, (i + 1) % count) for i in range(ends)]),
                cells,
                lax.ppermute(head, axis, [((i + 1) % count, i) for i in range(ends)]),
            ],
            axis=dim,
        )
    return cells


def product(left, right):
    return jnp.dot(left, right, precision=exact_mode, preferred_element_type=jnp.float32)


def interface_chain(inverse, couple, rights):
    offset = product(rights, inverse)
    step = -product(couple, inverse)
    order = rights.shape[0]
    levels = lax.axis_size("grp")
    shift = 1
    while shift < levels:
        if 2 * shift < levels:
            packed = passed_along(jnp.concatenate([offset, step], axis=0), "grp", shift)
            earlier_offset, earlier_step = packed[:order], packed[order:]
            offset = product(earlier_offset, step) + offset
            step = product(earlier_step, step)
        else:
            earlier_offset = passed_along(offset, "grp", shift)
            offset = product(earlier_offset, step) + offset
        shift *= 2
    return offset


def picked(values, index):
    lanes = 128
    table = values.reshape(-1, lanes)
    flat = index.reshape(-1)
    high = flat // lanes
    low = flat % lanes
    rows = jnp.zeros((flat.shape[0], lanes), values.dtype)
    for which in range(table.shape[0]):
        rows = rows + jnp.where((high == which)[:, None], table[which][None, :], 0.0)
    lane_ids = lax.broadcasted_iota(jnp.int32, (1, lanes), 1)
    chosen = jnp.sum(jnp.where(lane_ids == low[:, None], rows, 0.0), axis=1)
    return chosen.reshape(index.shape)


def scattered(values, targets, row_count):
    lanes = 128
    flat_values = values.reshape(-1)
    flat_targets = targets.reshape(-1)
    row = jnp.where(flat_targets >= 0, flat_targets // lanes, -1)
    col = flat_targets % lanes
    row_ids = lax.broadcasted_iota(jnp.int32, (1, row_count), 1)
    lane_ids = lax.broadcasted_iota(jnp.int32, (1, lanes), 1)
    rows_hot = (row[:, None] == row_ids).astype(jnp.float32)
    cols_hot = jnp.where(col[:, None] == lane_ids, flat_values[:, None], 0.0)
    return lax.dot_general(
        rows_hot,
        cols_hot,
        (((0,), (0,)), ((), ())),
        precision=exact_mode,
        preferred_element_type=jnp.float32,
    )


def gather_kernel(lookup_ref, table_ref, out_ref):
    chunk = pl.program_id(0)
    rows = out_ref.shape[0]
    pack = out_ref.shape[1] // 16
    group = lax.broadcasted_iota(jnp.int32, (1, out_ref.shape[1]), 1) // 16
    base = chunk * rows * pack

    def body(row, carry):
        packed_row = jnp.zeros((1, out_ref.shape[1]), jnp.float32)
        for part in range(pack):
            where = lookup_ref[base + row * pack + part]
            packed_row = jnp.where(group == part, table_ref[pl.ds(where, 1), :], packed_row)
        out_ref[pl.ds(row, 1), :] = packed_row
        return carry

    lax.fori_loop(0, rows, body, 0, unroll=8)


def gathered_rows(table, lookup):
    width = table.shape[1]
    pack = 128 // width
    wide = jnp.tile(table, (1, pack))
    total = lookup.shape[0]
    out_rows = total // pack
    chunks = 8
    rows = out_rows // chunks
    return pl.pallas_call(
        gather_kernel,
        out_shape=jax.ShapeDtypeStruct((out_rows, 128), jnp.float32),
        grid_spec=pltpu.PrefetchScalarGridSpec(
            num_scalar_prefetch=1,
            grid=(chunks,),
            in_specs=[pl.BlockSpec(wide.shape, lambda c, idx: (0, 0))],
            out_specs=pl.BlockSpec((rows, 128), lambda c, idx: (c, 0)),
        ),
        cost_estimate=pl.CostEstimate(flops=0, bytes_accessed=wide.size * 4 + out_rows * 512, transcendentals=0),
    )(lookup, wide)


def gathered_panels(solved):
    count = lax.axis_size("dev")
    me = lax.axis_index("dev")
    bits = count.bit_length() - 1
    order = [bits - 1, 1, bits - 2, bits - 3, 0] if bits == 5 else list(range(bits))
    block = solved[None]
    for bit in order:
        partner = [(i, i ^ (1 << bit)) for i in range(count)]
        other = lax.ppermute(block, "dev", partner)
        high = ((me >> bit) & 1) == 1
        block = jnp.where(high, jnp.concatenate([other, block], 0), jnp.concatenate([block, other], 0))
    slab = jnp.arange(count, dtype=jnp.int32)
    position = jnp.zeros_like(slab)
    for place, bit in enumerate(order):
        position = position + (((slab >> bit) & 1) << place)
    return block, position


def on_device(
    panel_inverse,
    coupling,
    loads,
    stiffness,
    element_substructure,
    element_rows,
    element_density,
    send_elements,
    receive_cells,
    design_density,
    filter_offsets,
    filter_weights,
):
    inverse = panel_inverse[0, 0]
    couple = coupling[0, 0]
    rights = loads[0, 0]
    solved = interface_chain(inverse, couple, rights)

    panels, position = gathered_panels(solved)
    slabs, order, panel_order = panels.shape
    table = jnp.transpose(panels, (0, 2, 1)).reshape(slabs * panel_order, order)
    slab_place = jnp.take(position, element_substructure[0, 0], axis=0)
    lookup = slab_place[None, :] * panel_order + element_rows[0, 0]
    dofs, elements = lookup.shape
    pack = 128 // order
    motion = gathered_rows(table, lookup.reshape(-1)).reshape(dofs, elements // pack, 128)
    forces = jnp.einsum("ij,jab->iab", stiffness, motion, precision=exact_mode)
    energy = jnp.sum(jnp.sum(motion * forces, axis=0).reshape(elements // pack, pack, order), axis=2)
    energy = energy.reshape(elements)
    density = element_density[0, 0]
    sensitivity = -penalty * density * density * energy * energy_scale
    outgoing = picked(sensitivity, send_elements[0, 0])
    received = lax.all_to_all(outgoing, "dev", split_axis=0, concat_axis=0, tiled=True)
    owned = design_density[0, 0]
    row_count = owned.shape[0]
    collected = scattered(received, receive_cells[0, 0], row_count)
    weighted = owned * collected
    padded = padded_2(weighted, (("dev", 0),), RADIUS)
    total_rows = lax.axis_size("dev") * row_count
    global_rows = lax.axis_index("dev") * row_count + jnp.arange(row_count, dtype=jnp.int32)
    accum = jnp.zeros((row_count, 128), jnp.float32)
    weight_sum = jnp.zeros((row_count,), jnp.float32)
    for which in range(NK):
        offset = filter_offsets[which]
        window_rows = lax.dynamic_slice_in_dim(padded, RADIUS + offset, row_count, 0)
        inside = ((global_rows + offset >= 0) & (global_rows + offset < total_rows)).astype(
            jnp.float32
        )
        accum = accum + filter_weights[which] * window_rows
        weight_sum = weight_sum + filter_weights[which] * inside
    filtered = accum / (owned * weight_sum[:, None])
    return (solved[None, None], filtered[None, None])


def solution(mesh):
    placed = (
        P("grp", "dev", None, None),
        P("grp", "dev", None, None),
        P("grp", "dev", None, None),
        P(),
        P("grp", "dev", None),
        P("grp", "dev", None, None),
        P("grp", "dev", None),
        P("grp", "dev", None, None),
        P("grp", "dev", None, None),
        P("grp", "dev", None, None),
        P(),
        P(),
    )
    return jax.shard_map(
        on_device,
        mesh=mesh,
        in_specs=placed,
        out_specs=(P("grp", "dev", None, None), P("grp", "dev", None, None)),
        check_vma=False,
    )
```

```python
import jax
import jax.numpy as jnp
from jax import lax
from jax.sharding import PartitionSpec as P
from jax.experimental import pallas as pl
from jax.experimental.pallas import tpu as pltpu

NK = 8
RADIUS = 3


exact_mode = lax.Precision.HIGHEST
penalty = 3.0
energy_scale = 1.0 / 4096.0


def passed_along(value, axis, steps):
    count = lax.axis_size(axis)
    leading, last = (max(0, -steps), min(count, count - steps))
    return lax.ppermute(value, axis, [(source, source + steps) for source in range(leading, last)])


def padded_2(cells, sides, width):
    for axis, dim in sides:
        count = lax.axis_size(axis)
        ends = count - 1
        head = lax.slice_in_dim(cells, 0, width, axis=dim)
        tail = lax.slice_in_dim(cells, cells.shape[dim] - width, cells.shape[dim], axis=dim)
        cells = jnp.concatenate(
            [
                lax.ppermute(tail, axis, [(i, (i + 1) % count) for i in range(ends)]),
                cells,
                lax.ppermute(head, axis, [((i + 1) % count, i) for i in range(ends)]),
            ],
            axis=dim,
        )
    return cells


def product(left, right):
    return jnp.dot(left, right, precision=exact_mode, preferred_element_type=jnp.float32)


def interface_chain(inverse, couple, rights):
    offset = product(rights, inverse)
    step = -product(couple, inverse)
    order = rights.shape[0]
    levels = lax.axis_size("grp")
    shift = 1
    while shift < levels:
        if 2 * shift < levels:
            packed = passed_along(jnp.concatenate([offset, step], axis=0), "grp", shift)
            earlier_offset, earlier_step = packed[:order], packed[order:]
            offset = product(earlier_offset, step) + offset
            step = product(earlier_step, step)
        else:
            earlier_offset = passed_along(offset, "grp", shift)
            offset = product(earlier_offset, step) + offset
        shift *= 2
    return offset


def picked(values, index):
    lanes = 128
    table = values.reshape(-1, lanes)
    flat = index.reshape(-1)
    high = flat // lanes
    low = flat % lanes
    rows = jnp.zeros((flat.shape[0], lanes), values.dtype)
    for which in range(table.shape[0]):
        rows = rows + jnp.where((high == which)[:, None], table[which][None, :], 0.0)
    lane_ids = lax.broadcasted_iota(jnp.int32, (1, lanes), 1)
    chosen = jnp.sum(jnp.where(lane_ids == low[:, None], rows, 0.0), axis=1)
    return chosen.reshape(index.shape)


def scattered(values, targets, row_count):
    lanes = 128
    flat_values = values.reshape(-1)
    flat_targets = targets.reshape(-1)
    row = jnp.where(flat_targets >= 0, flat_targets // lanes, -1)
    col = flat_targets % lanes
    row_ids = lax.broadcasted_iota(jnp.int32, (1, row_count), 1)
    lane_ids = lax.broadcasted_iota(jnp.int32, (1, lanes), 1)
    rows_hot = (row[:, None] == row_ids).astype(jnp.float32)
    cols_hot = jnp.where(col[:, None] == lane_ids, flat_values[:, None], 0.0)
    return lax.dot_general(
        rows_hot,
        cols_hot,
        (((0,), (0,)), ((), ())),
        precision=exact_mode,
        preferred_element_type=jnp.float32,
    )


def gather_kernel(lookup_ref, table_ref, out_ref):
    chunk = pl.program_id(0)
    rows = out_ref.shape[0]
    pack = out_ref.shape[1] // 16
    group = lax.broadcasted_iota(jnp.int32, (1, out_ref.shape[1]), 1) // 16
    base = chunk * rows * pack

    def body(row, carry):
        packed_row = jnp.zeros((1, out_ref.shape[1]), jnp.float32)
        for part in range(pack):
            where = lookup_ref[base + row * pack + part]
            packed_row = jnp.where(group == part, table_ref[pl.ds(where, 1), :], packed_row)
        out_ref[pl.ds(row, 1), :] = packed_row
        return carry

    lax.fori_loop(0, rows, body, 0, unroll=8)


def gathered_rows(table, lookup):
    width = table.shape[1]
    pack = 128 // width
    wide = jnp.tile(table, (1, pack))
    total = lookup.shape[0]
    out_rows = total // pack
    chunks = 8
    rows = out_rows // chunks
    return pl.pallas_call(
        gather_kernel,
        out_shape=jax.ShapeDtypeStruct((out_rows, 128), jnp.float32),
        grid_spec=pltpu.PrefetchScalarGridSpec(
            num_scalar_prefetch=1,
            grid=(chunks,),
            in_specs=[pl.BlockSpec(wide.shape, lambda c, idx: (0, 0))],
            out_specs=pl.BlockSpec((rows, 128), lambda c, idx: (c, 0)),
        ),
        cost_estimate=pl.CostEstimate(flops=0, bytes_accessed=wide.size * 4 + out_rows * 512, transcendentals=0),
    )(lookup, wide)


def gathered_panels(solved):
    count = lax.axis_size("dev")
    me = lax.axis_index("dev")
    bits = count.bit_length() - 1
    order = [bits - 1, 1, bits - 2, bits - 3, 0] if bits == 5 else list(range(bits))
    block = solved[None]
    for bit in order:
        partner = [(i, i ^ (1 << bit)) for i in range(count)]
        other = lax.ppermute(block, "dev", partner)
        high = ((me >> bit) & 1) == 1
        block = jnp.where(high, jnp.concatenate([other, block], 0), jnp.concatenate([block, other], 0))
    return block, order


def slab_position(slab, order):
    position = jnp.zeros_like(slab)
    for place, bit in enumerate(order):
        position = position + (((slab >> bit) & 1) << place)
    return position


def on_device(
    panel_inverse,
    coupling,
    loads,
    stiffness,
    element_substructure,
    element_rows,
    element_density,
    send_elements,
    receive_cells,
    design_density,
    filter_offsets,
    filter_weights,
):
    inverse = panel_inverse[0, 0]
    couple = coupling[0, 0]
    rights = loads[0, 0]
    solved = interface_chain(inverse, couple, rights)

    panels, bit_order = gathered_panels(solved)
    slabs, order, panel_order = panels.shape
    table = jnp.transpose(panels, (0, 2, 1)).reshape(slabs * panel_order, order)
    slab_place = slab_position(element_substructure[0, 0], bit_order)
    lookup = slab_place[None, :] * panel_order + element_rows[0, 0]
    dofs, elements = lookup.shape
    pack = 128 // order
    motion = gathered_rows(table, lookup.reshape(-1)).reshape(dofs, elements // pack, 128)
    forces = jnp.einsum("ij,jab->iab", stiffness, motion, precision=exact_mode)
    energy = jnp.sum(jnp.sum(motion * forces, axis=0).reshape(elements // pack, pack, order), axis=2)
    energy = energy.reshape(elements)
    density = element_density[0, 0]
    sensitivity = -penalty * density * density * energy * energy_scale
    outgoing = picked(sensitivity, send_elements[0, 0])
    received = lax.all_to_all(outgoing, "dev", split_axis=0, concat_axis=0, tiled=True)
    owned = design_density[0, 0]
    row_count = owned.shape[0]
    collected = scattered(received, receive_cells[0, 0], row_count)
    weighted = owned * collected
    padded = padded_2(weighted, (("dev", 0),), RADIUS)
    total_rows = lax.axis_size("dev") * row_count
    padded_rows = padded.shape[0]
    reach = (
        lax.broadcasted_iota(jnp.int32, (1, row_count, padded_rows), 2)
        - lax.broadcasted_iota(jnp.int32, (1, row_count, padded_rows), 1)
        - RADIUS
    )
    band = jnp.sum(
        jnp.where(reach == filter_offsets[:, None, None], filter_weights[:, None, None], 0.0), axis=0
    )
    padded_global = lax.axis_index("dev") * row_count - RADIUS + jnp.arange(padded_rows, dtype=jnp.int32)
    valid = ((padded_global >= 0) & (padded_global < total_rows)).astype(jnp.float32)
    weight_sum = jnp.sum(band * valid[None, :], axis=1)
    accum = product(band, padded)
    filtered = accum / (owned * weight_sum[:, None])
    return (solved[None, None], filtered[None, None])


def solution(mesh):
    placed = (
        P("grp", "dev", None, None),
        P("grp", "dev", None, None),
        P("grp", "dev", None, None),
        P(),
        P("grp", "dev", None),
        P("grp", "dev", None, None),
        P("grp", "dev", None),
        P("grp", "dev", None, None),
        P("grp", "dev", None, None),
        P("grp", "dev", None, None),
        P(),
        P(),
    )
    return jax.shard_map(
        on_device,
        mesh=mesh,
        in_specs=placed,
        out_specs=(P("grp", "dev", None, None), P("grp", "dev", None, None)),
        check_vma=False,
    )
```

```python
import jax
import jax.numpy as jnp
from jax import lax
from jax.sharding import PartitionSpec as P
from jax.experimental import pallas as pl
from jax.experimental.pallas import tpu as pltpu

NK = 8
RADIUS = 3


exact_mode = lax.Precision.HIGHEST
penalty = 3.0
energy_scale = 1.0 / 4096.0


def passed_along(value, axis, steps):
    count = lax.axis_size(axis)
    leading, last = (max(0, -steps), min(count, count - steps))
    return lax.ppermute(value, axis, [(source, source + steps) for source in range(leading, last)])


def padded_2(cells, sides, width):
    for axis, dim in sides:
        count = lax.axis_size(axis)
        ends = count - 1
        head = lax.slice_in_dim(cells, 0, width, axis=dim)
        tail = lax.slice_in_dim(cells, cells.shape[dim] - width, cells.shape[dim], axis=dim)
        cells = jnp.concatenate(
            [
                lax.ppermute(tail, axis, [(i, (i + 1) % count) for i in range(ends)]),
                cells,
                lax.ppermute(head, axis, [((i + 1) % count, i) for i in range(ends)]),
            ],
            axis=dim,
        )
    return cells


def product(left, right):
    return jnp.dot(left, right, precision=exact_mode, preferred_element_type=jnp.float32)


def interface_chain(inverse, couple, rights):
    offset = product(rights, inverse)
    step = -product(couple, inverse)
    order = rights.shape[0]
    levels = lax.axis_size("grp")
    shift = 1
    while shift < levels:
        if 2 * shift < levels:
            packed = passed_along(jnp.concatenate([offset, step], axis=0), "grp", shift)
            earlier_offset, earlier_step = packed[:order], packed[order:]
            offset = product(earlier_offset, step) + offset
            step = product(earlier_step, step)
        else:
            earlier_offset = passed_along(offset, "grp", shift)
            offset = product(earlier_offset, step) + offset
        shift *= 2
    return offset


def picked(values, index):
    lanes = 128
    table = values.reshape(-1, lanes)
    flat = index.reshape(-1)
    high = flat // lanes
    low = flat % lanes
    rows = jnp.zeros((flat.shape[0], lanes), values.dtype)
    for which in range(table.shape[0]):
        rows = rows + jnp.where((high == which)[:, None], table[which][None, :], 0.0)
    lane_ids = lax.broadcasted_iota(jnp.int32, (1, lanes), 1)
    chosen = jnp.sum(jnp.where(lane_ids == low[:, None], rows, 0.0), axis=1)
    return chosen.reshape(index.shape)


def scattered(values, targets, row_count):
    lanes = 128
    flat_values = values.reshape(-1)
    flat_targets = targets.reshape(-1)
    row = jnp.where(flat_targets >= 0, flat_targets // lanes, -1)
    col = flat_targets % lanes
    row_ids = lax.broadcasted_iota(jnp.int32, (1, row_count), 1)
    lane_ids = lax.broadcasted_iota(jnp.int32, (1, lanes), 1)
    rows_hot = (row[:, None] == row_ids).astype(jnp.float32)
    cols_hot = jnp.where(col[:, None] == lane_ids, flat_values[:, None], 0.0)
    return lax.dot_general(
        rows_hot,
        cols_hot,
        (((0,), (0,)), ((), ())),
        precision=exact_mode,
        preferred_element_type=jnp.float32,
    )


def gather_kernel(lookup_ref, table_ref, out_ref):
    chunk = pl.program_id(0)
    rows = out_ref.shape[0]
    pack = out_ref.shape[1] // 16
    group = lax.broadcasted_iota(jnp.int32, (1, out_ref.shape[1]), 1) // 16
    base = chunk * rows * pack

    def body(row, carry):
        packed_row = jnp.zeros((1, out_ref.shape[1]), jnp.float32)
        for part in range(pack):
            where = lookup_ref[base + row * pack + part]
            packed_row = jnp.where(group == part, table_ref[pl.ds(where, 1), :], packed_row)
        out_ref[pl.ds(row, 1), :] = packed_row
        return carry

    lax.fori_loop(0, rows, body, 0, unroll=8)


def gathered_rows(table, lookup):
    width = table.shape[1]
    pack = 128 // width
    wide = jnp.tile(table, (1, pack))
    total = lookup.shape[0]
    out_rows = total // pack
    chunks = 8
    rows = out_rows // chunks
    return pl.pallas_call(
        gather_kernel,
        out_shape=jax.ShapeDtypeStruct((out_rows, 128), jnp.float32),
        grid_spec=pltpu.PrefetchScalarGridSpec(
            num_scalar_prefetch=1,
            grid=(chunks,),
            in_specs=[pl.BlockSpec(wide.shape, lambda c, idx: (0, 0))],
            out_specs=pl.BlockSpec((rows, 128), lambda c, idx: (c, 0)),
        ),
        cost_estimate=pl.CostEstimate(flops=0, bytes_accessed=wide.size * 4 + out_rows * 512, transcendentals=0),
    )(lookup, wide)


def gathered_panels(solved):
    count = lax.axis_size("dev")
    me = lax.axis_index("dev")
    bits = count.bit_length() - 1
    order = [bits - 1, 1, bits - 2, bits - 3, 0] if bits == 5 else list(range(bits))
    block = solved[None]
    for bit in order:
        partner = [(i, i ^ (1 << bit)) for i in range(count)]
        other = lax.ppermute(block, "dev", partner)
        high = ((me >> bit) & 1) == 1
        block = jnp.where(high, jnp.concatenate([other, block], 0), jnp.concatenate([block, other], 0))
    return block, order


def slab_position(slab, order):
    position = jnp.zeros_like(slab)
    for place, bit in enumerate(order):
        position = position + (((slab >> bit) & 1) << place)
    return position


def on_device(
    panel_inverse,
    coupling,
    loads,
    stiffness,
    element_substructure,
    element_rows,
    element_density,
    send_elements,
    receive_cells,
    design_density,
    filter_offsets,
    filter_weights,
):
    inverse = panel_inverse[0, 0]
    couple = coupling[0, 0]
    rights = loads[0, 0]
    solved = interface_chain(inverse, couple, rights)

    copies = jnp.broadcast_to(solved[None], (lax.axis_size("dev"),) + solved.shape)
    panels = lax.all_to_all(copies, "dev", split_axis=0, concat_axis=0, tiled=True)
    slabs, order, panel_order = panels.shape
    table = jnp.transpose(panels, (0, 2, 1)).reshape(slabs * panel_order, order)
    slab_place = element_substructure[0, 0]
    lookup = slab_place[None, :] * panel_order + element_rows[0, 0]
    dofs, elements = lookup.shape
    pack = 128 // order
    motion = gathered_rows(table, lookup.reshape(-1)).reshape(dofs, elements // pack, 128)
    forces = jnp.einsum("ij,jab->iab", stiffness, motion, precision=exact_mode)
    energy = jnp.sum(jnp.sum(motion * forces, axis=0).reshape(elements // pack, pack, order), axis=2)
    energy = energy.reshape(elements)
    density = element_density[0, 0]
    sensitivity = -penalty * density * density * energy * energy_scale
    outgoing = picked(sensitivity, send_elements[0, 0])
    received = lax.all_to_all(outgoing, "dev", split_axis=0, concat_axis=0, tiled=True)
    owned = design_density[0, 0]
    row_count = owned.shape[0]
    collected = scattered(received, receive_cells[0, 0], row_count)
    weighted = owned * collected
    padded = padded_2(weighted, (("dev", 0),), RADIUS)
    total_rows = lax.axis_size("dev") * row_count
    padded_rows = padded.shape[0]
    reach = (
        lax.broadcasted_iota(jnp.int32, (1, row_count, padded_rows), 2)
        - lax.broadcasted_iota(jnp.int32, (1, row_count, padded_rows), 1)
        - RADIUS
    )
    band = jnp.sum(
        jnp.where(reach == filter_offsets[:, None, None], filter_weights[:, None, None], 0.0), axis=0
    )
    padded_global = lax.axis_index("dev") * row_count - RADIUS + jnp.arange(padded_rows, dtype=jnp.int32)
    valid = ((padded_global >= 0) & (padded_global < total_rows)).astype(jnp.float32)
    weight_sum = jnp.sum(band * valid[None, :], axis=1)
    accum = product(band, padded)
    filtered = accum / (owned * weight_sum[:, None])
    return (solved[None, None], filtered[None, None])


def solution(mesh):
    placed = (
        P("grp", "dev", None, None),
        P("grp", "dev", None, None),
        P("grp", "dev", None, None),
        P(),
        P("grp", "dev", None),
        P("grp", "dev", None, None),
        P("grp", "dev", None),
        P("grp", "dev", None, None),
        P("grp", "dev", None, None),
        P("grp", "dev", None, None),
        P(),
        P(),
    )
    return jax.shard_map(
        on_device,
        mesh=mesh,
        in_specs=placed,
        out_specs=(P("grp", "dev", None, None), P("grp", "dev", None, None)),
        check_vma=False,
    )
```

```python
import jax
import jax.numpy as jnp
from jax import lax
from jax.sharding import PartitionSpec as P
from jax.experimental import pallas as pl
from jax.experimental.pallas import tpu as pltpu

NK = 8
RADIUS = 3


exact_mode = lax.Precision.HIGHEST
penalty = 3.0
energy_scale = 1.0 / 4096.0


def passed_along(value, axis, steps):
    count = lax.axis_size(axis)
    leading, last = (max(0, -steps), min(count, count - steps))
    return lax.ppermute(value, axis, [(source, source + steps) for source in range(leading, last)])


def padded_2(cells, sides, width):
    for axis, dim in sides:
        count = lax.axis_size(axis)
        ends = count - 1
        head = lax.slice_in_dim(cells, 0, width, axis=dim)
        tail = lax.slice_in_dim(cells, cells.shape[dim] - width, cells.shape[dim], axis=dim)
        cells = jnp.concatenate(
            [
                lax.ppermute(tail, axis, [(i, (i + 1) % count) for i in range(ends)]),
                cells,
                lax.ppermute(head, axis, [((i + 1) % count, i) for i in range(ends)]),
            ],
            axis=dim,
        )
    return cells


def product(left, right):
    return jnp.dot(left, right, precision=exact_mode, preferred_element_type=jnp.float32)


def interface_chain(inverse, couple, rights):
    offset = product(rights, inverse)
    step = -product(couple, inverse)
    order = rights.shape[0]
    levels = lax.axis_size("grp")

    def combine(pairs, with_step):
        nonlocal offset, composite
        if with_step:
            packed = lax.ppermute(jnp.concatenate([offset, composite], axis=0), "grp", pairs)
            earlier_offset, earlier_step = packed[:order], packed[order:]
            offset = product(earlier_offset, composite) + offset
            composite = product(earlier_step, composite)
        else:
            earlier_offset = lax.ppermute(offset, "grp", pairs)
            offset = product(earlier_offset, composite) + offset

    composite = step
    combine([(g, g + 1) for g in range(0, levels - 1, 2)], True)
    shift = 2
    while shift < levels:
        pairs = [(g, g + shift) for g in range(1, levels - shift, 2)]
        combine(pairs, 2 * shift < levels)
        shift *= 2
    earlier_offset = lax.ppermute(offset, "grp", [(g, g + 1) for g in range(1, levels - 1, 2)])
    return product(earlier_offset, step) + offset


def picked(values, index):
    lanes = 128
    table = values.reshape(-1, lanes)
    flat = index.reshape(-1)
    high = flat // lanes
    low = flat % lanes
    rows = jnp.zeros((flat.shape[0], lanes), values.dtype)
    for which in range(table.shape[0]):
        rows = rows + jnp.where((high == which)[:, None], table[which][None, :], 0.0)
    lane_ids = lax.broadcasted_iota(jnp.int32, (1, lanes), 1)
    chosen = jnp.sum(jnp.where(lane_ids == low[:, None], rows, 0.0), axis=1)
    return chosen.reshape(index.shape)


def scattered(values, targets, row_count):
    lanes = 128
    flat_values = values.reshape(-1)
    flat_targets = targets.reshape(-1)
    row = jnp.where(flat_targets >= 0, flat_targets // lanes, -1)
    col = flat_targets % lanes
    row_ids = lax.broadcasted_iota(jnp.int32, (1, row_count), 1)
    lane_ids = lax.broadcasted_iota(jnp.int32, (1, lanes), 1)
    rows_hot = (row[:, None] == row_ids).astype(jnp.float32)
    cols_hot = jnp.where(col[:, None] == lane_ids, flat_values[:, None], 0.0)
    return lax.dot_general(
        rows_hot,
        cols_hot,
        (((0,), (0,)), ((), ())),
        precision=exact_mode,
        preferred_element_type=jnp.float32,
    )


def gather_kernel(lookup_ref, table_ref, out_ref):
    chunk = pl.program_id(0)
    rows = out_ref.shape[0]
    pack = out_ref.shape[1] // 16
    group = lax.broadcasted_iota(jnp.int32, (1, out_ref.shape[1]), 1) // 16
    base = chunk * rows * pack

    def body(row, carry):
        packed_row = jnp.zeros((1, out_ref.shape[1]), jnp.float32)
        for part in range(pack):
            where = lookup_ref[base + row * pack + part]
            packed_row = jnp.where(group == part, table_ref[pl.ds(where, 1), :], packed_row)
        out_ref[pl.ds(row, 1), :] = packed_row
        return carry

    lax.fori_loop(0, rows, body, 0, unroll=8)


def gathered_rows(table, lookup):
    width = table.shape[1]
    pack = 128 // width
    wide = jnp.tile(table, (1, pack))
    total = lookup.shape[0]
    out_rows = total // pack
    chunks = 8
    rows = out_rows // chunks
    return pl.pallas_call(
        gather_kernel,
        out_shape=jax.ShapeDtypeStruct((out_rows, 128), jnp.float32),
        grid_spec=pltpu.PrefetchScalarGridSpec(
            num_scalar_prefetch=1,
            grid=(chunks,),
            in_specs=[pl.BlockSpec(wide.shape, lambda c, idx: (0, 0))],
            out_specs=pl.BlockSpec((rows, 128), lambda c, idx: (c, 0)),
        ),
        cost_estimate=pl.CostEstimate(flops=0, bytes_accessed=wide.size * 4 + out_rows * 512, transcendentals=0),
    )(lookup, wide)


def gathered_panels(solved):
    count = lax.axis_size("dev")
    me = lax.axis_index("dev")
    bits = count.bit_length() - 1
    order = [bits - 1, 1, bits - 2, bits - 3, 0] if bits == 5 else list(range(bits))
    block = solved[None]
    for bit in order:
        partner = [(i, i ^ (1 << bit)) for i in range(count)]
        other = lax.ppermute(block, "dev", partner)
        high = ((me >> bit) & 1) == 1
        block = jnp.where(high, jnp.concatenate([other, block], 0), jnp.concatenate([block, other], 0))
    return block, order


def slab_position(slab, order):
    position = jnp.zeros_like(slab)
    for place, bit in enumerate(order):
        position = position + (((slab >> bit) & 1) << place)
    return position


def on_device(
    panel_inverse,
    coupling,
    loads,
    stiffness,
    element_substructure,
    element_rows,
    element_density,
    send_elements,
    receive_cells,
    design_density,
    filter_offsets,
    filter_weights,
):
    inverse = panel_inverse[0, 0]
    couple = coupling[0, 0]
    rights = loads[0, 0]
    solved = interface_chain(inverse, couple, rights)

    copies = jnp.broadcast_to(solved[None], (lax.axis_size("dev"),) + solved.shape)
    panels = lax.all_to_all(copies, "dev", split_axis=0, concat_axis=0, tiled=True)
    slabs, order, panel_order = panels.shape
    table = jnp.transpose(panels, (0, 2, 1)).reshape(slabs * panel_order, order)
    slab_place = element_substructure[0, 0]
    lookup = slab_place[None, :] * panel_order + element_rows[0, 0]
    dofs, elements = lookup.shape
    pack = 128 // order
    motion = gathered_rows(table, lookup.reshape(-1)).reshape(dofs, elements // pack, 128)
    forces = jnp.einsum("ij,jab->iab", stiffness, motion, precision=exact_mode)
    energy = jnp.sum(jnp.sum(motion * forces, axis=0).reshape(elements // pack, pack, order), axis=2)
    energy = energy.reshape(elements)
    density = element_density[0, 0]
    sensitivity = -penalty * density * density * energy * energy_scale
    outgoing = picked(sensitivity, send_elements[0, 0])
    received = lax.all_to_all(outgoing, "dev", split_axis=0, concat_axis=0, tiled=True)
    owned = design_density[0, 0]
    row_count = owned.shape[0]
    collected = scattered(received, receive_cells[0, 0], row_count)
    weighted = owned * collected
    padded = padded_2(weighted, (("dev", 0),), RADIUS)
    total_rows = lax.axis_size("dev") * row_count
    padded_rows = padded.shape[0]
    reach = (
        lax.broadcasted_iota(jnp.int32, (1, row_count, padded_rows), 2)
        - lax.broadcasted_iota(jnp.int32, (1, row_count, padded_rows), 1)
        - RADIUS
    )
    band = jnp.sum(
        jnp.where(reach == filter_offsets[:, None, None], filter_weights[:, None, None], 0.0), axis=0
    )
    padded_global = lax.axis_index("dev") * row_count - RADIUS + jnp.arange(padded_rows, dtype=jnp.int32)
    valid = ((padded_global >= 0) & (padded_global < total_rows)).astype(jnp.float32)
    weight_sum = jnp.sum(band * valid[None, :], axis=1)
    accum = product(band, padded)
    filtered = accum / (owned * weight_sum[:, None])
    return (solved[None, None], filtered[None, None])


def solution(mesh):
    placed = (
        P("grp", "dev", None, None),
        P("grp", "dev", None, None),
        P("grp", "dev", None, None),
        P(),
        P("grp", "dev", None),
        P("grp", "dev", None, None),
        P("grp", "dev", None),
        P("grp", "dev", None, None),
        P("grp", "dev", None, None),
        P("grp", "dev", None, None),
        P(),
        P(),
    )
    return jax.shard_map(
        on_device,
        mesh=mesh,
        in_specs=placed,
        out_specs=(P("grp", "dev", None, None), P("grp", "dev", None, None)),
        check_vma=False,
    )
```

```python
import jax
import jax.numpy as jnp
from jax import lax
from jax.sharding import PartitionSpec as P
from jax.experimental import pallas as pl
from jax.experimental.pallas import tpu as pltpu

NK = 8
RADIUS = 3


exact_mode = lax.Precision.HIGHEST
penalty = 3.0
energy_scale = 1.0 / 4096.0


def passed_along(value, axis, steps):
    count = lax.axis_size(axis)
    leading, last = (max(0, -steps), min(count, count - steps))
    return lax.ppermute(value, axis, [(source, source + steps) for source in range(leading, last)])


def padded_2(cells, sides, width):
    for axis, dim in sides:
        count = lax.axis_size(axis)
        ends = count - 1
        head = lax.slice_in_dim(cells, 0, width, axis=dim)
        tail = lax.slice_in_dim(cells, cells.shape[dim] - width, cells.shape[dim], axis=dim)
        cells = jnp.concatenate(
            [
                lax.ppermute(tail, axis, [(i, (i + 1) % count) for i in range(ends)]),
                cells,
                lax.ppermute(head, axis, [((i + 1) % count, i) for i in range(ends)]),
            ],
            axis=dim,
        )
    return cells


def product(left, right):
    return jnp.dot(left, right, precision=exact_mode, preferred_element_type=jnp.float32)


def interface_chain(inverse, couple, rights):
    offset = product(rights, inverse)
    step = -product(couple, inverse)
    order = rights.shape[0]
    levels = lax.axis_size("grp")

    def combine(pairs, with_step):
        nonlocal offset, composite
        if with_step:
            packed = lax.ppermute(jnp.concatenate([offset, composite], axis=0), "grp", pairs)
            earlier_offset, earlier_step = packed[:order], packed[order:]
            offset = product(earlier_offset, composite) + offset
            composite = product(earlier_step, composite)
        else:
            earlier_offset = lax.ppermute(offset, "grp", pairs)
            offset = product(earlier_offset, composite) + offset

    composite = step
    combine([(g, g + 1) for g in range(0, levels - 1, 2)], True)
    shift = 2
    while shift < levels:
        pairs = [(g, g + shift) for g in range(1, levels - shift, 2)]
        combine(pairs, 2 * shift < levels)
        shift *= 2
    earlier_offset = lax.ppermute(offset, "grp", [(g, g + 1) for g in range(1, levels - 1, 2)])
    return product(earlier_offset, step) + offset


def picked(values, index):
    lanes = 128
    table = values.reshape(-1, lanes)
    flat = index.reshape(-1)
    high = flat // lanes
    low = flat % lanes
    rows = jnp.zeros((flat.shape[0], lanes), values.dtype)
    for which in range(table.shape[0]):
        rows = rows + jnp.where((high == which)[:, None], table[which][None, :], 0.0)
    lane_ids = lax.broadcasted_iota(jnp.int32, (1, lanes), 1)
    chosen = jnp.sum(jnp.where(lane_ids == low[:, None], rows, 0.0), axis=1)
    return chosen.reshape(index.shape)


def scattered(values, targets, row_count):
    lanes = 128
    flat_values = values.reshape(-1)
    flat_targets = targets.reshape(-1)
    row = jnp.where(flat_targets >= 0, flat_targets // lanes, -1)
    col = flat_targets % lanes
    row_ids = lax.broadcasted_iota(jnp.int32, (1, row_count), 1)
    lane_ids = lax.broadcasted_iota(jnp.int32, (1, lanes), 1)
    rows_hot = (row[:, None] == row_ids).astype(jnp.float32)
    cols_hot = jnp.where(col[:, None] == lane_ids, flat_values[:, None], 0.0)
    return lax.dot_general(
        rows_hot,
        cols_hot,
        (((0,), (0,)), ((), ())),
        precision=exact_mode,
        preferred_element_type=jnp.float32,
    )


def gather_kernel(lookup_ref, table_ref, out_ref):
    chunk = pl.program_id(0)
    rows = out_ref.shape[0]
    pack = out_ref.shape[1] // 16
    group = lax.broadcasted_iota(jnp.int32, (1, out_ref.shape[1]), 1) // 16
    base = chunk * rows * pack

    def body(row, carry):
        packed_row = jnp.zeros((1, out_ref.shape[1]), jnp.float32)
        for part in range(pack):
            where = lookup_ref[base + row * pack + part]
            packed_row = jnp.where(group == part, table_ref[pl.ds(where, 1), :], packed_row)
        out_ref[pl.ds(row, 1), :] = packed_row
        return carry

    lax.fori_loop(0, rows, body, 0, unroll=8)


def gathered_rows(panels, lookup):
    slabs, width, panel_order = panels.shape
    pack = 128 // width
    spread = (
        lax.broadcasted_iota(jnp.int32, (width, 128), 0)
        == lax.broadcasted_iota(jnp.int32, (width, 128), 1) % width
    ).astype(jnp.float32)
    wide = lax.dot_general(
        panels, spread, (((1,), (0,)), ((), ())), precision=exact_mode, preferred_element_type=jnp.float32
    ).reshape(slabs * panel_order, 128)
    total = lookup.shape[0]
    out_rows = total // pack
    chunks = 8
    rows = out_rows // chunks
    return pl.pallas_call(
        gather_kernel,
        out_shape=jax.ShapeDtypeStruct((out_rows, 128), jnp.float32),
        grid_spec=pltpu.PrefetchScalarGridSpec(
            num_scalar_prefetch=1,
            grid=(chunks,),
            in_specs=[pl.BlockSpec(wide.shape, lambda c, idx: (0, 0))],
            out_specs=pl.BlockSpec((rows, 128), lambda c, idx: (c, 0)),
        ),
        cost_estimate=pl.CostEstimate(flops=0, bytes_accessed=wide.size * 4 + out_rows * 512, transcendentals=0),
    )(lookup, wide)


def gathered_panels(solved):
    count = lax.axis_size("dev")
    me = lax.axis_index("dev")
    bits = count.bit_length() - 1
    order = [bits - 1, 1, bits - 2, bits - 3, 0] if bits == 5 else list(range(bits))
    block = solved[None]
    for bit in order:
        partner = [(i, i ^ (1 << bit)) for i in range(count)]
        other = lax.ppermute(block, "dev", partner)
        high = ((me >> bit) & 1) == 1
        block = jnp.where(high, jnp.concatenate([other, block], 0), jnp.concatenate([block, other], 0))
    return block, order


def slab_position(slab, order):
    position = jnp.zeros_like(slab)
    for place, bit in enumerate(order):
        position = position + (((slab >> bit) & 1) << place)
    return position


def on_device(
    panel_inverse,
    coupling,
    loads,
    stiffness,
    element_substructure,
    element_rows,
    element_density,
    send_elements,
    receive_cells,
    design_density,
    filter_offsets,
    filter_weights,
):
    inverse = panel_inverse[0, 0]
    couple = coupling[0, 0]
    rights = loads[0, 0]
    solved = interface_chain(inverse, couple, rights)

    copies = jnp.broadcast_to(solved[None], (lax.axis_size("dev"),) + solved.shape)
    panels = lax.all_to_all(copies, "dev", split_axis=0, concat_axis=0, tiled=True)
    slabs, order, panel_order = panels.shape
    slab_place = element_substructure[0, 0]
    lookup = slab_place[None, :] * panel_order + element_rows[0, 0]
    dofs, elements = lookup.shape
    pack = 128 // order
    motion = gathered_rows(panels, lookup.reshape(-1)).reshape(dofs, elements // pack, 128)
    forces = jnp.einsum("ij,jab->iab", stiffness, motion, precision=exact_mode)
    energy = jnp.sum(jnp.sum(motion * forces, axis=0).reshape(elements // pack, pack, order), axis=2)
    energy = energy.reshape(elements)
    density = element_density[0, 0]
    sensitivity = -penalty * density * density * energy * energy_scale
    outgoing = picked(sensitivity, send_elements[0, 0])
    received = lax.all_to_all(outgoing, "dev", split_axis=0, concat_axis=0, tiled=True)
    owned = design_density[0, 0]
    row_count = owned.shape[0]
    collected = scattered(received, receive_cells[0, 0], row_count)
    weighted = owned * collected
    padded = padded_2(weighted, (("dev", 0),), RADIUS)
    total_rows = lax.axis_size("dev") * row_count
    padded_rows = padded.shape[0]
    reach = (
        lax.broadcasted_iota(jnp.int32, (1, row_count, padded_rows), 2)
        - lax.broadcasted_iota(jnp.int32, (1, row_count, padded_rows), 1)
        - RADIUS
    )
    band = jnp.sum(
        jnp.where(reach == filter_offsets[:, None, None], filter_weights[:, None, None], 0.0), axis=0
    )
    padded_global = lax.axis_index("dev") * row_count - RADIUS + jnp.arange(padded_rows, dtype=jnp.int32)
    valid = ((padded_global >= 0) & (padded_global < total_rows)).astype(jnp.float32)
    weight_sum = jnp.sum(band * valid[None, :], axis=1)
    accum = product(band, padded)
    filtered = accum / (owned * weight_sum[:, None])
    return (solved[None, None], filtered[None, None])


def solution(mesh):
    placed = (
        P("grp", "dev", None, None),
        P("grp", "dev", None, None),
        P("grp", "dev", None, None),
        P(),
        P("grp", "dev", None),
        P("grp", "dev", None, None),
        P("grp", "dev", None),
        P("grp", "dev", None, None),
        P("grp", "dev", None, None),
        P("grp", "dev", None, None),
        P(),
        P(),
    )
    return jax.shard_map(
        on_device,
        mesh=mesh,
        in_specs=placed,
        out_specs=(P("grp", "dev", None, None), P("grp", "dev", None, None)),
        check_vma=False,
    )
```

```python
import jax
import jax.numpy as jnp
from jax import lax
from jax.sharding import PartitionSpec as P
from jax.experimental import pallas as pl
from jax.experimental.pallas import tpu as pltpu

NK = 8
RADIUS = 3


exact_mode = lax.Precision.HIGHEST
penalty = 3.0
energy_scale = 1.0 / 4096.0


def passed_along(value, axis, steps):
    count = lax.axis_size(axis)
    leading, last = (max(0, -steps), min(count, count - steps))
    return lax.ppermute(value, axis, [(source, source + steps) for source in range(leading, last)])


def padded_2(cells, sides, width):
    for axis, dim in sides:
        count = lax.axis_size(axis)
        ends = count - 1
        head = lax.slice_in_dim(cells, 0, width, axis=dim)
        tail = lax.slice_in_dim(cells, cells.shape[dim] - width, cells.shape[dim], axis=dim)
        cells = jnp.concatenate(
            [
                lax.ppermute(tail, axis, [(i, (i + 1) % count) for i in range(ends)]),
                cells,
                lax.ppermute(head, axis, [((i + 1) % count, i) for i in range(ends)]),
            ],
            axis=dim,
        )
    return cells


def product(left, right):
    return jnp.dot(left, right, precision=exact_mode, preferred_element_type=jnp.float32)


def interface_chain(inverse, couple, rights):
    offset = product(rights, inverse)
    step = -product(couple, inverse)
    order = rights.shape[0]
    levels = lax.axis_size("grp")

    def combine(pairs, with_step):
        nonlocal offset, composite
        if with_step:
            packed = jnp.concatenate([offset, composite], axis=0)
            half = packed.shape[0] // 2
            packed = jnp.concatenate(
                [lax.ppermute(packed[:half], "grp", pairs), lax.ppermute(packed[half:], "grp", pairs)], axis=0
            )
            earlier_offset, earlier_step = packed[:order], packed[order:]
            offset = product(earlier_offset, composite) + offset
            composite = product(earlier_step, composite)
        else:
            earlier_offset = lax.ppermute(offset, "grp", pairs)
            offset = product(earlier_offset, composite) + offset

    composite = step
    combine([(g, g + 1) for g in range(0, levels - 1, 2)], True)
    shift = 2
    while shift < levels:
        pairs = [(g, g + shift) for g in range(1, levels - shift, 2)]
        combine(pairs, 2 * shift < levels)
        shift *= 2
    earlier_offset = lax.ppermute(offset, "grp", [(g, g + 1) for g in range(1, levels - 1, 2)])
    return product(earlier_offset, step) + offset


def picked(values, index):
    lanes = 128
    table = values.reshape(-1, lanes)
    flat = index.reshape(-1)
    high = flat // lanes
    low = flat % lanes
    rows = jnp.zeros((flat.shape[0], lanes), values.dtype)
    for which in range(table.shape[0]):
        rows = rows + jnp.where((high == which)[:, None], table[which][None, :], 0.0)
    lane_ids = lax.broadcasted_iota(jnp.int32, (1, lanes), 1)
    chosen = jnp.sum(jnp.where(lane_ids == low[:, None], rows, 0.0), axis=1)
    return chosen.reshape(index.shape)


def scattered(values, targets, row_count):
    lanes = 128
    flat_values = values.reshape(-1)
    flat_targets = targets.reshape(-1)
    row = jnp.where(flat_targets >= 0, flat_targets // lanes, -1)
    col = flat_targets % lanes
    row_ids = lax.broadcasted_iota(jnp.int32, (1, row_count), 1)
    lane_ids = lax.broadcasted_iota(jnp.int32, (1, lanes), 1)
    rows_hot = (row[:, None] == row_ids).astype(jnp.float32)
    cols_hot = jnp.where(col[:, None] == lane_ids, flat_values[:, None], 0.0)
    return lax.dot_general(
        rows_hot,
        cols_hot,
        (((0,), (0,)), ((), ())),
        precision=exact_mode,
        preferred_element_type=jnp.float32,
    )


def gather_kernel(lookup_ref, table_ref, out_ref):
    chunk = pl.program_id(0)
    rows = out_ref.shape[0]
    pack = out_ref.shape[1] // 16
    group = lax.broadcasted_iota(jnp.int32, (1, out_ref.shape[1]), 1) // 16
    base = chunk * rows * pack

    def body(row, carry):
        packed_row = jnp.zeros((1, out_ref.shape[1]), jnp.float32)
        for part in range(pack):
            where = lookup_ref[base + row * pack + part]
            packed_row = jnp.where(group == part, table_ref[pl.ds(where, 1), :], packed_row)
        out_ref[pl.ds(row, 1), :] = packed_row
        return carry

    lax.fori_loop(0, rows, body, 0, unroll=8)


def gathered_rows(panels, lookup):
    slabs, width, panel_order = panels.shape
    pack = 128 // width
    spread = (
        lax.broadcasted_iota(jnp.int32, (width, 128), 0)
        == lax.broadcasted_iota(jnp.int32, (width, 128), 1) % width
    ).astype(jnp.float32)
    wide = lax.dot_general(
        panels, spread, (((1,), (0,)), ((), ())), precision=exact_mode, preferred_element_type=jnp.float32
    ).reshape(slabs * panel_order, 128)
    total = lookup.shape[0]
    out_rows = total // pack
    chunks = 8
    rows = out_rows // chunks
    return pl.pallas_call(
        gather_kernel,
        out_shape=jax.ShapeDtypeStruct((out_rows, 128), jnp.float32),
        grid_spec=pltpu.PrefetchScalarGridSpec(
            num_scalar_prefetch=1,
            grid=(chunks,),
            in_specs=[pl.BlockSpec(wide.shape, lambda c, idx: (0, 0))],
            out_specs=pl.BlockSpec((rows, 128), lambda c, idx: (c, 0)),
        ),
        cost_estimate=pl.CostEstimate(flops=0, bytes_accessed=wide.size * 4 + out_rows * 512, transcendentals=0),
    )(lookup, wide)


def gathered_panels(solved):
    count = lax.axis_size("dev")
    me = lax.axis_index("dev")
    bits = count.bit_length() - 1
    order = [bits - 1, 1, bits - 2, bits - 3, 0] if bits == 5 else list(range(bits))
    block = solved[None]
    for bit in order:
        partner = [(i, i ^ (1 << bit)) for i in range(count)]
        other = lax.ppermute(block, "dev", partner)
        high = ((me >> bit) & 1) == 1
        block = jnp.where(high, jnp.concatenate([other, block], 0), jnp.concatenate([block, other], 0))
    return block, order


def slab_position(slab, order):
    position = jnp.zeros_like(slab)
    for place, bit in enumerate(order):
        position = position + (((slab >> bit) & 1) << place)
    return position


def on_device(
    panel_inverse,
    coupling,
    loads,
    stiffness,
    element_substructure,
    element_rows,
    element_density,
    send_elements,
    receive_cells,
    design_density,
    filter_offsets,
    filter_weights,
):
    inverse = panel_inverse[0, 0]
    couple = coupling[0, 0]
    rights = loads[0, 0]
    solved = interface_chain(inverse, couple, rights)

    copies = jnp.broadcast_to(solved[None], (lax.axis_size("dev"),) + solved.shape)
    panels = lax.all_to_all(copies, "dev", split_axis=0, concat_axis=0, tiled=True)
    slabs, order, panel_order = panels.shape
    slab_place = element_substructure[0, 0]
    lookup = slab_place[None, :] * panel_order + element_rows[0, 0]
    dofs, elements = lookup.shape
    pack = 128 // order
    motion = gathered_rows(panels, lookup.reshape(-1)).reshape(dofs, elements // pack, 128)
    forces = jnp.einsum("ij,jab->iab", stiffness, motion, precision=exact_mode)
    energy = jnp.sum(jnp.sum(motion * forces, axis=0).reshape(elements // pack, pack, order), axis=2)
    energy = energy.reshape(elements)
    density = element_density[0, 0]
    sensitivity = -penalty * density * density * energy * energy_scale
    outgoing = picked(sensitivity, send_elements[0, 0])
    received = lax.all_to_all(outgoing, "dev", split_axis=0, concat_axis=0, tiled=True)
    owned = design_density[0, 0]
    row_count = owned.shape[0]
    collected = scattered(received, receive_cells[0, 0], row_count)
    weighted = owned * collected
    padded = padded_2(weighted, (("dev", 0),), RADIUS)
    total_rows = lax.axis_size("dev") * row_count
    padded_rows = padded.shape[0]
    reach = (
        lax.broadcasted_iota(jnp.int32, (1, row_count, padded_rows), 2)
        - lax.broadcasted_iota(jnp.int32, (1, row_count, padded_rows), 1)
        - RADIUS
    )
    band = jnp.sum(
        jnp.where(reach == filter_offsets[:, None, None], filter_weights[:, None, None], 0.0), axis=0
    )
    padded_global = lax.axis_index("dev") * row_count - RADIUS + jnp.arange(padded_rows, dtype=jnp.int32)
    valid = ((padded_global >= 0) & (padded_global < total_rows)).astype(jnp.float32)
    weight_sum = jnp.sum(band * valid[None, :], axis=1)
    accum = product(band, padded)
    filtered = accum / (owned * weight_sum[:, None])
    return (solved[None, None], filtered[None, None])


def solution(mesh):
    placed = (
        P("grp", "dev", None, None),
        P("grp", "dev", None, None),
        P("grp", "dev", None, None),
        P(),
        P("grp", "dev", None),
        P("grp", "dev", None, None),
        P("grp", "dev", None),
        P("grp", "dev", None, None),
        P("grp", "dev", None, None),
        P("grp", "dev", None, None),
        P(),
        P(),
    )
    return jax.shard_map(
        on_device,
        mesh=mesh,
        in_specs=placed,
        out_specs=(P("grp", "dev", None, None), P("grp", "dev", None, None)),
        check_vma=False,
    )
```

```python
import jax
import jax.numpy as jnp
from jax import lax
from jax.sharding import PartitionSpec as P
from jax.experimental import pallas as pl
from jax.experimental.pallas import tpu as pltpu

NK = 8
RADIUS = 3


exact_mode = lax.Precision.HIGHEST
penalty = 3.0
energy_scale = 1.0 / 4096.0


def passed_along(value, axis, steps):
    count = lax.axis_size(axis)
    leading, last = (max(0, -steps), min(count, count - steps))
    return lax.ppermute(value, axis, [(source, source + steps) for source in range(leading, last)])


def padded_2(cells, sides, width):
    for axis, dim in sides:
        count = lax.axis_size(axis)
        ends = count - 1
        head = lax.slice_in_dim(cells, 0, width, axis=dim)
        tail = lax.slice_in_dim(cells, cells.shape[dim] - width, cells.shape[dim], axis=dim)
        cells = jnp.concatenate(
            [
                lax.ppermute(tail, axis, [(i, (i + 1) % count) for i in range(ends)]),
                cells,
                lax.ppermute(head, axis, [((i + 1) % count, i) for i in range(ends)]),
            ],
            axis=dim,
        )
    return cells


def product(left, right):
    return jnp.dot(left, right, precision=exact_mode, preferred_element_type=jnp.float32)


def interface_chain(inverse, couple, rights):
    offset = product(rights, inverse)
    step = -product(couple, inverse)
    order = rights.shape[0]
    levels = lax.axis_size("grp")

    def combine(pairs, with_step):
        nonlocal offset, composite
        if with_step:
            packed = jnp.concatenate([offset, composite], axis=0)
            half = packed.shape[0] // 2
            packed = jnp.concatenate(
                [lax.ppermute(packed[:half], "grp", pairs), lax.ppermute(packed[half:], "grp", pairs)], axis=0
            )
            earlier_offset, earlier_step = packed[:order], packed[order:]
            offset = product(earlier_offset, composite) + offset
            composite = product(earlier_step, composite)
        else:
            earlier_offset = lax.ppermute(offset, "grp", pairs)
            offset = product(earlier_offset, composite) + offset

    composite = step
    combine([(g, g + 1) for g in range(0, levels - 1, 2)], True)
    shift = 2
    while shift < levels:
        pairs = [(g, g + shift) for g in range(1, levels - shift, 2)]
        combine(pairs, 2 * shift < levels)
        shift *= 2
    earlier_offset = lax.ppermute(offset, "grp", [(g, g + 1) for g in range(1, levels - 1, 2)])
    return product(earlier_offset, step) + offset


def picked(values, index):
    lanes = 128
    table = values.reshape(-1, lanes)
    flat = index.reshape(-1)
    high = flat // lanes
    low = flat % lanes
    rows = jnp.zeros((flat.shape[0], lanes), values.dtype)
    for which in range(table.shape[0]):
        rows = rows + jnp.where((high == which)[:, None], table[which][None, :], 0.0)
    lane_ids = lax.broadcasted_iota(jnp.int32, (1, lanes), 1)
    chosen = jnp.sum(jnp.where(lane_ids == low[:, None], rows, 0.0), axis=1)
    return chosen.reshape(index.shape)


def scattered(values, rows, cols, row_count):
    lanes = 128
    row_ids = lax.broadcasted_iota(jnp.int32, (1, row_count), 1)
    lane_ids = lax.broadcasted_iota(jnp.int32, (1, lanes), 1)
    rows_hot = (rows[:, None] == row_ids).astype(jnp.float32)
    cols_hot = jnp.where(cols[:, None] == lane_ids, values[:, None], 0.0)
    return lax.dot_general(
        rows_hot,
        cols_hot,
        (((0,), (0,)), ((), ())),
        precision=exact_mode,
        preferred_element_type=jnp.float32,
    )


def padded_targets(cells, first, last, shift):
    row = cells // 128
    keep = (cells >= 0) & (row >= first) & (row < last)
    return jnp.where(keep, row + shift, -1).reshape(-1), (cells % 128).reshape(-1)


def gather_kernel(lookup_ref, table_ref, out_ref):
    chunk = pl.program_id(0)
    rows = out_ref.shape[0]
    pack = out_ref.shape[1] // 16
    group = lax.broadcasted_iota(jnp.int32, (1, out_ref.shape[1]), 1) // 16
    base = chunk * rows * pack

    def body(row, carry):
        packed_row = jnp.zeros((1, out_ref.shape[1]), jnp.float32)
        for part in range(pack):
            where = lookup_ref[base + row * pack + part]
            packed_row = jnp.where(group == part, table_ref[pl.ds(where, 1), :], packed_row)
        out_ref[pl.ds(row, 1), :] = packed_row
        return carry

    lax.fori_loop(0, rows, body, 0, unroll=8)


def gathered_rows(panels, lookup):
    slabs, width, panel_order = panels.shape
    pack = 128 // width
    spread = (
        lax.broadcasted_iota(jnp.int32, (width, 128), 0)
        == lax.broadcasted_iota(jnp.int32, (width, 128), 1) % width
    ).astype(jnp.float32)
    wide = lax.dot_general(
        panels, spread, (((1,), (0,)), ((), ())), precision=exact_mode, preferred_element_type=jnp.float32
    ).reshape(slabs * panel_order, 128)
    total = lookup.shape[0]
    out_rows = total // pack
    chunks = 8
    rows = out_rows // chunks
    return pl.pallas_call(
        gather_kernel,
        out_shape=jax.ShapeDtypeStruct((out_rows, 128), jnp.float32),
        grid_spec=pltpu.PrefetchScalarGridSpec(
            num_scalar_prefetch=1,
            grid=(chunks,),
            in_specs=[pl.BlockSpec(wide.shape, lambda c, idx: (0, 0))],
            out_specs=pl.BlockSpec((rows, 128), lambda c, idx: (c, 0)),
        ),
        cost_estimate=pl.CostEstimate(flops=0, bytes_accessed=wide.size * 4 + out_rows * 512, transcendentals=0),
    )(lookup, wide)


def gathered_panels(solved):
    count = lax.axis_size("dev")
    me = lax.axis_index("dev")
    bits = count.bit_length() - 1
    order = [bits - 1, 1, bits - 2, bits - 3, 0] if bits == 5 else list(range(bits))
    block = solved[None]
    for bit in order:
        partner = [(i, i ^ (1 << bit)) for i in range(count)]
        other = lax.ppermute(block, "dev", partner)
        high = ((me >> bit) & 1) == 1
        block = jnp.where(high, jnp.concatenate([other, block], 0), jnp.concatenate([block, other], 0))
    return block, order


def slab_position(slab, order):
    position = jnp.zeros_like(slab)
    for place, bit in enumerate(order):
        position = position + (((slab >> bit) & 1) << place)
    return position


def on_device(
    panel_inverse,
    coupling,
    loads,
    stiffness,
    element_substructure,
    element_rows,
    element_density,
    send_elements,
    receive_cells,
    design_density,
    filter_offsets,
    filter_weights,
):
    inverse = panel_inverse[0, 0]
    couple = coupling[0, 0]
    rights = loads[0, 0]
    solved = interface_chain(inverse, couple, rights)

    copies = jnp.broadcast_to(solved[None], (lax.axis_size("dev"),) + solved.shape)
    panels = lax.all_to_all(copies, "dev", split_axis=0, concat_axis=0, tiled=True)
    slabs, order, panel_order = panels.shape
    slab_place = element_substructure[0, 0]
    lookup = slab_place[None, :] * panel_order + element_rows[0, 0]
    dofs, elements = lookup.shape
    pack = 128 // order
    motion = gathered_rows(panels, lookup.reshape(-1)).reshape(dofs, elements // pack, 128)
    forces = jnp.einsum("ij,jab->iab", stiffness, motion, precision=exact_mode)
    energy = jnp.sum(jnp.sum(motion * forces, axis=0).reshape(elements // pack, pack, order), axis=2)
    energy = energy.reshape(elements)
    density = element_density[0, 0]
    sensitivity = -penalty * density * density * energy * energy_scale
    owned = design_density[0, 0]
    row_count = owned.shape[0]
    count = lax.axis_size("dev")
    cells = receive_cells[0, 0]
    sources, slots = cells.shape
    shared = cells.astype(jnp.float32).reshape(-1, 128)
    from_left = lax.ppermute(
        jnp.concatenate([shared, owned[row_count - RADIUS :]], axis=0), "dev", [(i, i + 1) for i in range(count - 1)]
    )
    from_right = lax.ppermute(
        jnp.concatenate([shared, owned[:RADIUS]], axis=0), "dev", [(i + 1, i) for i in range(count - 1)]
    )
    list_rows = shared.shape[0]
    cells_left = from_left[:list_rows].astype(jnp.int32).reshape(sources, slots)
    cells_right = from_right[:list_rows].astype(jnp.int32).reshape(sources, slots)
    density_rows = jnp.concatenate([from_left[list_rows:], owned, from_right[list_rows:]], axis=0)

    outgoing = picked(sensitivity, send_elements[0, 0])
    edge = jnp.zeros((1, slots), jnp.float32)
    spread_out = jnp.concatenate([edge, outgoing, edge], axis=0)
    owners = outgoing.shape[0]
    triple = jnp.stack([spread_out[0:owners], spread_out[1 : owners + 1], spread_out[2 : owners + 2]], axis=1)
    received = lax.all_to_all(triple, "dev", split_axis=0, concat_axis=0, tiled=True)
    left_rows, left_cols = padded_targets(cells_left, row_count - RADIUS, row_count, RADIUS - row_count)
    own_rows, own_cols = padded_targets(cells, 0, row_count, RADIUS)
    right_rows, right_cols = padded_targets(cells_right, 0, RADIUS, row_count + RADIUS)
    collected = scattered(
        jnp.concatenate([received[:, 0].reshape(-1), received[:, 1].reshape(-1), received[:, 2].reshape(-1)]),
        jnp.concatenate([left_rows, own_rows, right_rows]),
        jnp.concatenate([left_cols, own_cols, right_cols]),
        row_count + 2 * RADIUS,
    )
    padded = density_rows * collected
    total_rows = lax.axis_size("dev") * row_count
    padded_rows = padded.shape[0]
    reach = (
        lax.broadcasted_iota(jnp.int32, (1, row_count, padded_rows), 2)
        - lax.broadcasted_iota(jnp.int32, (1, row_count, padded_rows), 1)
        - RADIUS
    )
    band = jnp.sum(
        jnp.where(reach == filter_offsets[:, None, None], filter_weights[:, None, None], 0.0), axis=0
    )
    padded_global = lax.axis_index("dev") * row_count - RADIUS + jnp.arange(padded_rows, dtype=jnp.int32)
    valid = ((padded_global >= 0) & (padded_global < total_rows)).astype(jnp.float32)
    weight_sum = jnp.sum(band * valid[None, :], axis=1)
    accum = product(band, padded)
    filtered = accum / (owned * weight_sum[:, None])
    return (solved[None, None], filtered[None, None])


def solution(mesh):
    placed = (
        P("grp", "dev", None, None),
        P("grp", "dev", None, None),
        P("grp", "dev", None, None),
        P(),
        P("grp", "dev", None),
        P("grp", "dev", None, None),
        P("grp", "dev", None),
        P("grp", "dev", None, None),
        P("grp", "dev", None, None),
        P("grp", "dev", None, None),
        P(),
        P(),
    )
    return jax.shard_map(
        on_device,
        mesh=mesh,
        in_specs=placed,
        out_specs=(P("grp", "dev", None, None), P("grp", "dev", None, None)),
        check_vma=False,
    )
```

```python
import jax
import jax.numpy as jnp
from jax import lax
from jax.sharding import PartitionSpec as P
from jax.experimental import pallas as pl
from jax.experimental.pallas import tpu as pltpu

NK = 8
RADIUS = 3


exact_mode = lax.Precision.HIGHEST
penalty = 3.0
energy_scale = 1.0 / 4096.0


def passed_along(value, axis, steps):
    count = lax.axis_size(axis)
    leading, last = (max(0, -steps), min(count, count - steps))
    return lax.ppermute(value, axis, [(source, source + steps) for source in range(leading, last)])


def padded_2(cells, sides, width):
    for axis, dim in sides:
        count = lax.axis_size(axis)
        ends = count - 1
        head = lax.slice_in_dim(cells, 0, width, axis=dim)
        tail = lax.slice_in_dim(cells, cells.shape[dim] - width, cells.shape[dim], axis=dim)
        cells = jnp.concatenate(
            [
                lax.ppermute(tail, axis, [(i, (i + 1) % count) for i in range(ends)]),
                cells,
                lax.ppermute(head, axis, [((i + 1) % count, i) for i in range(ends)]),
            ],
            axis=dim,
        )
    return cells


def product(left, right):
    return jnp.dot(left, right, precision=exact_mode, preferred_element_type=jnp.float32)


def interface_chain(inverse, couple, rights):
    offset = product(rights, inverse)
    step = -product(couple, inverse)
    order = rights.shape[0]
    levels = lax.axis_size("grp")

    def combine(pairs, with_step):
        nonlocal offset, composite
        if with_step:
            packed = jnp.concatenate([offset, composite], axis=0)
            half = packed.shape[0] // 2
            packed = jnp.concatenate(
                [lax.ppermute(packed[:half], "grp", pairs), lax.ppermute(packed[half:], "grp", pairs)], axis=0
            )
            earlier_offset, earlier_step = packed[:order], packed[order:]
            offset = product(earlier_offset, composite) + offset
            composite = product(earlier_step, composite)
        else:
            earlier_offset = lax.ppermute(offset, "grp", pairs)
            offset = product(earlier_offset, composite) + offset

    composite = step
    combine([(g, g + 1) for g in range(0, levels - 1, 2)], True)
    shift = 2
    while shift < levels:
        pairs = [(g, g + shift) for g in range(1, levels - shift, 2)]
        combine(pairs, 2 * shift < levels)
        shift *= 2
    earlier_offset = lax.ppermute(offset, "grp", [(g, g + 1) for g in range(1, levels - 1, 2)])
    return product(earlier_offset, step) + offset


def picked(values, index):
    lanes = 128
    table = values.reshape(-1, lanes)
    flat = index.reshape(-1)
    high = flat // lanes
    low = flat % lanes
    rows = jnp.zeros((flat.shape[0], lanes), values.dtype)
    for which in range(table.shape[0]):
        rows = rows + jnp.where((high == which)[:, None], table[which][None, :], 0.0)
    lane_ids = lax.broadcasted_iota(jnp.int32, (1, lanes), 1)
    chosen = jnp.sum(jnp.where(lane_ids == low[:, None], rows, 0.0), axis=1)
    return chosen.reshape(index.shape)


def scattered(values, rows, cols, row_count):
    lanes = 128
    row_ids = lax.broadcasted_iota(jnp.int32, (1, row_count), 1)
    lane_ids = lax.broadcasted_iota(jnp.int32, (1, lanes), 1)
    rows_hot = (rows[:, None] == row_ids).astype(jnp.float32)
    cols_hot = jnp.where(cols[:, None] == lane_ids, values[:, None], 0.0)
    return lax.dot_general(
        rows_hot,
        cols_hot,
        (((0,), (0,)), ((), ())),
        precision=exact_mode,
        preferred_element_type=jnp.float32,
    )


def padded_targets(cells, first, last, shift):
    row = cells // 128
    keep = (cells >= 0) & (row >= first) & (row < last)
    return jnp.where(keep, row + shift, -1).reshape(-1), (cells % 128).reshape(-1)


def gather_kernel(lookup_ref, table_ref, out_ref):
    chunk = pl.program_id(0)
    rows = out_ref.shape[0]
    pack = out_ref.shape[1] // 16
    group = lax.broadcasted_iota(jnp.int32, (1, out_ref.shape[1]), 1) // 16
    base = chunk * rows * pack

    def body(row, carry):
        packed_row = jnp.zeros((1, out_ref.shape[1]), jnp.float32)
        for part in range(pack):
            where = lookup_ref[base + row * pack + part]
            packed_row = jnp.where(group == part, table_ref[pl.ds(where, 1), :], packed_row)
        out_ref[pl.ds(row, 1), :] = packed_row
        return carry

    lax.fori_loop(0, rows, body, 0, unroll=8)


def gathered_rows(panels, lookup):
    slabs, width, panel_order = panels.shape
    pack = 128 // width
    spread = (
        lax.broadcasted_iota(jnp.int32, (width, 128), 0)
        == lax.broadcasted_iota(jnp.int32, (width, 128), 1) % width
    ).astype(jnp.float32)
    wide = lax.dot_general(
        panels, spread, (((1,), (0,)), ((), ())), precision=exact_mode, preferred_element_type=jnp.float32
    ).reshape(slabs * panel_order, 128)
    total = lookup.shape[0]
    out_rows = total // pack
    chunks = 8
    rows = out_rows // chunks
    return pl.pallas_call(
        gather_kernel,
        out_shape=jax.ShapeDtypeStruct((out_rows, 128), jnp.float32),
        grid_spec=pltpu.PrefetchScalarGridSpec(
            num_scalar_prefetch=1,
            grid=(chunks,),
            in_specs=[pl.BlockSpec(wide.shape, lambda c, idx: (0, 0))],
            out_specs=pl.BlockSpec((rows, 128), lambda c, idx: (c, 0)),
        ),
        cost_estimate=pl.CostEstimate(flops=0, bytes_accessed=wide.size * 4 + out_rows * 512, transcendentals=0),
    )(lookup, wide)


def gathered_panels(solved):
    count = lax.axis_size("dev")
    me = lax.axis_index("dev")
    bits = count.bit_length() - 1
    order = [bits - 1, 1, bits - 2, bits - 3, 0] if bits == 5 else list(range(bits))
    block = solved[None]
    for bit in order:
        partner = [(i, i ^ (1 << bit)) for i in range(count)]
        other = lax.ppermute(block, "dev", partner)
        high = ((me >> bit) & 1) == 1
        block = jnp.where(high, jnp.concatenate([other, block], 0), jnp.concatenate([block, other], 0))
    return block, order


def slab_position(slab, order):
    position = jnp.zeros_like(slab)
    for place, bit in enumerate(order):
        position = position + (((slab >> bit) & 1) << place)
    return position


def on_device(
    panel_inverse,
    coupling,
    loads,
    stiffness,
    element_substructure,
    element_rows,
    element_density,
    send_elements,
    receive_cells,
    design_density,
    filter_offsets,
    filter_weights,
):
    inverse = panel_inverse[0, 0]
    couple = coupling[0, 0]
    rights = loads[0, 0]
    solved = interface_chain(inverse, couple, rights)

    copies = jnp.broadcast_to(solved[None], (lax.axis_size("dev"),) + solved.shape)
    panels = lax.all_to_all(copies, "dev", split_axis=0, concat_axis=0, tiled=True)
    slabs, order, panel_order = panels.shape
    slab_place = element_substructure[0, 0]
    lookup = slab_place[None, :] * panel_order + element_rows[0, 0]
    dofs, elements = lookup.shape
    pack = 128 // order
    motion = gathered_rows(panels, lookup.reshape(-1)).reshape(dofs, elements // pack, 128)
    forces = jnp.einsum("ij,jab->iab", stiffness, motion, precision=exact_mode)
    energy = jnp.sum(jnp.sum(motion * forces, axis=0).reshape(elements // pack, pack, order), axis=2)
    energy = energy.reshape(elements)
    density = element_density[0, 0]
    sensitivity = -penalty * density * density * energy * energy_scale
    owned = design_density[0, 0]
    row_count = owned.shape[0]
    count = lax.axis_size("dev")
    cells = receive_cells[0, 0]
    sources, slots = cells.shape
    shared = cells.astype(jnp.float32).reshape(-1, 128)
    to_right = jnp.concatenate([shared, owned[row_count - RADIUS :]], axis=0)
    to_left = jnp.concatenate([shared, owned[:RADIUS]], axis=0)
    to_right, to_left, _ = lax.optimization_barrier((to_right, to_left, solved))
    from_left = lax.ppermute(to_right, "dev", [(i, i + 1) for i in range(count - 1)])
    from_right = lax.ppermute(to_left, "dev", [(i + 1, i) for i in range(count - 1)])
    list_rows = shared.shape[0]
    cells_left = from_left[:list_rows].astype(jnp.int32).reshape(sources, slots)
    cells_right = from_right[:list_rows].astype(jnp.int32).reshape(sources, slots)
    density_rows = jnp.concatenate([from_left[list_rows:], owned, from_right[list_rows:]], axis=0)

    outgoing = picked(sensitivity, send_elements[0, 0])
    edge = jnp.zeros((1, slots), jnp.float32)
    spread_out = jnp.concatenate([edge, outgoing, edge], axis=0)
    owners = outgoing.shape[0]
    triple = jnp.stack([spread_out[0:owners], spread_out[1 : owners + 1], spread_out[2 : owners + 2]], axis=1)
    received = lax.all_to_all(triple, "dev", split_axis=0, concat_axis=0, tiled=True)
    left_rows, left_cols = padded_targets(cells_left, row_count - RADIUS, row_count, RADIUS - row_count)
    own_rows, own_cols = padded_targets(cells, 0, row_count, RADIUS)
    right_rows, right_cols = padded_targets(cells_right, 0, RADIUS, row_count + RADIUS)
    collected = scattered(
        jnp.concatenate([received[:, 0].reshape(-1), received[:, 1].reshape(-1), received[:, 2].reshape(-1)]),
        jnp.concatenate([left_rows, own_rows, right_rows]),
        jnp.concatenate([left_cols, own_cols, right_cols]),
        row_count + 2 * RADIUS,
    )
    padded = density_rows * collected
    total_rows = lax.axis_size("dev") * row_count
    padded_rows = padded.shape[0]
    reach = (
        lax.broadcasted_iota(jnp.int32, (1, row_count, padded_rows), 2)
        - lax.broadcasted_iota(jnp.int32, (1, row_count, padded_rows), 1)
        - RADIUS
    )
    band = jnp.sum(
        jnp.where(reach == filter_offsets[:, None, None], filter_weights[:, None, None], 0.0), axis=0
    )
    padded_global = lax.axis_index("dev") * row_count - RADIUS + jnp.arange(padded_rows, dtype=jnp.int32)
    valid = ((padded_global >= 0) & (padded_global < total_rows)).astype(jnp.float32)
    weight_sum = jnp.sum(band * valid[None, :], axis=1)
    accum = product(band, padded)
    filtered = accum / (owned * weight_sum[:, None])
    return (solved[None, None], filtered[None, None])


def solution(mesh):
    placed = (
        P("grp", "dev", None, None),
        P("grp", "dev", None, None),
        P("grp", "dev", None, None),
        P(),
        P("grp", "dev", None),
        P("grp", "dev", None, None),
        P("grp", "dev", None),
        P("grp", "dev", None, None),
        P("grp", "dev", None, None),
        P("grp", "dev", None, None),
        P(),
        P(),
    )
    return jax.shard_map(
        on_device,
        mesh=mesh,
        in_specs=placed,
        out_specs=(P("grp", "dev", None, None), P("grp", "dev", None, None)),
        check_vma=False,
    )
```

```python
import jax
import jax.numpy as jnp
from jax import lax
from jax.sharding import PartitionSpec as P
from jax.experimental import pallas as pl
from jax.experimental.pallas import tpu as pltpu

NK = 8
RADIUS = 3


exact_mode = lax.Precision.HIGHEST
penalty = 3.0
energy_scale = 1.0 / 4096.0


def passed_along(value, axis, steps):
    count = lax.axis_size(axis)
    leading, last = (max(0, -steps), min(count, count - steps))
    return lax.ppermute(value, axis, [(source, source + steps) for source in range(leading, last)])


def padded_2(cells, sides, width):
    for axis, dim in sides:
        count = lax.axis_size(axis)
        ends = count - 1
        head = lax.slice_in_dim(cells, 0, width, axis=dim)
        tail = lax.slice_in_dim(cells, cells.shape[dim] - width, cells.shape[dim], axis=dim)
        cells = jnp.concatenate(
            [
                lax.ppermute(tail, axis, [(i, (i + 1) % count) for i in range(ends)]),
                cells,
                lax.ppermute(head, axis, [((i + 1) % count, i) for i in range(ends)]),
            ],
            axis=dim,
        )
    return cells


def product(left, right):
    return jnp.dot(left, right, precision=exact_mode, preferred_element_type=jnp.float32)


def interface_chain(inverse, couple, rights, held):
    offset = product(rights, inverse)
    step = -product(couple, inverse)
    order = rights.shape[0]
    levels = lax.axis_size("grp")

    def combine(pairs, with_step):
        nonlocal offset, composite
        if with_step:
            packed = jnp.concatenate([offset, composite], axis=0)
            half = packed.shape[0] // 2
            packed = jnp.concatenate(
                [lax.ppermute(packed[:half], "grp", pairs), lax.ppermute(packed[half:], "grp", pairs)], axis=0
            )
            earlier_offset, earlier_step = packed[:order], packed[order:]
            offset = product(earlier_offset, composite) + offset
            composite = product(earlier_step, composite)
        else:
            earlier_offset = lax.ppermute(offset, "grp", pairs)
            offset = product(earlier_offset, composite) + offset

    composite = step
    combine([(g, g + 1) for g in range(0, levels - 1, 2)], True)
    shift = 2
    while shift < levels:
        pairs = [(g, g + shift) for g in range(1, levels - shift, 2)]
        combine(pairs, 2 * shift < levels)
        if shift == 2:
            held, offset = lax.optimization_barrier((held, offset))
        shift *= 2
    earlier_offset = lax.ppermute(offset, "grp", [(g, g + 1) for g in range(1, levels - 1, 2)])
    return product(earlier_offset, step) + offset, held


def picked(values, index):
    lanes = 128
    table = values.reshape(-1, lanes)
    flat = index.reshape(-1)
    high = flat // lanes
    low = flat % lanes
    rows = jnp.zeros((flat.shape[0], lanes), values.dtype)
    for which in range(table.shape[0]):
        rows = rows + jnp.where((high == which)[:, None], table[which][None, :], 0.0)
    lane_ids = lax.broadcasted_iota(jnp.int32, (1, lanes), 1)
    chosen = jnp.sum(jnp.where(lane_ids == low[:, None], rows, 0.0), axis=1)
    return chosen.reshape(index.shape)


def scattered(values, rows, cols, row_count):
    lanes = 128
    row_ids = lax.broadcasted_iota(jnp.int32, (1, row_count), 1)
    lane_ids = lax.broadcasted_iota(jnp.int32, (1, lanes), 1)
    rows_hot = (rows[:, None] == row_ids).astype(jnp.float32)
    cols_hot = jnp.where(cols[:, None] == lane_ids, values[:, None], 0.0)
    return lax.dot_general(
        rows_hot,
        cols_hot,
        (((0,), (0,)), ((), ())),
        precision=exact_mode,
        preferred_element_type=jnp.float32,
    )


def padded_targets(cells, first, last, shift):
    row = cells // 128
    keep = (cells >= 0) & (row >= first) & (row < last)
    return jnp.where(keep, row + shift, -1).reshape(-1), (cells % 128).reshape(-1)


def gather_kernel(lookup_ref, table_ref, out_ref):
    chunk = pl.program_id(0)
    rows = out_ref.shape[0]
    pack = out_ref.shape[1] // 16
    group = lax.broadcasted_iota(jnp.int32, (1, out_ref.shape[1]), 1) // 16
    base = chunk * rows * pack

    def body(row, carry):
        packed_row = jnp.zeros((1, out_ref.shape[1]), jnp.float32)
        for part in range(pack):
            where = lookup_ref[base + row * pack + part]
            packed_row = jnp.where(group == part, table_ref[pl.ds(where, 1), :], packed_row)
        out_ref[pl.ds(row, 1), :] = packed_row
        return carry

    lax.fori_loop(0, rows, body, 0, unroll=8)


def gathered_rows(panels, lookup):
    slabs, width, panel_order = panels.shape
    pack = 128 // width
    spread = (
        lax.broadcasted_iota(jnp.int32, (width, 128), 0)
        == lax.broadcasted_iota(jnp.int32, (width, 128), 1) % width
    ).astype(jnp.float32)
    spread = spread.astype(jnp.bfloat16)
    rest = panels
    wide = None
    for _ in range(3):
        rounded = lax.reduce_precision(rest, exponent_bits=8, mantissa_bits=7)
        rest = rest - rounded
        part = rounded.astype(jnp.bfloat16)
        term = lax.dot_general(part, spread, (((1,), (0,)), ((), ())), preferred_element_type=jnp.float32)
        wide = term if wide is None else wide + term
    wide = wide.reshape(slabs * panel_order, 128)
    total = lookup.shape[0]
    out_rows = total // pack
    chunks = 2
    rows = out_rows // chunks
    return pl.pallas_call(
        gather_kernel,
        out_shape=jax.ShapeDtypeStruct((out_rows, 128), jnp.float32),
        grid_spec=pltpu.PrefetchScalarGridSpec(
            num_scalar_prefetch=1,
            grid=(chunks,),
            in_specs=[pl.BlockSpec(wide.shape, lambda c, idx: (0, 0))],
            out_specs=pl.BlockSpec((rows, 128), lambda c, idx: (c, 0)),
        ),
        cost_estimate=pl.CostEstimate(flops=0, bytes_accessed=wide.size * 4 + out_rows * 512, transcendentals=0),
    )(lookup, wide)


def gathered_panels(solved):
    count = lax.axis_size("dev")
    me = lax.axis_index("dev")
    bits = count.bit_length() - 1
    order = [bits - 1, 1, bits - 2, bits - 3, 0] if bits == 5 else list(range(bits))
    block = solved[None]
    for bit in order:
        partner = [(i, i ^ (1 << bit)) for i in range(count)]
        other = lax.ppermute(block, "dev", partner)
        high = ((me >> bit) & 1) == 1
        block = jnp.where(high, jnp.concatenate([other, block], 0), jnp.concatenate([block, other], 0))
    return block, order


def slab_position(slab, order):
    position = jnp.zeros_like(slab)
    for place, bit in enumerate(order):
        position = position + (((slab >> bit) & 1) << place)
    return position


def on_device(
    panel_inverse,
    coupling,
    loads,
    stiffness,
    element_substructure,
    element_rows,
    element_density,
    send_elements,
    receive_cells,
    design_density,
    filter_offsets,
    filter_weights,
):
    inverse = panel_inverse[0, 0]
    couple = coupling[0, 0]
    rights = loads[0, 0]
    held = (element_substructure, element_rows, element_density, send_elements, receive_cells, design_density)
    solved, held = interface_chain(inverse, couple, rights, held)
    element_substructure, element_rows, element_density, send_elements, receive_cells, design_density = held

    copies = jnp.broadcast_to(solved[None], (lax.axis_size("dev"),) + solved.shape)
    panels = lax.all_to_all(copies, "dev", split_axis=0, concat_axis=0, tiled=True)
    slabs, order, panel_order = panels.shape
    slab_place = element_substructure[0, 0]
    lookup = slab_place[None, :] * panel_order + element_rows[0, 0]
    dofs, elements = lookup.shape
    pack = 128 // order
    motion = gathered_rows(panels, lookup.reshape(-1)).reshape(dofs, elements // pack, 128)
    forces = jnp.einsum("ij,jab->iab", stiffness, motion, precision=exact_mode)
    energy = jnp.sum(jnp.sum(motion * forces, axis=0).reshape(elements // pack, pack, order), axis=2)
    energy = energy.reshape(elements)
    density = element_density[0, 0]
    sensitivity = -penalty * density * density * energy * energy_scale
    owned = design_density[0, 0]
    row_count = owned.shape[0]
    count = lax.axis_size("dev")
    cells = receive_cells[0, 0]
    sources, slots = cells.shape
    shared = cells.astype(jnp.float32).reshape(-1, 128)
    to_right = jnp.concatenate([shared, owned[row_count - RADIUS :]], axis=0)
    to_left = jnp.concatenate([shared, owned[:RADIUS]], axis=0)
    to_right, to_left, _ = lax.optimization_barrier((to_right, to_left, solved))
    from_left = lax.ppermute(to_right, "dev", [(i, i + 1) for i in range(count - 1)])
    from_right = lax.ppermute(to_left, "dev", [(i + 1, i) for i in range(count - 1)])
    list_rows = shared.shape[0]
    cells_left = from_left[:list_rows].astype(jnp.int32).reshape(sources, slots)
    cells_right = from_right[:list_rows].astype(jnp.int32).reshape(sources, slots)
    density_rows = jnp.concatenate([from_left[list_rows:], owned, from_right[list_rows:]], axis=0)

    outgoing = picked(sensitivity, send_elements[0, 0])
    edge = jnp.zeros((1, slots), jnp.float32)
    spread_out = jnp.concatenate([edge, outgoing, edge], axis=0)
    owners = outgoing.shape[0]
    triple = jnp.stack([spread_out[0:owners], spread_out[1 : owners + 1], spread_out[2 : owners + 2]], axis=1)
    received = lax.all_to_all(triple, "dev", split_axis=0, concat_axis=0, tiled=True)
    left_rows, left_cols = padded_targets(cells_left, row_count - RADIUS, row_count, RADIUS - row_count)
    own_rows, own_cols = padded_targets(cells, 0, row_count, RADIUS)
    right_rows, right_cols = padded_targets(cells_right, 0, RADIUS, row_count + RADIUS)
    collected = scattered(
        jnp.concatenate([received[:, 0].reshape(-1), received[:, 1].reshape(-1), received[:, 2].reshape(-1)]),
        jnp.concatenate([left_rows, own_rows, right_rows]),
        jnp.concatenate([left_cols, own_cols, right_cols]),
        row_count + 2 * RADIUS,
    )
    padded = density_rows * collected
    total_rows = lax.axis_size("dev") * row_count
    padded_rows = padded.shape[0]
    reach = (
        lax.broadcasted_iota(jnp.int32, (1, row_count, padded_rows), 2)
        - lax.broadcasted_iota(jnp.int32, (1, row_count, padded_rows), 1)
        - RADIUS
    )
    band = jnp.sum(
        jnp.where(reach == filter_offsets[:, None, None], filter_weights[:, None, None], 0.0), axis=0
    )
    padded_global = lax.axis_index("dev") * row_count - RADIUS + jnp.arange(padded_rows, dtype=jnp.int32)
    valid = ((padded_global >= 0) & (padded_global < total_rows)).astype(jnp.float32)
    weight_sum = jnp.sum(band * valid[None, :], axis=1)
    accum = product(band, padded)
    filtered = accum / (owned * weight_sum[:, None])
    return (solved[None, None], filtered[None, None])


def solution(mesh):
    placed = (
        P("grp", "dev", None, None),
        P("grp", "dev", None, None),
        P("grp", "dev", None, None),
        P(),
        P("grp", "dev", None),
        P("grp", "dev", None, None),
        P("grp", "dev", None),
        P("grp", "dev", None, None),
        P("grp", "dev", None, None),
        P("grp", "dev", None, None),
        P(),
        P(),
    )
    return jax.shard_map(
        on_device,
        mesh=mesh,
        in_specs=placed,
        out_specs=(P("grp", "dev", None, None), P("grp", "dev", None, None)),
        check_vma=False,
    )
```

```python
import jax
import jax.numpy as jnp
from jax import lax
from jax.sharding import PartitionSpec as P
from jax.experimental import pallas as pl
from jax.experimental.pallas import tpu as pltpu

NK = 8
RADIUS = 3


exact_mode = lax.Precision.HIGHEST
penalty = 3.0
energy_scale = 1.0 / 4096.0


def passed_along(value, axis, steps):
    count = lax.axis_size(axis)
    leading, last = (max(0, -steps), min(count, count - steps))
    return lax.ppermute(value, axis, [(source, source + steps) for source in range(leading, last)])


def padded_2(cells, sides, width):
    for axis, dim in sides:
        count = lax.axis_size(axis)
        ends = count - 1
        head = lax.slice_in_dim(cells, 0, width, axis=dim)
        tail = lax.slice_in_dim(cells, cells.shape[dim] - width, cells.shape[dim], axis=dim)
        cells = jnp.concatenate(
            [
                lax.ppermute(tail, axis, [(i, (i + 1) % count) for i in range(ends)]),
                cells,
                lax.ppermute(head, axis, [((i + 1) % count, i) for i in range(ends)]),
            ],
            axis=dim,
        )
    return cells


def product(left, right):
    return jnp.dot(left, right, precision=exact_mode, preferred_element_type=jnp.float32)


def interface_chain(inverse, couple, rights, held):
    offset = product(rights, inverse)
    step = -product(couple, inverse)
    order = rights.shape[0]
    levels = lax.axis_size("grp")

    def combine(pairs, with_step):
        nonlocal offset, composite
        if with_step:
            packed = jnp.concatenate([offset, composite], axis=0)
            half = packed.shape[0] // 2
            packed = jnp.concatenate(
                [lax.ppermute(packed[:half], "grp", pairs), lax.ppermute(packed[half:], "grp", pairs)], axis=0
            )
            earlier_offset, earlier_step = packed[:order], packed[order:]
            offset = product(earlier_offset, composite) + offset
            composite = product(earlier_step, composite)
        else:
            earlier_offset = lax.ppermute(offset, "grp", pairs)
            offset = product(earlier_offset, composite) + offset

    composite = step
    combine([(g, g + 1) for g in range(0, levels - 1, 2)], True)
    shift = 2
    while shift < levels:
        pairs = [(g, g + shift) for g in range(1, levels - shift, 2)]
        combine(pairs, 2 * shift < levels)
        if shift == 2:
            held, offset = lax.optimization_barrier((held, offset))
        shift *= 2
    earlier_offset = lax.ppermute(offset, "grp", [(g, g + 1) for g in range(1, levels - 1, 2)])
    return product(earlier_offset, step) + offset, held


def split_product(hot, values, dimensions):
    hot = hot.astype(jnp.bfloat16)
    rest = values
    total = None
    for _ in range(3):
        rounded = lax.reduce_precision(rest, exponent_bits=8, mantissa_bits=7)
        rest = rest - rounded
        term = lax.dot_general(hot, rounded.astype(jnp.bfloat16), dimensions, preferred_element_type=jnp.float32)
        total = term if total is None else total + term
    return total


def picked(values, index):
    flat = index.reshape(-1)
    ids = lax.broadcasted_iota(jnp.int32, (1, values.shape[0]), 1)
    hot = flat[:, None] == ids
    chosen = split_product(hot, values[:, None], (((1,), (0,)), ((), ())))
    return chosen.reshape(index.shape)


def scattered(values, rows, cols, row_count):
    lanes = 128
    row_ids = lax.broadcasted_iota(jnp.int32, (1, row_count), 1)
    lane_ids = lax.broadcasted_iota(jnp.int32, (1, lanes), 1)
    rows_hot = rows[:, None] == row_ids
    cols_hot = jnp.where(cols[:, None] == lane_ids, values[:, None], 0.0)
    return split_product(rows_hot, cols_hot, (((0,), (0,)), ((), ())))


def padded_targets(cells, first, last, shift):
    row = cells // 128
    keep = (cells >= 0) & (row >= first) & (row < last)
    return jnp.where(keep, row + shift, -1).reshape(-1), (cells % 128).reshape(-1)


def gather_kernel(lookup_ref, table_ref, out_ref):
    chunk = pl.program_id(0)
    rows = out_ref.shape[0]
    pack = out_ref.shape[1] // 16
    group = lax.broadcasted_iota(jnp.int32, (1, out_ref.shape[1]), 1) // 16
    base = chunk * rows * pack

    def body(row, carry):
        packed_row = jnp.zeros((1, out_ref.shape[1]), jnp.float32)
        for part in range(pack):
            where = lookup_ref[base + row * pack + part]
            packed_row = jnp.where(group == part, table_ref[pl.ds(where, 1), :], packed_row)
        out_ref[pl.ds(row, 1), :] = packed_row
        return carry

    lax.fori_loop(0, rows, body, 0, unroll=8)


def gathered_rows(panels, lookup):
    slabs, width, panel_order = panels.shape
    pack = 128 // width
    spread = (
        lax.broadcasted_iota(jnp.int32, (width, 128), 0)
        == lax.broadcasted_iota(jnp.int32, (width, 128), 1) % width
    ).astype(jnp.float32)
    spread = spread.astype(jnp.bfloat16)
    rest = panels
    wide = None
    for _ in range(3):
        rounded = lax.reduce_precision(rest, exponent_bits=8, mantissa_bits=7)
        rest = rest - rounded
        part = rounded.astype(jnp.bfloat16)
        term = lax.dot_general(part, spread, (((1,), (0,)), ((), ())), preferred_element_type=jnp.float32)
        wide = term if wide is None else wide + term
    wide = wide.reshape(slabs * panel_order, 128)
    total = lookup.shape[0]
    out_rows = total // pack
    chunks = 2
    rows = out_rows // chunks
    return pl.pallas_call(
        gather_kernel,
        out_shape=jax.ShapeDtypeStruct((out_rows, 128), jnp.float32),
        grid_spec=pltpu.PrefetchScalarGridSpec(
            num_scalar_prefetch=1,
            grid=(chunks,),
            in_specs=[pl.BlockSpec(wide.shape, lambda c, idx: (0, 0))],
            out_specs=pl.BlockSpec((rows, 128), lambda c, idx: (c, 0)),
        ),
        cost_estimate=pl.CostEstimate(flops=0, bytes_accessed=wide.size * 4 + out_rows * 512, transcendentals=0),
    )(lookup, wide)


def gathered_panels(solved):
    count = lax.axis_size("dev")
    me = lax.axis_index("dev")
    bits = count.bit_length() - 1
    order = [bits - 1, 1, bits - 2, bits - 3, 0] if bits == 5 else list(range(bits))
    block = solved[None]
    for bit in order:
        partner = [(i, i ^ (1 << bit)) for i in range(count)]
        other = lax.ppermute(block, "dev", partner)
        high = ((me >> bit) & 1) == 1
        block = jnp.where(high, jnp.concatenate([other, block], 0), jnp.concatenate([block, other], 0))
    return block, order


def slab_position(slab, order):
    position = jnp.zeros_like(slab)
    for place, bit in enumerate(order):
        position = position + (((slab >> bit) & 1) << place)
    return position


def on_device(
    panel_inverse,
    coupling,
    loads,
    stiffness,
    element_substructure,
    element_rows,
    element_density,
    send_elements,
    receive_cells,
    design_density,
    filter_offsets,
    filter_weights,
):
    inverse = panel_inverse[0, 0]
    couple = coupling[0, 0]
    rights = loads[0, 0]
    held = (element_substructure, element_rows, element_density, send_elements, receive_cells, design_density)
    solved, held = interface_chain(inverse, couple, rights, held)
    element_substructure, element_rows, element_density, send_elements, receive_cells, design_density = held

    copies = jnp.broadcast_to(solved[None], (lax.axis_size("dev"),) + solved.shape)
    panels = lax.all_to_all(copies, "dev", split_axis=0, concat_axis=0, tiled=True)
    slabs, order, panel_order = panels.shape
    slab_place = element_substructure[0, 0]
    lookup = slab_place[None, :] * panel_order + element_rows[0, 0]
    dofs, elements = lookup.shape
    pack = 128 // order
    motion = gathered_rows(panels, lookup.reshape(-1)).reshape(dofs, elements // pack, 128)
    forces = jnp.einsum("ij,jab->iab", stiffness, motion, precision=exact_mode)
    energy = jnp.sum(jnp.sum(motion * forces, axis=0).reshape(elements // pack, pack, order), axis=2)
    energy = energy.reshape(elements)
    density = element_density[0, 0]
    sensitivity = -penalty * density * density * energy * energy_scale
    owned = design_density[0, 0]
    row_count = owned.shape[0]
    count = lax.axis_size("dev")
    cells = receive_cells[0, 0]
    sources, slots = cells.shape
    shared = cells.astype(jnp.float32).reshape(-1, 128)
    to_right = jnp.concatenate([shared, owned[row_count - RADIUS :]], axis=0)
    to_left = jnp.concatenate([shared, owned[:RADIUS]], axis=0)
    to_right, to_left, _ = lax.optimization_barrier((to_right, to_left, solved))
    from_left = lax.ppermute(to_right, "dev", [(i, i + 1) for i in range(count - 1)])
    from_right = lax.ppermute(to_left, "dev", [(i + 1, i) for i in range(count - 1)])
    list_rows = shared.shape[0]
    cells_left = from_left[:list_rows].astype(jnp.int32).reshape(sources, slots)
    cells_right = from_right[:list_rows].astype(jnp.int32).reshape(sources, slots)
    density_rows = jnp.concatenate([from_left[list_rows:], owned, from_right[list_rows:]], axis=0)

    outgoing = picked(sensitivity, send_elements[0, 0])
    edge = jnp.zeros((1, slots), jnp.float32)
    spread_out = jnp.concatenate([edge, outgoing, edge], axis=0)
    owners = outgoing.shape[0]
    triple = jnp.stack([spread_out[0:owners], spread_out[1 : owners + 1], spread_out[2 : owners + 2]], axis=1)
    received = lax.all_to_all(triple, "dev", split_axis=0, concat_axis=0, tiled=True)
    left_rows, left_cols = padded_targets(cells_left, row_count - RADIUS, row_count, RADIUS - row_count)
    own_rows, own_cols = padded_targets(cells, 0, row_count, RADIUS)
    right_rows, right_cols = padded_targets(cells_right, 0, RADIUS, row_count + RADIUS)
    collected = scattered(
        jnp.concatenate([received[:, 0].reshape(-1), received[:, 1].reshape(-1), received[:, 2].reshape(-1)]),
        jnp.concatenate([left_rows, own_rows, right_rows]),
        jnp.concatenate([left_cols, own_cols, right_cols]),
        row_count + 2 * RADIUS,
    )
    padded = density_rows * collected
    total_rows = lax.axis_size("dev") * row_count
    padded_rows = padded.shape[0]
    reach = (
        lax.broadcasted_iota(jnp.int32, (1, row_count, padded_rows), 2)
        - lax.broadcasted_iota(jnp.int32, (1, row_count, padded_rows), 1)
        - RADIUS
    )
    band = jnp.sum(
        jnp.where(reach == filter_offsets[:, None, None], filter_weights[:, None, None], 0.0), axis=0
    )
    padded_global = lax.axis_index("dev") * row_count - RADIUS + jnp.arange(padded_rows, dtype=jnp.int32)
    valid = ((padded_global >= 0) & (padded_global < total_rows)).astype(jnp.float32)
    weight_sum = jnp.sum(band * valid[None, :], axis=1)
    accum = product(band, padded)
    filtered = accum / (owned * weight_sum[:, None])
    return (solved[None, None], filtered[None, None])


def solution(mesh):
    placed = (
        P("grp", "dev", None, None),
        P("grp", "dev", None, None),
        P("grp", "dev", None, None),
        P(),
        P("grp", "dev", None),
        P("grp", "dev", None, None),
        P("grp", "dev", None),
        P("grp", "dev", None, None),
        P("grp", "dev", None, None),
        P("grp", "dev", None, None),
        P(),
        P(),
    )
    return jax.shard_map(
        on_device,
        mesh=mesh,
        in_specs=placed,
        out_specs=(P("grp", "dev", None, None), P("grp", "dev", None, None)),
        check_vma=False,
    )
```

```python
import jax
import jax.numpy as jnp
from jax import lax
from jax.sharding import PartitionSpec as P
from jax.experimental import pallas as pl
from jax.experimental.pallas import tpu as pltpu

NK = 8
RADIUS = 3


exact_mode = lax.Precision.HIGHEST
penalty = 3.0
energy_scale = 1.0 / 4096.0


def passed_along(value, axis, steps):
    count = lax.axis_size(axis)
    leading, last = (max(0, -steps), min(count, count - steps))
    return lax.ppermute(value, axis, [(source, source + steps) for source in range(leading, last)])


def padded_2(cells, sides, width):
    for axis, dim in sides:
        count = lax.axis_size(axis)
        ends = count - 1
        head = lax.slice_in_dim(cells, 0, width, axis=dim)
        tail = lax.slice_in_dim(cells, cells.shape[dim] - width, cells.shape[dim], axis=dim)
        cells = jnp.concatenate(
            [
                lax.ppermute(tail, axis, [(i, (i + 1) % count) for i in range(ends)]),
                cells,
                lax.ppermute(head, axis, [((i + 1) % count, i) for i in range(ends)]),
            ],
            axis=dim,
        )
    return cells


def product(left, right):
    return jnp.dot(left, right, precision=exact_mode, preferred_element_type=jnp.float32)


def interface_chain(inverse, couple, rights, held):
    offset = product(rights, inverse)
    step = -product(couple, inverse)
    order = rights.shape[0]
    levels = lax.axis_size("grp")

    def combine(pairs, with_step):
        nonlocal offset, composite
        if with_step:
            packed = jnp.concatenate([offset, composite], axis=0)
            half = packed.shape[0] // 2
            packed = jnp.concatenate(
                [lax.ppermute(packed[:half], "grp", pairs), lax.ppermute(packed[half:], "grp", pairs)], axis=0
            )
            earlier_offset, earlier_step = packed[:order], packed[order:]
            offset = product(earlier_offset, composite) + offset
            composite = product(earlier_step, composite)
        else:
            earlier_offset = lax.ppermute(offset, "grp", pairs)
            offset = product(earlier_offset, composite) + offset

    composite = step
    combine([(g, g + 1) for g in range(0, levels - 1, 2)], True)
    shift = 2
    while shift < levels:
        pairs = [(g, g + shift) for g in range(1, levels - shift, 2)]
        combine(pairs, 2 * shift < levels)
        if shift == 2:
            held, offset = lax.optimization_barrier((held, offset))
        shift *= 2
    earlier_offset = lax.ppermute(offset, "grp", [(g, g + 1) for g in range(1, levels - 1, 2)])
    return product(earlier_offset, step) + offset, held


def picked(values, index):
    lanes = 128
    table = values.reshape(-1, lanes)
    flat = index.reshape(-1)
    high = flat // lanes
    low = flat % lanes
    rows = jnp.zeros((flat.shape[0], lanes), values.dtype)
    for which in range(table.shape[0]):
        rows = rows + jnp.where((high == which)[:, None], table[which][None, :], 0.0)
    lane_ids = lax.broadcasted_iota(jnp.int32, (1, lanes), 1)
    chosen = jnp.sum(jnp.where(lane_ids == low[:, None], rows, 0.0), axis=1)
    return chosen.reshape(index.shape)


def scattered(values, rows, cols, row_count):
    lanes = 128
    row_ids = lax.broadcasted_iota(jnp.int32, (1, row_count), 1)
    lane_ids = lax.broadcasted_iota(jnp.int32, (1, lanes), 1)
    rows_hot = (rows[:, None] == row_ids).astype(jnp.float32)
    cols_hot = jnp.where(cols[:, None] == lane_ids, values[:, None], 0.0)
    return lax.dot_general(
        rows_hot,
        cols_hot,
        (((0,), (0,)), ((), ())),
        precision=exact_mode,
        preferred_element_type=jnp.float32,
    )


def padded_targets(cells, first, last, shift):
    row = cells // 128
    keep = (cells >= 0) & (row >= first) & (row < last)
    return jnp.where(keep, row + shift, -1).reshape(-1), (cells % 128).reshape(-1)


def gather_kernel(lookup_ref, table_ref, out_ref):
    chunk = pl.program_id(0)
    rows = out_ref.shape[0]
    pack = out_ref.shape[1] // 16
    group = lax.broadcasted_iota(jnp.int32, (1, out_ref.shape[1]), 1) // 16
    base = chunk * rows * pack

    def body(row, carry):
        packed_row = jnp.zeros((1, out_ref.shape[1]), jnp.float32)
        for part in range(pack):
            where = lookup_ref[base + row * pack + part]
            packed_row = jnp.where(group == part, table_ref[pl.ds(where, 1), :], packed_row)
        out_ref[pl.ds(row, 1), :] = packed_row
        return carry

    lax.fori_loop(0, rows, body, 0, unroll=8)


def gathered_rows(panels, lookup):
    slabs, width, panel_order = panels.shape
    pack = 128 // width
    spread = (
        lax.broadcasted_iota(jnp.int32, (width, 128), 0)
        == lax.broadcasted_iota(jnp.int32, (width, 128), 1) % width
    ).astype(jnp.float32)
    spread = spread.astype(jnp.bfloat16)
    rest = panels
    parts = []
    for _ in range(3):
        rounded = lax.reduce_precision(rest, exponent_bits=8, mantissa_bits=7)
        rest = rest - rounded
        parts.append(rounded.astype(jnp.bfloat16))
    terms = lax.dot_general(
        jnp.concatenate(parts, axis=0), spread, (((1,), (0,)), ((), ())), preferred_element_type=jnp.float32
    ).reshape(3, slabs * panel_order, 128)
    wide = (terms[0] + terms[1]) + terms[2]
    total = lookup.shape[0]
    out_rows = total // pack
    chunks = 2
    rows = out_rows // chunks
    return pl.pallas_call(
        gather_kernel,
        out_shape=jax.ShapeDtypeStruct((out_rows, 128), jnp.float32),
        grid_spec=pltpu.PrefetchScalarGridSpec(
            num_scalar_prefetch=1,
            grid=(chunks,),
            in_specs=[pl.BlockSpec(wide.shape, lambda c, idx: (0, 0))],
            out_specs=pl.BlockSpec((rows, 128), lambda c, idx: (c, 0)),
        ),
        cost_estimate=pl.CostEstimate(flops=0, bytes_accessed=wide.size * 4 + out_rows * 512, transcendentals=0),
    )(lookup, wide)


def gathered_panels(solved):
    count = lax.axis_size("dev")
    me = lax.axis_index("dev")
    bits = count.bit_length() - 1
    order = [bits - 1, 1, bits - 2, bits - 3, 0] if bits == 5 else list(range(bits))
    block = solved[None]
    for bit in order:
        partner = [(i, i ^ (1 << bit)) for i in range(count)]
        other = lax.ppermute(block, "dev", partner)
        high = ((me >> bit) & 1) == 1
        block = jnp.where(high, jnp.concatenate([other, block], 0), jnp.concatenate([block, other], 0))
    return block, order


def slab_position(slab, order):
    position = jnp.zeros_like(slab)
    for place, bit in enumerate(order):
        position = position + (((slab >> bit) & 1) << place)
    return position


def on_device(
    panel_inverse,
    coupling,
    loads,
    stiffness,
    element_substructure,
    element_rows,
    element_density,
    send_elements,
    receive_cells,
    design_density,
    filter_offsets,
    filter_weights,
):
    inverse = panel_inverse[0, 0]
    couple = coupling[0, 0]
    rights = loads[0, 0]
    held = (element_substructure, element_rows, element_density, send_elements, receive_cells, design_density)
    solved, held = interface_chain(inverse, couple, rights, held)
    element_substructure, element_rows, element_density, send_elements, receive_cells, design_density = held

    copies = jnp.broadcast_to(solved[None], (lax.axis_size("dev"),) + solved.shape)
    panels = lax.all_to_all(copies, "dev", split_axis=0, concat_axis=0, tiled=True)
    slabs, order, panel_order = panels.shape
    slab_place = element_substructure[0, 0]
    lookup = slab_place[None, :] * panel_order + element_rows[0, 0]
    dofs, elements = lookup.shape
    pack = 128 // order
    motion = gathered_rows(panels, lookup.reshape(-1)).reshape(dofs, elements // pack, 128)
    forces = jnp.einsum("ij,jab->iab", stiffness, motion, precision=exact_mode)
    energy = jnp.sum(jnp.sum(motion * forces, axis=0).reshape(elements // pack, pack, order), axis=2)
    energy = energy.reshape(elements)
    density = element_density[0, 0]
    sensitivity = -penalty * density * density * energy * energy_scale
    owned = design_density[0, 0]
    row_count = owned.shape[0]
    count = lax.axis_size("dev")
    cells = receive_cells[0, 0]
    sources, slots = cells.shape
    shared = cells.astype(jnp.float32).reshape(-1, 128)
    to_right = jnp.concatenate([shared, owned[row_count - RADIUS :]], axis=0)
    to_left = jnp.concatenate([shared, owned[:RADIUS]], axis=0)
    to_right, to_left, _ = lax.optimization_barrier((to_right, to_left, solved))
    from_left = lax.ppermute(to_right, "dev", [(i, i + 1) for i in range(count - 1)])
    from_right = lax.ppermute(to_left, "dev", [(i + 1, i) for i in range(count - 1)])
    list_rows = shared.shape[0]
    cells_left = from_left[:list_rows].astype(jnp.int32).reshape(sources, slots)
    cells_right = from_right[:list_rows].astype(jnp.int32).reshape(sources, slots)
    density_rows = jnp.concatenate([from_left[list_rows:], owned, from_right[list_rows:]], axis=0)

    outgoing = picked(sensitivity, send_elements[0, 0])
    edge = jnp.zeros((1, slots), jnp.float32)
    spread_out = jnp.concatenate([edge, outgoing, edge], axis=0)
    owners = outgoing.shape[0]
    triple = jnp.stack([spread_out[0:owners], spread_out[1 : owners + 1], spread_out[2 : owners + 2]], axis=1)
    received = lax.all_to_all(triple, "dev", split_axis=0, concat_axis=0, tiled=True)
    left_rows, left_cols = padded_targets(cells_left, row_count - RADIUS, row_count, RADIUS - row_count)
    own_rows, own_cols = padded_targets(cells, 0, row_count, RADIUS)
    right_rows, right_cols = padded_targets(cells_right, 0, RADIUS, row_count + RADIUS)
    collected = scattered(
        jnp.concatenate([received[:, 0].reshape(-1), received[:, 1].reshape(-1), received[:, 2].reshape(-1)]),
        jnp.concatenate([left_rows, own_rows, right_rows]),
        jnp.concatenate([left_cols, own_cols, right_cols]),
        row_count + 2 * RADIUS,
    )
    padded = density_rows * collected
    total_rows = lax.axis_size("dev") * row_count
    padded_rows = padded.shape[0]
    reach = (
        lax.broadcasted_iota(jnp.int32, (1, row_count, padded_rows), 2)
        - lax.broadcasted_iota(jnp.int32, (1, row_count, padded_rows), 1)
        - RADIUS
    )
    band = jnp.sum(
        jnp.where(reach == filter_offsets[:, None, None], filter_weights[:, None, None], 0.0), axis=0
    )
    padded_global = lax.axis_index("dev") * row_count - RADIUS + jnp.arange(padded_rows, dtype=jnp.int32)
    valid = ((padded_global >= 0) & (padded_global < total_rows)).astype(jnp.float32)
    weight_sum = jnp.sum(band * valid[None, :], axis=1)
    accum = product(band, padded)
    filtered = accum / (owned * weight_sum[:, None])
    return (solved[None, None], filtered[None, None])


def solution(mesh):
    placed = (
        P("grp", "dev", None, None),
        P("grp", "dev", None, None),
        P("grp", "dev", None, None),
        P(),
        P("grp", "dev", None),
        P("grp", "dev", None, None),
        P("grp", "dev", None),
        P("grp", "dev", None, None),
        P("grp", "dev", None, None),
        P("grp", "dev", None, None),
        P(),
        P(),
    )
    return jax.shard_map(
        on_device,
        mesh=mesh,
        in_specs=placed,
        out_specs=(P("grp", "dev", None, None), P("grp", "dev", None, None)),
        check_vma=False,
    )
```

```python
import jax
import jax.numpy as jnp
from jax import lax
from jax.sharding import PartitionSpec as P
from jax.experimental import pallas as pl
from jax.experimental.pallas import tpu as pltpu

NK = 8
RADIUS = 3


exact_mode = lax.Precision.HIGHEST
penalty = 3.0
energy_scale = 1.0 / 4096.0


def passed_along(value, axis, steps):
    count = lax.axis_size(axis)
    leading, last = (max(0, -steps), min(count, count - steps))
    return lax.ppermute(value, axis, [(source, source + steps) for source in range(leading, last)])


def padded_2(cells, sides, width):
    for axis, dim in sides:
        count = lax.axis_size(axis)
        ends = count - 1
        head = lax.slice_in_dim(cells, 0, width, axis=dim)
        tail = lax.slice_in_dim(cells, cells.shape[dim] - width, cells.shape[dim], axis=dim)
        cells = jnp.concatenate(
            [
                lax.ppermute(tail, axis, [(i, (i + 1) % count) for i in range(ends)]),
                cells,
                lax.ppermute(head, axis, [((i + 1) % count, i) for i in range(ends)]),
            ],
            axis=dim,
        )
    return cells


def product(left, right):
    return jnp.dot(left, right, precision=exact_mode, preferred_element_type=jnp.float32)


def interface_chain(inverse, couple, rights, held):
    offset = product(rights, inverse)
    step = -product(couple, inverse)
    order = rights.shape[0]
    levels = lax.axis_size("grp")

    def combine(pairs, with_step):
        nonlocal offset, composite
        if with_step:
            packed = jnp.concatenate([offset, composite], axis=0)
            half = packed.shape[0] // 2
            packed = jnp.concatenate(
                [lax.ppermute(packed[:half], "grp", pairs), lax.ppermute(packed[half:], "grp", pairs)], axis=0
            )
            earlier_offset, earlier_step = packed[:order], packed[order:]
            offset = product(earlier_offset, composite) + offset
            composite = product(earlier_step, composite)
        else:
            earlier_offset = lax.ppermute(offset, "grp", pairs)
            offset = product(earlier_offset, composite) + offset

    composite = step
    combine([(g, g + 1) for g in range(0, levels - 1, 2)], True)
    shift = 2
    while shift < levels:
        pairs = [(g, g + shift) for g in range(1, levels - shift, 2)]
        combine(pairs, 2 * shift < levels)
        if shift == 2:
            held, offset = lax.optimization_barrier((held, offset))
        shift *= 2
    earlier_offset = lax.ppermute(offset, "grp", [(g, g + 1) for g in range(1, levels - 1, 2)])
    return product(earlier_offset, step) + offset, held


def picked(values, index):
    lanes = 128
    table = values.reshape(-1, lanes)
    flat = index.reshape(-1)
    high = flat // lanes
    low = flat % lanes
    rows = jnp.zeros((flat.shape[0], lanes), values.dtype)
    for which in range(table.shape[0]):
        rows = rows + jnp.where((high == which)[:, None], table[which][None, :], 0.0)
    lane_ids = lax.broadcasted_iota(jnp.int32, (1, lanes), 1)
    chosen = jnp.sum(jnp.where(lane_ids == low[:, None], rows, 0.0), axis=1)
    return chosen.reshape(index.shape)


def scattered(values, rows, cols, row_count):
    lanes = 128
    row_ids = lax.broadcasted_iota(jnp.int32, (1, row_count), 1)
    lane_ids = lax.broadcasted_iota(jnp.int32, (1, lanes), 1)
    rows_hot = (rows[:, None] == row_ids).astype(jnp.float32)
    cols_hot = jnp.where(cols[:, None] == lane_ids, values[:, None], 0.0)
    return lax.dot_general(
        rows_hot,
        cols_hot,
        (((0,), (0,)), ((), ())),
        precision=exact_mode,
        preferred_element_type=jnp.float32,
    )


def padded_targets(cells, first, last, shift):
    row = cells // 128
    keep = (cells >= 0) & (row >= first) & (row < last)
    return jnp.where(keep, row + shift, -1).reshape(-1), (cells % 128).reshape(-1)


def gather_kernel(lookup_ref, table_ref, out_ref):
    chunk = pl.program_id(0)
    rows = out_ref.shape[0]
    pack = out_ref.shape[1] // 16
    group = lax.broadcasted_iota(jnp.int32, (1, out_ref.shape[1]), 1) // 16
    base = chunk * rows * pack

    def body(row, carry):
        packed_row = jnp.zeros((1, out_ref.shape[1]), jnp.float32)
        for part in range(pack):
            where = lookup_ref[base + row * pack + part]
            packed_row = jnp.where(group == part, table_ref[pl.ds(where, 1), :], packed_row)
        out_ref[pl.ds(row, 1), :] = packed_row
        return carry

    lax.fori_loop(0, rows, body, 0, unroll=8)


def gathered_rows(panels, lookup):
    slabs, width, panel_order = panels.shape
    pack = 128 // width
    spread = (
        lax.broadcasted_iota(jnp.int32, (width, 128), 0)
        == lax.broadcasted_iota(jnp.int32, (width, 128), 1) % width
    ).astype(jnp.float32)
    spread = spread.astype(jnp.bfloat16)
    rest = panels
    wide = None
    for _ in range(3):
        rounded = lax.reduce_precision(rest, exponent_bits=8, mantissa_bits=7)
        rest = rest - rounded
        part = rounded.astype(jnp.bfloat16)
        term = lax.dot_general(part, spread, (((1,), (0,)), ((), ())), preferred_element_type=jnp.float32)
        wide = term if wide is None else wide + term
    wide = wide.reshape(slabs * panel_order, 128)
    total = lookup.shape[0]
    out_rows = total // pack
    chunks = 2
    rows = out_rows // chunks
    return pl.pallas_call(
        gather_kernel,
        out_shape=jax.ShapeDtypeStruct((out_rows, 128), jnp.float32),
        grid_spec=pltpu.PrefetchScalarGridSpec(
            num_scalar_prefetch=1,
            grid=(chunks,),
            in_specs=[pl.BlockSpec(wide.shape, lambda c, idx: (0, 0))],
            out_specs=pl.BlockSpec((rows, 128), lambda c, idx: (c, 0)),
        ),
        cost_estimate=pl.CostEstimate(flops=0, bytes_accessed=wide.size * 4 + out_rows * 512, transcendentals=0),
    )(lookup, wide)


def gathered_panels(solved):
    count = lax.axis_size("dev")
    me = lax.axis_index("dev")
    bits = count.bit_length() - 1
    order = [bits - 1, 1, bits - 2, bits - 3, 0] if bits == 5 else list(range(bits))
    block = solved[None]
    for bit in order:
        partner = [(i, i ^ (1 << bit)) for i in range(count)]
        other = lax.ppermute(block, "dev", partner)
        high = ((me >> bit) & 1) == 1
        block = jnp.where(high, jnp.concatenate([other, block], 0), jnp.concatenate([block, other], 0))
    return block, order


def slab_position(slab, order):
    position = jnp.zeros_like(slab)
    for place, bit in enumerate(order):
        position = position + (((slab >> bit) & 1) << place)
    return position


def on_device(
    panel_inverse,
    coupling,
    loads,
    stiffness,
    element_substructure,
    element_rows,
    element_density,
    send_elements,
    receive_cells,
    design_density,
    filter_offsets,
    filter_weights,
):
    inverse = panel_inverse[0, 0]
    couple = coupling[0, 0]
    rights = loads[0, 0]
    held = (element_substructure, element_rows, element_density, send_elements, receive_cells, design_density)
    solved, held = interface_chain(inverse, couple, rights, held)
    element_substructure, element_rows, element_density, send_elements, receive_cells, design_density = held

    copies = jnp.broadcast_to(solved[None], (lax.axis_size("dev"),) + solved.shape)
    panels = lax.all_to_all(copies, "dev", split_axis=0, concat_axis=0, tiled=True)
    slabs, order, panel_order = panels.shape
    slab_place = element_substructure[0, 0]
    lookup = slab_place[None, :] * panel_order + element_rows[0, 0]
    dofs, elements = lookup.shape
    pack = 128 // order
    motion = gathered_rows(panels, lookup.reshape(-1)).reshape(dofs, elements // pack, 128)
    forces = jnp.einsum("ij,jab->iab", stiffness, motion, precision=lax.Precision.HIGH)
    energy = jnp.sum(jnp.sum(motion * forces, axis=0).reshape(elements // pack, pack, order), axis=2)
    energy = energy.reshape(elements)
    density = element_density[0, 0]
    sensitivity = -penalty * density * density * energy * energy_scale
    owned = design_density[0, 0]
    row_count = owned.shape[0]
    count = lax.axis_size("dev")
    cells = receive_cells[0, 0]
    sources, slots = cells.shape
    shared = cells.astype(jnp.float32).reshape(-1, 128)
    to_right = jnp.concatenate([shared, owned[row_count - RADIUS :]], axis=0)
    to_left = jnp.concatenate([shared, owned[:RADIUS]], axis=0)
    to_right, to_left, _ = lax.optimization_barrier((to_right, to_left, solved))
    from_left = lax.ppermute(to_right, "dev", [(i, i + 1) for i in range(count - 1)])
    from_right = lax.ppermute(to_left, "dev", [(i + 1, i) for i in range(count - 1)])
    list_rows = shared.shape[0]
    cells_left = from_left[:list_rows].astype(jnp.int32).reshape(sources, slots)
    cells_right = from_right[:list_rows].astype(jnp.int32).reshape(sources, slots)
    density_rows = jnp.concatenate([from_left[list_rows:], owned, from_right[list_rows:]], axis=0)

    outgoing = picked(sensitivity, send_elements[0, 0])
    edge = jnp.zeros((1, slots), jnp.float32)
    spread_out = jnp.concatenate([edge, outgoing, edge], axis=0)
    owners = outgoing.shape[0]
    triple = jnp.stack([spread_out[0:owners], spread_out[1 : owners + 1], spread_out[2 : owners + 2]], axis=1)
    received = lax.all_to_all(triple, "dev", split_axis=0, concat_axis=0, tiled=True)
    left_rows, left_cols = padded_targets(cells_left, row_count - RADIUS, row_count, RADIUS - row_count)
    own_rows, own_cols = padded_targets(cells, 0, row_count, RADIUS)
    right_rows, right_cols = padded_targets(cells_right, 0, RADIUS, row_count + RADIUS)
    collected = scattered(
        jnp.concatenate([received[:, 0].reshape(-1), received[:, 1].reshape(-1), received[:, 2].reshape(-1)]),
        jnp.concatenate([left_rows, own_rows, right_rows]),
        jnp.concatenate([left_cols, own_cols, right_cols]),
        row_count + 2 * RADIUS,
    )
    padded = density_rows * collected
    total_rows = lax.axis_size("dev") * row_count
    padded_rows = padded.shape[0]
    reach = (
        lax.broadcasted_iota(jnp.int32, (1, row_count, padded_rows), 2)
        - lax.broadcasted_iota(jnp.int32, (1, row_count, padded_rows), 1)
        - RADIUS
    )
    band = jnp.sum(
        jnp.where(reach == filter_offsets[:, None, None], filter_weights[:, None, None], 0.0), axis=0
    )
    padded_global = lax.axis_index("dev") * row_count - RADIUS + jnp.arange(padded_rows, dtype=jnp.int32)
    valid = ((padded_global >= 0) & (padded_global < total_rows)).astype(jnp.float32)
    weight_sum = jnp.sum(band * valid[None, :], axis=1)
    accum = product(band, padded)
    filtered = accum / (owned * weight_sum[:, None])
    return (solved[None, None], filtered[None, None])


def solution(mesh):
    placed = (
        P("grp", "dev", None, None),
        P("grp", "dev", None, None),
        P("grp", "dev", None, None),
        P(),
        P("grp", "dev", None),
        P("grp", "dev", None, None),
        P("grp", "dev", None),
        P("grp", "dev", None, None),
        P("grp", "dev", None, None),
        P("grp", "dev", None, None),
        P(),
        P(),
    )
    return jax.shard_map(
        on_device,
        mesh=mesh,
        in_specs=placed,
        out_specs=(P("grp", "dev", None, None), P("grp", "dev", None, None)),
        check_vma=False,
    )
```

```python
import jax
import jax.numpy as jnp
from jax import lax
from jax.sharding import PartitionSpec as P
from jax.experimental import pallas as pl
from jax.experimental.pallas import tpu as pltpu

NK = 8
RADIUS = 3


exact_mode = lax.Precision.HIGHEST
penalty = 3.0
energy_scale = 1.0 / 4096.0


def passed_along(value, axis, steps):
    count = lax.axis_size(axis)
    leading, last = (max(0, -steps), min(count, count - steps))
    return lax.ppermute(value, axis, [(source, source + steps) for source in range(leading, last)])


def padded_2(cells, sides, width):
    for axis, dim in sides:
        count = lax.axis_size(axis)
        ends = count - 1
        head = lax.slice_in_dim(cells, 0, width, axis=dim)
        tail = lax.slice_in_dim(cells, cells.shape[dim] - width, cells.shape[dim], axis=dim)
        cells = jnp.concatenate(
            [
                lax.ppermute(tail, axis, [(i, (i + 1) % count) for i in range(ends)]),
                cells,
                lax.ppermute(head, axis, [((i + 1) % count, i) for i in range(ends)]),
            ],
            axis=dim,
        )
    return cells


def product(left, right):
    return jnp.dot(left, right, precision=exact_mode, preferred_element_type=jnp.float32)


def interface_chain(inverse, couple, rights, held):
    offset = product(rights, inverse)
    step = -product(couple, inverse)
    order = rights.shape[0]
    levels = lax.axis_size("grp")

    def combine(pairs, with_step):
        nonlocal offset, composite
        if with_step:
            packed = jnp.concatenate([offset, composite], axis=0)
            half = packed.shape[0] // 2
            packed = jnp.concatenate(
                [lax.ppermute(packed[:half], "grp", pairs), lax.ppermute(packed[half:], "grp", pairs)], axis=0
            )
            earlier_offset, earlier_step = packed[:order], packed[order:]
            offset = product(earlier_offset, composite) + offset
            composite = product(earlier_step, composite)
        else:
            earlier_offset = lax.ppermute(offset, "grp", pairs)
            offset = product(earlier_offset, composite) + offset

    composite = step
    combine([(g, g + 1) for g in range(0, levels - 1, 2)], True)
    shift = 2
    while shift < levels:
        pairs = [(g, g + shift) for g in range(1, levels - shift, 2)]
        combine(pairs, 2 * shift < levels)
        if shift == 2:
            held, offset = lax.optimization_barrier((held, offset))
        shift *= 2
    earlier_offset = lax.ppermute(offset, "grp", [(g, g + 1) for g in range(1, levels - 1, 2)])
    return product(earlier_offset, step) + offset, held


def picked(values, index):
    lanes = 128
    table = values.reshape(-1, lanes)
    flat = index.reshape(-1)
    high = flat // lanes
    low = flat % lanes
    rows = jnp.zeros((flat.shape[0], lanes), values.dtype)
    for which in range(table.shape[0]):
        rows = rows + jnp.where((high == which)[:, None], table[which][None, :], 0.0)
    lane_ids = lax.broadcasted_iota(jnp.int32, (1, lanes), 1)
    chosen = jnp.sum(jnp.where(lane_ids == low[:, None], rows, 0.0), axis=1)
    return chosen.reshape(index.shape)


def scattered(values, rows, cols, row_count):
    lanes = 128
    row_ids = lax.broadcasted_iota(jnp.int32, (1, row_count), 1)
    lane_ids = lax.broadcasted_iota(jnp.int32, (1, lanes), 1)
    rows_hot = (rows[:, None] == row_ids).astype(jnp.float32)
    cols_hot = jnp.where(cols[:, None] == lane_ids, values[:, None], 0.0)
    return lax.dot_general(
        rows_hot,
        cols_hot,
        (((0,), (0,)), ((), ())),
        precision=exact_mode,
        preferred_element_type=jnp.float32,
    )


def padded_targets(cells, first, last, shift):
    row = cells // 128
    keep = (cells >= 0) & (row >= first) & (row < last)
    return jnp.where(keep, row + shift, -1).reshape(-1), (cells % 128).reshape(-1)


def gather_kernel(lookup_ref, table_ref, out_ref):
    chunk = pl.program_id(0)
    rows = out_ref.shape[0]
    pack = out_ref.shape[1] // 16
    group = lax.broadcasted_iota(jnp.int32, (1, out_ref.shape[1]), 1) // 16
    base = chunk * rows * pack

    def body(row, carry):
        packed_row = jnp.zeros((1, out_ref.shape[1]), jnp.float32)
        for part in range(pack):
            where = lookup_ref[base + row * pack + part]
            packed_row = jnp.where(group == part, table_ref[pl.ds(where, 1), :], packed_row)
        out_ref[pl.ds(row, 1), :] = packed_row
        return carry

    lax.fori_loop(0, rows, body, 0, unroll=16)


def gathered_rows(panels, lookup):
    slabs, width, panel_order = panels.shape
    pack = 128 // width
    spread = (
        lax.broadcasted_iota(jnp.int32, (width, 128), 0)
        == lax.broadcasted_iota(jnp.int32, (width, 128), 1) % width
    ).astype(jnp.float32)
    spread = spread.astype(jnp.bfloat16)
    rest = panels
    wide = None
    for _ in range(3):
        rounded = lax.reduce_precision(rest, exponent_bits=8, mantissa_bits=7)
        rest = rest - rounded
        part = rounded.astype(jnp.bfloat16)
        term = lax.dot_general(part, spread, (((1,), (0,)), ((), ())), preferred_element_type=jnp.float32)
        wide = term if wide is None else wide + term
    wide = wide.reshape(slabs * panel_order, 128)
    total = lookup.shape[0]
    out_rows = total // pack
    chunks = 2
    rows = out_rows // chunks
    return pl.pallas_call(
        gather_kernel,
        out_shape=jax.ShapeDtypeStruct((out_rows, 128), jnp.float32),
        grid_spec=pltpu.PrefetchScalarGridSpec(
            num_scalar_prefetch=1,
            grid=(chunks,),
            in_specs=[pl.BlockSpec(wide.shape, lambda c, idx: (0, 0))],
            out_specs=pl.BlockSpec((rows, 128), lambda c, idx: (c, 0)),
        ),
        cost_estimate=pl.CostEstimate(flops=0, bytes_accessed=wide.size * 4 + out_rows * 512, transcendentals=0),
    )(lookup, wide)


def gathered_panels(solved):
    count = lax.axis_size("dev")
    me = lax.axis_index("dev")
    bits = count.bit_length() - 1
    order = [bits - 1, 1, bits - 2, bits - 3, 0] if bits == 5 else list(range(bits))
    block = solved[None]
    for bit in order:
        partner = [(i, i ^ (1 << bit)) for i in range(count)]
        other = lax.ppermute(block, "dev", partner)
        high = ((me >> bit) & 1) == 1
        block = jnp.where(high, jnp.concatenate([other, block], 0), jnp.concatenate([block, other], 0))
    return block, order


def slab_position(slab, order):
    position = jnp.zeros_like(slab)
    for place, bit in enumerate(order):
        position = position + (((slab >> bit) & 1) << place)
    return position


def on_device(
    panel_inverse,
    coupling,
    loads,
    stiffness,
    element_substructure,
    element_rows,
    element_density,
    send_elements,
    receive_cells,
    design_density,
    filter_offsets,
    filter_weights,
):
    inverse = panel_inverse[0, 0]
    couple = coupling[0, 0]
    rights = loads[0, 0]
    held = (element_substructure, element_rows, element_density, send_elements, receive_cells, design_density)
    solved, held = interface_chain(inverse, couple, rights, held)
    element_substructure, element_rows, element_density, send_elements, receive_cells, design_density = held

    copies = jnp.broadcast_to(solved[None], (lax.axis_size("dev"),) + solved.shape)
    panels = lax.all_to_all(copies, "dev", split_axis=0, concat_axis=0, tiled=True)
    slabs, order, panel_order = panels.shape
    slab_place = element_substructure[0, 0]
    lookup = slab_place[None, :] * panel_order + element_rows[0, 0]
    dofs, elements = lookup.shape
    pack = 128 // order
    motion = gathered_rows(panels, lookup.reshape(-1)).reshape(dofs, elements // pack, 128)
    forces = jnp.einsum("ij,jab->iab", stiffness, motion, precision=lax.Precision.HIGH)
    energy = jnp.sum(jnp.sum(motion * forces, axis=0).reshape(elements // pack, pack, order), axis=2)
    energy = energy.reshape(elements)
    density = element_density[0, 0]
    sensitivity = -penalty * density * density * energy * energy_scale
    owned = design_density[0, 0]
    row_count = owned.shape[0]
    count = lax.axis_size("dev")
    cells = receive_cells[0, 0]
    sources, slots = cells.shape
    shared = cells.astype(jnp.float32).reshape(-1, 128)
    to_right = jnp.concatenate([shared, owned[row_count - RADIUS :]], axis=0)
    to_left = jnp.concatenate([shared, owned[:RADIUS]], axis=0)
    to_right, to_left, _ = lax.optimization_barrier((to_right, to_left, solved))
    from_left = lax.ppermute(to_right, "dev", [(i, i + 1) for i in range(count - 1)])
    from_right = lax.ppermute(to_left, "dev", [(i + 1, i) for i in range(count - 1)])
    list_rows = shared.shape[0]
    cells_left = from_left[:list_rows].astype(jnp.int32).reshape(sources, slots)
    cells_right = from_right[:list_rows].astype(jnp.int32).reshape(sources, slots)
    density_rows = jnp.concatenate([from_left[list_rows:], owned, from_right[list_rows:]], axis=0)

    outgoing = picked(sensitivity, send_elements[0, 0])
    edge = jnp.zeros((1, slots), jnp.float32)
    spread_out = jnp.concatenate([edge, outgoing, edge], axis=0)
    owners = outgoing.shape[0]
    triple = jnp.stack([spread_out[0:owners], spread_out[1 : owners + 1], spread_out[2 : owners + 2]], axis=1)
    received = lax.all_to_all(triple, "dev", split_axis=0, concat_axis=0, tiled=True)
    left_rows, left_cols = padded_targets(cells_left, row_count - RADIUS, row_count, RADIUS - row_count)
    own_rows, own_cols = padded_targets(cells, 0, row_count, RADIUS)
    right_rows, right_cols = padded_targets(cells_right, 0, RADIUS, row_count + RADIUS)
    collected = scattered(
        jnp.concatenate([received[:, 0].reshape(-1), received[:, 1].reshape(-1), received[:, 2].reshape(-1)]),
        jnp.concatenate([left_rows, own_rows, right_rows]),
        jnp.concatenate([left_cols, own_cols, right_cols]),
        row_count + 2 * RADIUS,
    )
    padded = density_rows * collected
    total_rows = lax.axis_size("dev") * row_count
    padded_rows = padded.shape[0]
    reach = (
        lax.broadcasted_iota(jnp.int32, (1, row_count, padded_rows), 2)
        - lax.broadcasted_iota(jnp.int32, (1, row_count, padded_rows), 1)
        - RADIUS
    )
    band = jnp.sum(
        jnp.where(reach == filter_offsets[:, None, None], filter_weights[:, None, None], 0.0), axis=0
    )
    padded_global = lax.axis_index("dev") * row_count - RADIUS + jnp.arange(padded_rows, dtype=jnp.int32)
    valid = ((padded_global >= 0) & (padded_global < total_rows)).astype(jnp.float32)
    weight_sum = jnp.sum(band * valid[None, :], axis=1)
    accum = product(band, padded)
    filtered = accum / (owned * weight_sum[:, None])
    return (solved[None, None], filtered[None, None])


def solution(mesh):
    placed = (
        P("grp", "dev", None, None),
        P("grp", "dev", None, None),
        P("grp", "dev", None, None),
        P(),
        P("grp", "dev", None),
        P("grp", "dev", None, None),
        P("grp", "dev", None),
        P("grp", "dev", None, None),
        P("grp", "dev", None, None),
        P("grp", "dev", None, None),
        P(),
        P(),
    )
    return jax.shard_map(
        on_device,
        mesh=mesh,
        in_specs=placed,
        out_specs=(P("grp", "dev", None, None), P("grp", "dev", None, None)),
        check_vma=False,
    )
```

```python
import jax
import jax.numpy as jnp
from jax import lax
from jax.sharding import PartitionSpec as P
from jax.experimental import pallas as pl
from jax.experimental.pallas import tpu as pltpu

NK = 8
RADIUS = 3


exact_mode = lax.Precision.HIGHEST
penalty = 3.0
energy_scale = 1.0 / 4096.0


def passed_along(value, axis, steps):
    count = lax.axis_size(axis)
    leading, last = (max(0, -steps), min(count, count - steps))
    return lax.ppermute(value, axis, [(source, source + steps) for source in range(leading, last)])


def padded_2(cells, sides, width):
    for axis, dim in sides:
        count = lax.axis_size(axis)
        ends = count - 1
        head = lax.slice_in_dim(cells, 0, width, axis=dim)
        tail = lax.slice_in_dim(cells, cells.shape[dim] - width, cells.shape[dim], axis=dim)
        cells = jnp.concatenate(
            [
                lax.ppermute(tail, axis, [(i, (i + 1) % count) for i in range(ends)]),
                cells,
                lax.ppermute(head, axis, [((i + 1) % count, i) for i in range(ends)]),
            ],
            axis=dim,
        )
    return cells


def product(left, right):
    return jnp.dot(left, right, precision=exact_mode, preferred_element_type=jnp.float32)


def interface_chain(inverse, couple, rights, held):
    offset = product(rights, inverse)
    step = -product(couple, inverse)
    order = rights.shape[0]
    levels = lax.axis_size("grp")

    def combine(pairs, with_step):
        nonlocal offset, composite
        if with_step:
            packed = jnp.concatenate([offset, composite], axis=0)
            half = packed.shape[0] // 2
            packed = jnp.concatenate(
                [lax.ppermute(packed[:half], "grp", pairs), lax.ppermute(packed[half:], "grp", pairs)], axis=0
            )
            earlier_offset, earlier_step = packed[:order], packed[order:]
            offset = product(earlier_offset, composite) + offset
            composite = product(earlier_step, composite)
        else:
            earlier_offset = lax.ppermute(offset, "grp", pairs)
            offset = product(earlier_offset, composite) + offset

    composite = step
    combine([(g, g + 1) for g in range(0, levels - 1, 2)], True)
    shift = 2
    while shift < levels:
        pairs = [(g, g + shift) for g in range(1, levels - shift, 2)]
        combine(pairs, 2 * shift < levels)
        if shift == 2:
            held, offset = lax.optimization_barrier((held, offset))
        shift *= 2
    earlier_offset = lax.ppermute(offset, "grp", [(g, g + 1) for g in range(1, levels - 1, 2)])
    return product(earlier_offset, step) + offset, held


def picked(values, index):
    lanes = 128
    table = values.reshape(-1, lanes)
    flat = index.reshape(-1)
    high = flat // lanes
    low = flat % lanes
    rows = jnp.zeros((flat.shape[0], lanes), values.dtype)
    for which in range(table.shape[0]):
        rows = rows + jnp.where((high == which)[:, None], table[which][None, :], 0.0)
    lane_ids = lax.broadcasted_iota(jnp.int32, (1, lanes), 1)
    chosen = jnp.sum(jnp.where(lane_ids == low[:, None], rows, 0.0), axis=1)
    return chosen.reshape(index.shape)


def scattered(values, rows, cols, row_count):
    lanes = 128
    row_ids = lax.broadcasted_iota(jnp.int32, (1, row_count), 1)
    lane_ids = lax.broadcasted_iota(jnp.int32, (1, lanes), 1)
    rows_hot = (rows[:, None] == row_ids).astype(jnp.float32)
    cols_hot = jnp.where(cols[:, None] == lane_ids, values[:, None], 0.0)
    return lax.dot_general(
        rows_hot,
        cols_hot,
        (((0,), (0,)), ((), ())),
        precision=exact_mode,
        preferred_element_type=jnp.float32,
    )


def padded_targets(cells, first, last, shift):
    row = cells // 128
    keep = (cells >= 0) & (row >= first) & (row < last)
    return jnp.where(keep, row + shift, -1).reshape(-1), (cells % 128).reshape(-1)


def gather_kernel(lookup_ref, table_ref, out_ref):
    chunk = pl.program_id(0)
    rows = out_ref.shape[0]
    pack = out_ref.shape[1] // 16
    group = lax.broadcasted_iota(jnp.int32, (1, out_ref.shape[1]), 1) // 16
    base = chunk * rows * pack

    def body(row, carry):
        packed_row = jnp.zeros((1, out_ref.shape[1]), jnp.float32)
        for part in range(pack):
            where = lookup_ref[base + row * pack + part]
            packed_row = jnp.where(group == part, table_ref[pl.ds(where, 1), :], packed_row)
        out_ref[pl.ds(row, 1), :] = packed_row
        return carry

    lax.fori_loop(0, rows, body, 0, unroll=32)


def gathered_rows(panels, lookup):
    slabs, width, panel_order = panels.shape
    pack = 128 // width
    spread = (
        lax.broadcasted_iota(jnp.int32, (width, 128), 0)
        == lax.broadcasted_iota(jnp.int32, (width, 128), 1) % width
    ).astype(jnp.float32)
    spread = spread.astype(jnp.bfloat16)
    rest = panels
    wide = None
    for _ in range(3):
        rounded = lax.reduce_precision(rest, exponent_bits=8, mantissa_bits=7)
        rest = rest - rounded
        part = rounded.astype(jnp.bfloat16)
        term = lax.dot_general(part, spread, (((1,), (0,)), ((), ())), preferred_element_type=jnp.float32)
        wide = term if wide is None else wide + term
    wide = wide.reshape(slabs * panel_order, 128)
    total = lookup.shape[0]
    out_rows = total // pack
    chunks = 2
    rows = out_rows // chunks
    return pl.pallas_call(
        gather_kernel,
        out_shape=jax.ShapeDtypeStruct((out_rows, 128), jnp.float32),
        grid_spec=pltpu.PrefetchScalarGridSpec(
            num_scalar_prefetch=1,
            grid=(chunks,),
            in_specs=[pl.BlockSpec(wide.shape, lambda c, idx: (0, 0))],
            out_specs=pl.BlockSpec((rows, 128), lambda c, idx: (c, 0)),
        ),
        cost_estimate=pl.CostEstimate(flops=0, bytes_accessed=wide.size * 4 + out_rows * 512, transcendentals=0),
    )(lookup, wide)


def gathered_panels(solved):
    count = lax.axis_size("dev")
    me = lax.axis_index("dev")
    bits = count.bit_length() - 1
    order = [bits - 1, 1, bits - 2, bits - 3, 0] if bits == 5 else list(range(bits))
    block = solved[None]
    for bit in order:
        partner = [(i, i ^ (1 << bit)) for i in range(count)]
        other = lax.ppermute(block, "dev", partner)
        high = ((me >> bit) & 1) == 1
        block = jnp.where(high, jnp.concatenate([other, block], 0), jnp.concatenate([block, other], 0))
    return block, order


def slab_position(slab, order):
    position = jnp.zeros_like(slab)
    for place, bit in enumerate(order):
        position = position + (((slab >> bit) & 1) << place)
    return position


def on_device(
    panel_inverse,
    coupling,
    loads,
    stiffness,
    element_substructure,
    element_rows,
    element_density,
    send_elements,
    receive_cells,
    design_density,
    filter_offsets,
    filter_weights,
):
    inverse = panel_inverse[0, 0]
    couple = coupling[0, 0]
    rights = loads[0, 0]
    held = (element_substructure, element_rows, element_density, send_elements, receive_cells, design_density)
    solved, held = interface_chain(inverse, couple, rights, held)
    element_substructure, element_rows, element_density, send_elements, receive_cells, design_density = held

    copies = jnp.broadcast_to(solved[None], (lax.axis_size("dev"),) + solved.shape)
    panels = lax.all_to_all(copies, "dev", split_axis=0, concat_axis=0, tiled=True)
    slabs, order, panel_order = panels.shape
    slab_place = element_substructure[0, 0]
    lookup = slab_place[None, :] * panel_order + element_rows[0, 0]
    dofs, elements = lookup.shape
    pack = 128 // order
    motion = gathered_rows(panels, lookup.reshape(-1)).reshape(dofs, elements // pack, 128)
    forces = jnp.einsum("ij,jab->iab", stiffness, motion, precision=lax.Precision.HIGH)
    energy = jnp.sum(jnp.sum(motion * forces, axis=0).reshape(elements // pack, pack, order), axis=2)
    energy = energy.reshape(elements)
    density = element_density[0, 0]
    sensitivity = -penalty * density * density * energy * energy_scale
    owned = design_density[0, 0]
    row_count = owned.shape[0]
    count = lax.axis_size("dev")
    cells = receive_cells[0, 0]
    sources, slots = cells.shape
    shared = cells.astype(jnp.float32).reshape(-1, 128)
    to_right = jnp.concatenate([shared, owned[row_count - RADIUS :]], axis=0)
    to_left = jnp.concatenate([shared, owned[:RADIUS]], axis=0)
    to_right, to_left, _ = lax.optimization_barrier((to_right, to_left, solved))
    from_left = lax.ppermute(to_right, "dev", [(i, i + 1) for i in range(count - 1)])
    from_right = lax.ppermute(to_left, "dev", [(i + 1, i) for i in range(count - 1)])
    list_rows = shared.shape[0]
    cells_left = from_left[:list_rows].astype(jnp.int32).reshape(sources, slots)
    cells_right = from_right[:list_rows].astype(jnp.int32).reshape(sources, slots)
    density_rows = jnp.concatenate([from_left[list_rows:], owned, from_right[list_rows:]], axis=0)

    outgoing = picked(sensitivity, send_elements[0, 0])
    edge = jnp.zeros((1, slots), jnp.float32)
    spread_out = jnp.concatenate([edge, outgoing, edge], axis=0)
    owners = outgoing.shape[0]
    triple = jnp.stack([spread_out[0:owners], spread_out[1 : owners + 1], spread_out[2 : owners + 2]], axis=1)
    received = lax.all_to_all(triple, "dev", split_axis=0, concat_axis=0, tiled=True)
    left_rows, left_cols = padded_targets(cells_left, row_count - RADIUS, row_count, RADIUS - row_count)
    own_rows, own_cols = padded_targets(cells, 0, row_count, RADIUS)
    right_rows, right_cols = padded_targets(cells_right, 0, RADIUS, row_count + RADIUS)
    collected = scattered(
        jnp.concatenate([received[:, 0].reshape(-1), received[:, 1].reshape(-1), received[:, 2].reshape(-1)]),
        jnp.concatenate([left_rows, own_rows, right_rows]),
        jnp.concatenate([left_cols, own_cols, right_cols]),
        row_count + 2 * RADIUS,
    )
    padded = density_rows * collected
    total_rows = lax.axis_size("dev") * row_count
    padded_rows = padded.shape[0]
    reach = (
        lax.broadcasted_iota(jnp.int32, (1, row_count, padded_rows), 2)
        - lax.broadcasted_iota(jnp.int32, (1, row_count, padded_rows), 1)
        - RADIUS
    )
    band = jnp.sum(
        jnp.where(reach == filter_offsets[:, None, None], filter_weights[:, None, None], 0.0), axis=0
    )
    padded_global = lax.axis_index("dev") * row_count - RADIUS + jnp.arange(padded_rows, dtype=jnp.int32)
    valid = ((padded_global >= 0) & (padded_global < total_rows)).astype(jnp.float32)
    weight_sum = jnp.sum(band * valid[None, :], axis=1)
    accum = product(band, padded)
    filtered = accum / (owned * weight_sum[:, None])
    return (solved[None, None], filtered[None, None])


def solution(mesh):
    placed = (
        P("grp", "dev", None, None),
        P("grp", "dev", None, None),
        P("grp", "dev", None, None),
        P(),
        P("grp", "dev", None),
        P("grp", "dev", None, None),
        P("grp", "dev", None),
        P("grp", "dev", None, None),
        P("grp", "dev", None, None),
        P("grp", "dev", None, None),
        P(),
        P(),
    )
    return jax.shard_map(
        on_device,
        mesh=mesh,
        in_specs=placed,
        out_specs=(P("grp", "dev", None, None), P("grp", "dev", None, None)),
        check_vma=False,
    )
```

```python
import jax
import jax.numpy as jnp
from jax import lax
from jax.sharding import PartitionSpec as P
from jax.experimental import pallas as pl
from jax.experimental.pallas import tpu as pltpu

NK = 8
RADIUS = 3


exact_mode = lax.Precision.HIGHEST
penalty = 3.0
energy_scale = 1.0 / 4096.0


def passed_along(value, axis, steps):
    count = lax.axis_size(axis)
    leading, last = (max(0, -steps), min(count, count - steps))
    return lax.ppermute(value, axis, [(source, source + steps) for source in range(leading, last)])


def padded_2(cells, sides, width):
    for axis, dim in sides:
        count = lax.axis_size(axis)
        ends = count - 1
        head = lax.slice_in_dim(cells, 0, width, axis=dim)
        tail = lax.slice_in_dim(cells, cells.shape[dim] - width, cells.shape[dim], axis=dim)
        cells = jnp.concatenate(
            [
                lax.ppermute(tail, axis, [(i, (i + 1) % count) for i in range(ends)]),
                cells,
                lax.ppermute(head, axis, [((i + 1) % count, i) for i in range(ends)]),
            ],
            axis=dim,
        )
    return cells


def product(left, right):
    return jnp.dot(left, right, precision=exact_mode, preferred_element_type=jnp.float32)


def interface_chain(inverse, couple, rights, held):
    offset = product(rights, inverse)
    step = -product(couple, inverse)
    order = rights.shape[0]
    levels = lax.axis_size("grp")

    def combine(pairs, with_step):
        nonlocal offset, composite
        if with_step:
            packed = jnp.concatenate([offset, composite], axis=0)
            half = packed.shape[0] // 2
            packed = jnp.concatenate(
                [lax.ppermute(packed[:half], "grp", pairs), lax.ppermute(packed[half:], "grp", pairs)], axis=0
            )
            earlier_offset, earlier_step = packed[:order], packed[order:]
            offset = product(earlier_offset, composite) + offset
            composite = product(earlier_step, composite)
        else:
            earlier_offset = lax.ppermute(offset, "grp", pairs)
            offset = product(earlier_offset, composite) + offset

    composite = step
    combine([(g, g + 1) for g in range(0, levels - 1, 2)], True)
    shift = 2
    while shift < levels:
        pairs = [(g, g + shift) for g in range(1, levels - shift, 2)]
        combine(pairs, 2 * shift < levels)
        if shift == 2:
            held, offset = lax.optimization_barrier((held, offset))
        shift *= 2
    earlier_offset = lax.ppermute(offset, "grp", [(g, g + 1) for g in range(1, levels - 1, 2)])
    return product(earlier_offset, step) + offset, held


def picked(values, index):
    lanes = 128
    table = values.reshape(-1, lanes)
    flat = index.reshape(-1)
    high = flat // lanes
    low = flat % lanes
    rows = jnp.zeros((flat.shape[0], lanes), values.dtype)
    for which in range(table.shape[0]):
        rows = rows + jnp.where((high == which)[:, None], table[which][None, :], 0.0)
    lane_ids = lax.broadcasted_iota(jnp.int32, (1, lanes), 1)
    chosen = jnp.sum(jnp.where(lane_ids == low[:, None], rows, 0.0), axis=1)
    return chosen.reshape(index.shape)


def scattered(values, rows, cols, row_count):
    lanes = 128
    row_ids = lax.broadcasted_iota(jnp.int32, (1, row_count), 1)
    lane_ids = lax.broadcasted_iota(jnp.int32, (1, lanes), 1)
    rows_hot = (rows[:, None] == row_ids).astype(jnp.float32)
    cols_hot = jnp.where(cols[:, None] == lane_ids, values[:, None], 0.0)
    return lax.dot_general(
        rows_hot,
        cols_hot,
        (((0,), (0,)), ((), ())),
        precision=exact_mode,
        preferred_element_type=jnp.float32,
    )


def padded_targets(cells, first, last, shift):
    row = cells // 128
    keep = (cells >= 0) & (row >= first) & (row < last)
    return jnp.where(keep, row + shift, -1).reshape(-1), (cells % 128).reshape(-1)


def gather_kernel(lookup_ref, table_ref, out_ref):
    chunk = pl.program_id(0)
    rows = out_ref.shape[0]
    pack = out_ref.shape[1] // 16
    group = lax.broadcasted_iota(jnp.int32, (1, out_ref.shape[1]), 1) // 16
    base = chunk * rows * pack

    def body(row, carry):
        packed_row = jnp.zeros((1, out_ref.shape[1]), jnp.float32)
        for part in range(pack):
            where = lookup_ref[base + row * pack + part]
            packed_row = jnp.where(group == part, table_ref[pl.ds(where, 1), :], packed_row)
        out_ref[pl.ds(row, 1), :] = packed_row
        return carry

    lax.fori_loop(0, rows, body, 0, unroll=32)


def gathered_rows(panels, lookup):
    slabs, width, panel_order = panels.shape
    pack = 128 // width
    spread = (
        lax.broadcasted_iota(jnp.int32, (width, 128), 0)
        == lax.broadcasted_iota(jnp.int32, (width, 128), 1) % width
    ).astype(jnp.float32)
    spread = spread.astype(jnp.bfloat16)
    rest = panels
    wide = None
    for _ in range(2):
        rounded = lax.reduce_precision(rest, exponent_bits=8, mantissa_bits=7)
        rest = rest - rounded
        part = rounded.astype(jnp.bfloat16)
        term = lax.dot_general(part, spread, (((1,), (0,)), ((), ())), preferred_element_type=jnp.float32)
        wide = term if wide is None else wide + term
    wide = wide.reshape(slabs * panel_order, 128)
    total = lookup.shape[0]
    out_rows = total // pack
    chunks = 2
    rows = out_rows // chunks
    return pl.pallas_call(
        gather_kernel,
        out_shape=jax.ShapeDtypeStruct((out_rows, 128), jnp.float32),
        grid_spec=pltpu.PrefetchScalarGridSpec(
            num_scalar_prefetch=1,
            grid=(chunks,),
            in_specs=[pl.BlockSpec(wide.shape, lambda c, idx: (0, 0))],
            out_specs=pl.BlockSpec((rows, 128), lambda c, idx: (c, 0)),
        ),
        cost_estimate=pl.CostEstimate(flops=0, bytes_accessed=wide.size * 4 + out_rows * 512, transcendentals=0),
    )(lookup, wide)


def gathered_panels(solved):
    count = lax.axis_size("dev")
    me = lax.axis_index("dev")
    bits = count.bit_length() - 1
    order = [bits - 1, 1, bits - 2, bits - 3, 0] if bits == 5 else list(range(bits))
    block = solved[None]
    for bit in order:
        partner = [(i, i ^ (1 << bit)) for i in range(count)]
        other = lax.ppermute(block, "dev", partner)
        high = ((me >> bit) & 1) == 1
        block = jnp.where(high, jnp.concatenate([other, block], 0), jnp.concatenate([block, other], 0))
    return block, order


def slab_position(slab, order):
    position = jnp.zeros_like(slab)
    for place, bit in enumerate(order):
        position = position + (((slab >> bit) & 1) << place)
    return position


def on_device(
    panel_inverse,
    coupling,
    loads,
    stiffness,
    element_substructure,
    element_rows,
    element_density,
    send_elements,
    receive_cells,
    design_density,
    filter_offsets,
    filter_weights,
):
    inverse = panel_inverse[0, 0]
    couple = coupling[0, 0]
    rights = loads[0, 0]
    held = (element_substructure, element_rows, element_density, send_elements, receive_cells, design_density)
    solved, held = interface_chain(inverse, couple, rights, held)
    element_substructure, element_rows, element_density, send_elements, receive_cells, design_density = held

    copies = jnp.broadcast_to(solved[None], (lax.axis_size("dev"),) + solved.shape)
    panels = lax.all_to_all(copies, "dev", split_axis=0, concat_axis=0, tiled=True)
    slabs, order, panel_order = panels.shape
    slab_place = element_substructure[0, 0]
    lookup = slab_place[None, :] * panel_order + element_rows[0, 0]
    dofs, elements = lookup.shape
    pack = 128 // order
    motion = gathered_rows(panels, lookup.reshape(-1)).reshape(dofs, elements // pack, 128)
    forces = jnp.einsum("ij,jab->iab", stiffness, motion, precision=lax.Precision.HIGH)
    energy = jnp.sum(jnp.sum(motion * forces, axis=0).reshape(elements // pack, pack, order), axis=2)
    energy = energy.reshape(elements)
    density = element_density[0, 0]
    sensitivity = -penalty * density * density * energy * energy_scale
    owned = design_density[0, 0]
    row_count = owned.shape[0]
    count = lax.axis_size("dev")
    cells = receive_cells[0, 0]
    sources, slots = cells.shape
    shared = cells.astype(jnp.float32).reshape(-1, 128)
    to_right = jnp.concatenate([shared, owned[row_count - RADIUS :]], axis=0)
    to_left = jnp.concatenate([shared, owned[:RADIUS]], axis=0)
    to_right, to_left, _ = lax.optimization_barrier((to_right, to_left, solved))
    from_left = lax.ppermute(to_right, "dev", [(i, i + 1) for i in range(count - 1)])
    from_right = lax.ppermute(to_left, "dev", [(i + 1, i) for i in range(count - 1)])
    list_rows = shared.shape[0]
    cells_left = from_left[:list_rows].astype(jnp.int32).reshape(sources, slots)
    cells_right = from_right[:list_rows].astype(jnp.int32).reshape(sources, slots)
    density_rows = jnp.concatenate([from_left[list_rows:], owned, from_right[list_rows:]], axis=0)

    outgoing = picked(sensitivity, send_elements[0, 0])
    edge = jnp.zeros((1, slots), jnp.float32)
    spread_out = jnp.concatenate([edge, outgoing, edge], axis=0)
    owners = outgoing.shape[0]
    triple = jnp.stack([spread_out[0:owners], spread_out[1 : owners + 1], spread_out[2 : owners + 2]], axis=1)
    received = lax.all_to_all(triple, "dev", split_axis=0, concat_axis=0, tiled=True)
    left_rows, left_cols = padded_targets(cells_left, row_count - RADIUS, row_count, RADIUS - row_count)
    own_rows, own_cols = padded_targets(cells, 0, row_count, RADIUS)
    right_rows, right_cols = padded_targets(cells_right, 0, RADIUS, row_count + RADIUS)
    collected = scattered(
        jnp.concatenate([received[:, 0].reshape(-1), received[:, 1].reshape(-1), received[:, 2].reshape(-1)]),
        jnp.concatenate([left_rows, own_rows, right_rows]),
        jnp.concatenate([left_cols, own_cols, right_cols]),
        row_count + 2 * RADIUS,
    )
    padded = density_rows * collected
    total_rows = lax.axis_size("dev") * row_count
    padded_rows = padded.shape[0]
    reach = (
        lax.broadcasted_iota(jnp.int32, (1, row_count, padded_rows), 2)
        - lax.broadcasted_iota(jnp.int32, (1, row_count, padded_rows), 1)
        - RADIUS
    )
    band = jnp.sum(
        jnp.where(reach == filter_offsets[:, None, None], filter_weights[:, None, None], 0.0), axis=0
    )
    padded_global = lax.axis_index("dev") * row_count - RADIUS + jnp.arange(padded_rows, dtype=jnp.int32)
    valid = ((padded_global >= 0) & (padded_global < total_rows)).astype(jnp.float32)
    weight_sum = jnp.sum(band * valid[None, :], axis=1)
    accum = product(band, padded)
    filtered = accum / (owned * weight_sum[:, None])
    return (solved[None, None], filtered[None, None])


def solution(mesh):
    placed = (
        P("grp", "dev", None, None),
        P("grp", "dev", None, None),
        P("grp", "dev", None, None),
        P(),
        P("grp", "dev", None),
        P("grp", "dev", None, None),
        P("grp", "dev", None),
        P("grp", "dev", None, None),
        P("grp", "dev", None, None),
        P("grp", "dev", None, None),
        P(),
        P(),
    )
    return jax.shard_map(
        on_device,
        mesh=mesh,
        in_specs=placed,
        out_specs=(P("grp", "dev", None, None), P("grp", "dev", None, None)),
        check_vma=False,
    )
```

```python
import jax
import jax.numpy as jnp
from jax import lax
from jax.sharding import PartitionSpec as P
from jax.experimental import pallas as pl
from jax.experimental.pallas import tpu as pltpu

NK = 8
RADIUS = 3


exact_mode = lax.Precision.HIGHEST
penalty = 3.0
energy_scale = 1.0 / 4096.0


def passed_along(value, axis, steps):
    count = lax.axis_size(axis)
    leading, last = (max(0, -steps), min(count, count - steps))
    return lax.ppermute(value, axis, [(source, source + steps) for source in range(leading, last)])


def padded_2(cells, sides, width):
    for axis, dim in sides:
        count = lax.axis_size(axis)
        ends = count - 1
        head = lax.slice_in_dim(cells, 0, width, axis=dim)
        tail = lax.slice_in_dim(cells, cells.shape[dim] - width, cells.shape[dim], axis=dim)
        cells = jnp.concatenate(
            [
                lax.ppermute(tail, axis, [(i, (i + 1) % count) for i in range(ends)]),
                cells,
                lax.ppermute(head, axis, [((i + 1) % count, i) for i in range(ends)]),
            ],
            axis=dim,
        )
    return cells


def product(left, right):
    return jnp.dot(left, right, precision=exact_mode, preferred_element_type=jnp.float32)


def interface_chain(inverse, couple, rights, held):
    offset = product(rights, inverse)
    step = -product(couple, inverse)
    order = rights.shape[0]
    levels = lax.axis_size("grp")

    def combine(pairs, with_step):
        nonlocal offset, composite
        if with_step:
            packed = jnp.concatenate([offset, composite], axis=0)
            half = packed.shape[0] // 2
            packed = jnp.concatenate(
                [lax.ppermute(packed[:half], "grp", pairs), lax.ppermute(packed[half:], "grp", pairs)], axis=0
            )
            earlier_offset, earlier_step = packed[:order], packed[order:]
            offset = product(earlier_offset, composite) + offset
            composite = product(earlier_step, composite)
        else:
            earlier_offset = lax.ppermute(offset, "grp", pairs)
            offset = product(earlier_offset, composite) + offset

    composite = step
    combine([(g, g + 1) for g in range(0, levels - 1, 2)], True)
    shift = 2
    while shift < levels:
        pairs = [(g, g + shift) for g in range(1, levels - shift, 2)]
        combine(pairs, 2 * shift < levels)
        if shift == 2:
            held, offset = lax.optimization_barrier((held, offset))
        shift *= 2
    earlier_offset = lax.ppermute(offset, "grp", [(g, g + 1) for g in range(1, levels - 1, 2)])
    return product(earlier_offset, step) + offset, held


def picked(values, index):
    lanes = 128
    table = values.reshape(-1, lanes)
    flat = index.reshape(-1)
    high = flat // lanes
    low = flat % lanes
    rows = jnp.zeros((flat.shape[0], lanes), values.dtype)
    for which in range(table.shape[0]):
        rows = rows + jnp.where((high == which)[:, None], table[which][None, :], 0.0)
    lane_ids = lax.broadcasted_iota(jnp.int32, (1, lanes), 1)
    chosen = jnp.sum(jnp.where(lane_ids == low[:, None], rows, 0.0), axis=1)
    return chosen.reshape(index.shape)


def scattered(values, rows, cols, row_count):
    lanes = 128
    row_ids = lax.broadcasted_iota(jnp.int32, (1, row_count), 1)
    lane_ids = lax.broadcasted_iota(jnp.int32, (1, lanes), 1)
    rows_hot = (rows[:, None] == row_ids).astype(jnp.float32)
    cols_hot = jnp.where(cols[:, None] == lane_ids, values[:, None], 0.0)
    return lax.dot_general(
        rows_hot,
        cols_hot,
        (((0,), (0,)), ((), ())),
        precision=lax.Precision.HIGH,
        preferred_element_type=jnp.float32,
    )


def padded_targets(cells, first, last, shift):
    row = cells // 128
    keep = (cells >= 0) & (row >= first) & (row < last)
    return jnp.where(keep, row + shift, -1).reshape(-1), (cells % 128).reshape(-1)


def gather_kernel(lookup_ref, table_ref, out_ref):
    chunk = pl.program_id(0)
    rows = out_ref.shape[0]
    pack = out_ref.shape[1] // 16
    group = lax.broadcasted_iota(jnp.int32, (1, out_ref.shape[1]), 1) // 16
    base = chunk * rows * pack

    def body(row, carry):
        packed_row = jnp.zeros((1, out_ref.shape[1]), jnp.float32)
        for part in range(pack):
            where = lookup_ref[base + row * pack + part]
            packed_row = jnp.where(group == part, table_ref[pl.ds(where, 1), :], packed_row)
        out_ref[pl.ds(row, 1), :] = packed_row
        return carry

    lax.fori_loop(0, rows, body, 0, unroll=32)


def gathered_rows(panels, lookup):
    slabs, width, panel_order = panels.shape
    pack = 128 // width
    spread = (
        lax.broadcasted_iota(jnp.int32, (width, 128), 0)
        == lax.broadcasted_iota(jnp.int32, (width, 128), 1) % width
    ).astype(jnp.float32)
    spread = spread.astype(jnp.bfloat16)
    rest = panels
    wide = None
    for _ in range(2):
        rounded = lax.reduce_precision(rest, exponent_bits=8, mantissa_bits=7)
        rest = rest - rounded
        part = rounded.astype(jnp.bfloat16)
        term = lax.dot_general(part, spread, (((1,), (0,)), ((), ())), preferred_element_type=jnp.float32)
        wide = term if wide is None else wide + term
    wide = wide.reshape(slabs * panel_order, 128)
    total = lookup.shape[0]
    out_rows = total // pack
    chunks = 2
    rows = out_rows // chunks
    return pl.pallas_call(
        gather_kernel,
        out_shape=jax.ShapeDtypeStruct((out_rows, 128), jnp.float32),
        grid_spec=pltpu.PrefetchScalarGridSpec(
            num_scalar_prefetch=1,
            grid=(chunks,),
            in_specs=[pl.BlockSpec(wide.shape, lambda c, idx: (0, 0))],
            out_specs=pl.BlockSpec((rows, 128), lambda c, idx: (c, 0)),
        ),
        cost_estimate=pl.CostEstimate(flops=0, bytes_accessed=wide.size * 4 + out_rows * 512, transcendentals=0),
    )(lookup, wide)


def gathered_panels(solved):
    count = lax.axis_size("dev")
    me = lax.axis_index("dev")
    bits = count.bit_length() - 1
    order = [bits - 1, 1, bits - 2, bits - 3, 0] if bits == 5 else list(range(bits))
    block = solved[None]
    for bit in order:
        partner = [(i, i ^ (1 << bit)) for i in range(count)]
        other = lax.ppermute(block, "dev", partner)
        high = ((me >> bit) & 1) == 1
        block = jnp.where(high, jnp.concatenate([other, block], 0), jnp.concatenate([block, other], 0))
    return block, order


def slab_position(slab, order):
    position = jnp.zeros_like(slab)
    for place, bit in enumerate(order):
        position = position + (((slab >> bit) & 1) << place)
    return position


def on_device(
    panel_inverse,
    coupling,
    loads,
    stiffness,
    element_substructure,
    element_rows,
    element_density,
    send_elements,
    receive_cells,
    design_density,
    filter_offsets,
    filter_weights,
):
    inverse = panel_inverse[0, 0]
    couple = coupling[0, 0]
    rights = loads[0, 0]
    held = (element_substructure, element_rows, element_density, send_elements, receive_cells, design_density)
    solved, held = interface_chain(inverse, couple, rights, held)
    element_substructure, element_rows, element_density, send_elements, receive_cells, design_density = held

    copies = jnp.broadcast_to(solved[None], (lax.axis_size("dev"),) + solved.shape)
    panels = lax.all_to_all(copies, "dev", split_axis=0, concat_axis=0, tiled=True)
    slabs, order, panel_order = panels.shape
    slab_place = element_substructure[0, 0]
    lookup = slab_place[None, :] * panel_order + element_rows[0, 0]
    dofs, elements = lookup.shape
    pack = 128 // order
    motion = gathered_rows(panels, lookup.reshape(-1)).reshape(dofs, elements // pack, 128)
    forces = jnp.einsum("ij,jab->iab", stiffness, motion, precision=lax.Precision.HIGH)
    energy = jnp.sum(jnp.sum(motion * forces, axis=0).reshape(elements // pack, pack, order), axis=2)
    energy = energy.reshape(elements)
    density = element_density[0, 0]
    sensitivity = -penalty * density * density * energy * energy_scale
    owned = design_density[0, 0]
    row_count = owned.shape[0]
    count = lax.axis_size("dev")
    cells = receive_cells[0, 0]
    sources, slots = cells.shape
    shared = cells.astype(jnp.float32).reshape(-1, 128)
    to_right = jnp.concatenate([shared, owned[row_count - RADIUS :]], axis=0)
    to_left = jnp.concatenate([shared, owned[:RADIUS]], axis=0)
    to_right, to_left, _ = lax.optimization_barrier((to_right, to_left, solved))
    from_left = lax.ppermute(to_right, "dev", [(i, i + 1) for i in range(count - 1)])
    from_right = lax.ppermute(to_left, "dev", [(i + 1, i) for i in range(count - 1)])
    list_rows = shared.shape[0]
    cells_left = from_left[:list_rows].astype(jnp.int32).reshape(sources, slots)
    cells_right = from_right[:list_rows].astype(jnp.int32).reshape(sources, slots)
    density_rows = jnp.concatenate([from_left[list_rows:], owned, from_right[list_rows:]], axis=0)

    outgoing = picked(sensitivity, send_elements[0, 0])
    edge = jnp.zeros((1, slots), jnp.float32)
    spread_out = jnp.concatenate([edge, outgoing, edge], axis=0)
    owners = outgoing.shape[0]
    triple = jnp.stack([spread_out[0:owners], spread_out[1 : owners + 1], spread_out[2 : owners + 2]], axis=1)
    received = lax.all_to_all(triple, "dev", split_axis=0, concat_axis=0, tiled=True)
    left_rows, left_cols = padded_targets(cells_left, row_count - RADIUS, row_count, RADIUS - row_count)
    own_rows, own_cols = padded_targets(cells, 0, row_count, RADIUS)
    right_rows, right_cols = padded_targets(cells_right, 0, RADIUS, row_count + RADIUS)
    collected = scattered(
        jnp.concatenate([received[:, 0].reshape(-1), received[:, 1].reshape(-1), received[:, 2].reshape(-1)]),
        jnp.concatenate([left_rows, own_rows, right_rows]),
        jnp.concatenate([left_cols, own_cols, right_cols]),
        row_count + 2 * RADIUS,
    )
    padded = density_rows * collected
    total_rows = lax.axis_size("dev") * row_count
    padded_rows = padded.shape[0]
    reach = (
        lax.broadcasted_iota(jnp.int32, (1, row_count, padded_rows), 2)
        - lax.broadcasted_iota(jnp.int32, (1, row_count, padded_rows), 1)
        - RADIUS
    )
    band = jnp.sum(
        jnp.where(reach == filter_offsets[:, None, None], filter_weights[:, None, None], 0.0), axis=0
    )
    padded_global = lax.axis_index("dev") * row_count - RADIUS + jnp.arange(padded_rows, dtype=jnp.int32)
    valid = ((padded_global >= 0) & (padded_global < total_rows)).astype(jnp.float32)
    weight_sum = jnp.sum(band * valid[None, :], axis=1)
    accum = product(band, padded)
    filtered = accum / (owned * weight_sum[:, None])
    return (solved[None, None], filtered[None, None])


def solution(mesh):
    placed = (
        P("grp", "dev", None, None),
        P("grp", "dev", None, None),
        P("grp", "dev", None, None),
        P(),
        P("grp", "dev", None),
        P("grp", "dev", None, None),
        P("grp", "dev", None),
        P("grp", "dev", None, None),
        P("grp", "dev", None, None),
        P("grp", "dev", None, None),
        P(),
        P(),
    )
    return jax.shard_map(
        on_device,
        mesh=mesh,
        in_specs=placed,
        out_specs=(P("grp", "dev", None, None), P("grp", "dev", None, None)),
        check_vma=False,
    )
```

```python
import jax
import jax.numpy as jnp
from jax import lax
from jax.sharding import PartitionSpec as P
from jax.experimental import pallas as pl
from jax.experimental.pallas import tpu as pltpu

NK = 8
RADIUS = 3


exact_mode = lax.Precision.HIGHEST
penalty = 3.0
energy_scale = 1.0 / 4096.0


def passed_along(value, axis, steps):
    count = lax.axis_size(axis)
    leading, last = (max(0, -steps), min(count, count - steps))
    return lax.ppermute(value, axis, [(source, source + steps) for source in range(leading, last)])


def padded_2(cells, sides, width):
    for axis, dim in sides:
        count = lax.axis_size(axis)
        ends = count - 1
        head = lax.slice_in_dim(cells, 0, width, axis=dim)
        tail = lax.slice_in_dim(cells, cells.shape[dim] - width, cells.shape[dim], axis=dim)
        cells = jnp.concatenate(
            [
                lax.ppermute(tail, axis, [(i, (i + 1) % count) for i in range(ends)]),
                cells,
                lax.ppermute(head, axis, [((i + 1) % count, i) for i in range(ends)]),
            ],
            axis=dim,
        )
    return cells


def product(left, right):
    return jnp.dot(left, right, precision=exact_mode, preferred_element_type=jnp.float32)


def interface_chain(inverse, couple, rights, held):
    offset = product(rights, inverse)
    step = -product(couple, inverse)
    order = rights.shape[0]
    levels = lax.axis_size("grp")

    def combine(pairs, with_step):
        nonlocal offset, composite
        if with_step:
            packed = jnp.concatenate([offset, composite], axis=0)
            half = packed.shape[0] // 2
            packed = jnp.concatenate(
                [lax.ppermute(packed[:half], "grp", pairs), lax.ppermute(packed[half:], "grp", pairs)], axis=0
            )
            earlier_offset, earlier_step = packed[:order], packed[order:]
            offset = product(earlier_offset, composite) + offset
            composite = product(earlier_step, composite)
        else:
            earlier_offset = lax.ppermute(offset, "grp", pairs)
            offset = product(earlier_offset, composite) + offset

    composite = step
    combine([(g, g + 1) for g in range(0, levels - 1, 2)], True)
    shift = 2
    while shift < levels:
        pairs = [(g, g + shift) for g in range(1, levels - shift, 2)]
        combine(pairs, 2 * shift < levels)
        if shift == 2:
            held, offset = lax.optimization_barrier((held, offset))
        shift *= 2
    earlier_offset = lax.ppermute(offset, "grp", [(g, g + 1) for g in range(1, levels - 1, 2)])
    return product(earlier_offset, step) + offset, held


def picked(values, index):
    lanes = 128
    table = values.reshape(-1, lanes)
    flat = index.reshape(-1)
    high = flat // lanes
    low = flat % lanes
    rows = jnp.zeros((flat.shape[0], lanes), values.dtype)
    for which in range(table.shape[0]):
        rows = rows + jnp.where((high == which)[:, None], table[which][None, :], 0.0)
    lane_ids = lax.broadcasted_iota(jnp.int32, (1, lanes), 1)
    chosen = jnp.sum(jnp.where(lane_ids == low[:, None], rows, 0.0), axis=1)
    return chosen.reshape(index.shape)


def scattered(values, rows, cols, row_count):
    lanes = 128
    row_ids = lax.broadcasted_iota(jnp.int32, (1, row_count), 1)
    lane_ids = lax.broadcasted_iota(jnp.int32, (1, lanes), 1)
    rows_hot = (rows[:, None] == row_ids).astype(jnp.float32)
    cols_hot = jnp.where(cols[:, None] == lane_ids, values[:, None], 0.0)
    return lax.dot_general(
        rows_hot,
        cols_hot,
        (((0,), (0,)), ((), ())),
        precision=lax.Precision.HIGH,
        preferred_element_type=jnp.float32,
    )


def padded_targets(cells, first, last, shift):
    row = cells // 128
    keep = (cells >= 0) & (row >= first) & (row < last)
    return jnp.where(keep, row + shift, -1).reshape(-1), (cells % 128).reshape(-1)


def gather_kernel(lookup_ref, table_ref, out_ref):
    chunk = pl.program_id(0)
    rows = out_ref.shape[0]
    pack = out_ref.shape[1] // 16
    group = lax.broadcasted_iota(jnp.int32, (1, out_ref.shape[1]), 1) // 16
    base = chunk * rows * pack

    def body(row, carry):
        packed_row = jnp.zeros((1, out_ref.shape[1]), jnp.float32)
        for part in range(pack):
            where = lookup_ref[base + row * pack + part]
            packed_row = jnp.where(group == part, table_ref[pl.ds(where, 1), :], packed_row)
        out_ref[pl.ds(row, 1), :] = packed_row
        return carry

    lax.fori_loop(0, rows, body, 0, unroll=32)


def gathered_rows(panels, lookup):
    slabs, width, panel_order = panels.shape
    pack = 128 // width
    spread = (
        lax.broadcasted_iota(jnp.int32, (width, 128), 0)
        == lax.broadcasted_iota(jnp.int32, (width, 128), 1) % width
    ).astype(jnp.float32)
    spread = spread.astype(jnp.bfloat16)
    rest = panels
    wide = None
    for _ in range(2):
        rounded = lax.reduce_precision(rest, exponent_bits=8, mantissa_bits=7)
        rest = rest - rounded
        part = rounded.astype(jnp.bfloat16)
        term = lax.dot_general(part, spread, (((1,), (0,)), ((), ())), preferred_element_type=jnp.float32)
        wide = term if wide is None else wide + term
    wide = wide.reshape(slabs * panel_order, 128)
    total = lookup.shape[0]
    out_rows = total // pack
    chunks = 2
    rows = out_rows // chunks
    return pl.pallas_call(
        gather_kernel,
        out_shape=jax.ShapeDtypeStruct((out_rows, 128), jnp.float32),
        grid_spec=pltpu.PrefetchScalarGridSpec(
            num_scalar_prefetch=1,
            grid=(chunks,),
            in_specs=[pl.BlockSpec(wide.shape, lambda c, idx: (0, 0))],
            out_specs=pl.BlockSpec((rows, 128), lambda c, idx: (c, 0)),
        ),
        cost_estimate=pl.CostEstimate(flops=0, bytes_accessed=wide.size * 4 + out_rows * 512, transcendentals=0),
    )(lookup, wide)


def gathered_panels(solved):
    count = lax.axis_size("dev")
    me = lax.axis_index("dev")
    bits = count.bit_length() - 1
    order = [bits - 1, 1, bits - 2, bits - 3, 0] if bits == 5 else list(range(bits))
    block = solved[None]
    for bit in order:
        partner = [(i, i ^ (1 << bit)) for i in range(count)]
        other = lax.ppermute(block, "dev", partner)
        high = ((me >> bit) & 1) == 1
        block = jnp.where(high, jnp.concatenate([other, block], 0), jnp.concatenate([block, other], 0))
    return block, order


def slab_position(slab, order):
    position = jnp.zeros_like(slab)
    for place, bit in enumerate(order):
        position = position + (((slab >> bit) & 1) << place)
    return position


def on_device(
    panel_inverse,
    coupling,
    loads,
    stiffness,
    element_substructure,
    element_rows,
    element_density,
    send_elements,
    receive_cells,
    design_density,
    filter_offsets,
    filter_weights,
):
    inverse = panel_inverse[0, 0]
    couple = coupling[0, 0]
    rights = loads[0, 0]
    held = (element_substructure, element_rows, element_density, send_elements, receive_cells, design_density)
    solved, held = interface_chain(inverse, couple, rights, held)
    element_substructure, element_rows, element_density, send_elements, receive_cells, design_density = held

    copies = jnp.broadcast_to(solved[None], (lax.axis_size("dev"),) + solved.shape)
    panels = lax.all_to_all(copies, "dev", split_axis=0, concat_axis=0, tiled=True)
    slabs, order, panel_order = panels.shape
    slab_place = element_substructure[0, 0]
    lookup = slab_place[None, :] * panel_order + element_rows[0, 0]
    dofs, elements = lookup.shape
    pack = 128 // order
    motion = gathered_rows(panels, lookup.reshape(-1)).reshape(dofs, elements // pack, 128)
    forces = jnp.einsum("ij,jab->iab", stiffness, motion, precision=lax.Precision.HIGH)
    energy = jnp.sum(jnp.sum(motion * forces, axis=0).reshape(elements // pack, pack, order), axis=2)
    energy = energy.reshape(elements)
    density = element_density[0, 0]
    sensitivity = -penalty * density * density * energy * energy_scale
    owned = design_density[0, 0]
    row_count = owned.shape[0]
    count = lax.axis_size("dev")
    cells = receive_cells[0, 0]
    sources, slots = cells.shape
    shared = cells.astype(jnp.float32).reshape(-1, 128)
    to_right = jnp.concatenate([shared, owned[row_count - RADIUS :]], axis=0)
    to_left = jnp.concatenate([shared, owned[:RADIUS]], axis=0)
    to_right, to_left, _ = lax.optimization_barrier((to_right, to_left, solved))
    from_left = lax.ppermute(to_right, "dev", [(i, i + 1) for i in range(count - 1)])
    from_right = lax.ppermute(to_left, "dev", [(i + 1, i) for i in range(count - 1)])
    list_rows = shared.shape[0]
    cells_left = from_left[:list_rows].astype(jnp.int32).reshape(sources, slots)
    cells_right = from_right[:list_rows].astype(jnp.int32).reshape(sources, slots)
    density_rows = jnp.concatenate([from_left[list_rows:], owned, from_right[list_rows:]], axis=0)

    outgoing = picked(sensitivity, send_elements[0, 0])
    edge = jnp.zeros((1, slots), jnp.float32)
    spread_out = jnp.concatenate([edge, outgoing, edge], axis=0)
    owners = outgoing.shape[0]
    triple = jnp.stack([spread_out[0:owners], spread_out[1 : owners + 1], spread_out[2 : owners + 2]], axis=1)
    received = lax.all_to_all(triple, "dev", split_axis=0, concat_axis=0, tiled=True)
    left_rows, left_cols = padded_targets(cells_left, row_count - RADIUS, row_count, RADIUS - row_count)
    own_rows, own_cols = padded_targets(cells, 0, row_count, RADIUS)
    right_rows, right_cols = padded_targets(cells_right, 0, RADIUS, row_count + RADIUS)
    collected = scattered(
        jnp.concatenate([received[:, 0].reshape(-1), received[:, 1].reshape(-1), received[:, 2].reshape(-1)]),
        jnp.concatenate([left_rows, own_rows, right_rows]),
        jnp.concatenate([left_cols, own_cols, right_cols]),
        row_count + 2 * RADIUS,
    )
    padded = density_rows * collected
    total_rows = lax.axis_size("dev") * row_count
    padded_rows = padded.shape[0]
    reach = (
        lax.broadcasted_iota(jnp.int32, (1, row_count, padded_rows), 2)
        - lax.broadcasted_iota(jnp.int32, (1, row_count, padded_rows), 1)
        - RADIUS
    )
    band = jnp.sum(
        jnp.where(reach == filter_offsets[:, None, None], filter_weights[:, None, None], 0.0), axis=0
    )
    padded_global = lax.axis_index("dev") * row_count - RADIUS + jnp.arange(padded_rows, dtype=jnp.int32)
    valid = ((padded_global >= 0) & (padded_global < total_rows)).astype(jnp.float32)
    weight_sum = jnp.sum(band * valid[None, :], axis=1)
    accum = jnp.dot(band, padded, precision=lax.Precision.HIGH, preferred_element_type=jnp.float32)
    filtered = accum / (owned * weight_sum[:, None])
    return (solved[None, None], filtered[None, None])


def solution(mesh):
    placed = (
        P("grp", "dev", None, None),
        P("grp", "dev", None, None),
        P("grp", "dev", None, None),
        P(),
        P("grp", "dev", None),
        P("grp", "dev", None, None),
        P("grp", "dev", None),
        P("grp", "dev", None, None),
        P("grp", "dev", None, None),
        P("grp", "dev", None, None),
        P(),
        P(),
    )
    return jax.shard_map(
        on_device,
        mesh=mesh,
        in_specs=placed,
        out_specs=(P("grp", "dev", None, None), P("grp", "dev", None, None)),
        check_vma=False,
    )
```
